512 devices in a mesh: blk: 128 (over x, z, y_lo), frq: 4 (over y_hi, core).
Axes of the slice: x: 4, y: 4 (y_hi: 2, y_lo: 2; y = y_hi * 2 + y_lo), z: 16, core: 2. Of those that a mesh axis runs over, the one named last changes fastest.
Arguments:
- spectra: bfloat16 [2, 3, 2048, 512], P(None, None, 'blk', 'frq'), may hold values from -6 to 6
- observed: bfloat16 [32768, 3, 3, 1024], P(('blk', 'frq')), may hold values from -6 to 6
- own_station: int32 [128, 128, 2], P('blk'), may hold values from 0 to 15
- partner_station: int32 [128, 128, 2], P('blk'), may hold values from 0 to 15, as said below
- pair_count: int32 [128, 128], P('blk'), may hold values from 1 to 2, as said below
Outputs:
- adjoint: float32 [1024, 3, 2048], P('frq', None, 'blk')
The draws below stay inside these ranges and needn't reach their ends.
Inputs may be any that keep to these rules, and one draw needn't show every extreme that they name: `partner_station`: within the reading block's own block pair, a slot's two stations differ. `pair_count`: the live slots of a block pair are its first ones; every reading block has a block pair with all 2 slots live.
All inputs are finite; a program needn't handle non-finite values.
Results may differ from the reference program's by a relative error of at most 0.003.
Values may be sent and summed in bfloat16 or wider, within the bound.
No kernel may reach another device: no remote copies, remote signals or barrier semaphores. Data moves between devices by JAX's collectives and lax.ppermute only.
A program may use at most 64 MiB of HBM per device.

```python
import math
import jax
import jax.numpy as jnp
from jax import lax

STA_DEV = 16
CAP = 2
NF = 512
BLOCKS = 128
STATIONS = 2048
PAIRS = 32768
NT = 1024


def station_pairs(key):
    shape = (BLOCKS, BLOCKS, CAP)
    own_draw = jax.random.randint(jax.random.fold_in(key, 11), shape, 0, STA_DEV)
    other_draw = jax.random.randint(jax.random.fold_in(key, 12), shape, 0, STA_DEV)
    offset = jax.random.randint(jax.random.fold_in(key, 13), shape, 1, STA_DEV)
    diagonal = (jnp.arange(BLOCKS)[:, None] == jnp.arange(BLOCKS)[None, :])[:, :, None]
    partner = jnp.where(diagonal, (own_draw + offset) % STA_DEV, other_draw)
    return (own_draw.astype(jnp.int32), partner.astype(jnp.int32))


def draw_own_station(key, part):
    return station_pairs(key)[0]


def draw_partner_station(key, part):
    return station_pairs(key)[1]


def draw_pair_count(key, part):
    counts = jax.random.randint(jax.random.fold_in(key, 21), (BLOCKS, BLOCKS), 1, CAP + 1)
    full_pick = jax.random.randint(jax.random.fold_in(key, 22), (BLOCKS,), 0, BLOCKS)
    chosen = jnp.arange(BLOCKS)[None, :] == full_pick[:, None]
    return jnp.where(chosen, CAP, counts).astype(jnp.int32)


def block_levels(own_key, shape, cuts, smallest, high):
    loudness = 1.0
    for axis_at, blocks in cuts:
        draws = jax.random.uniform(jax.random.fold_in(jax.random.fold_in(own_key, 6), axis_at), (blocks,), jnp.float32, smallest / len(cuts), high / len(cuts))
        loudness = loudness * jnp.repeat(jnp.exp(draws), shape[axis_at] // blocks).reshape((-1,) + (1,) * (len(shape) - 1 - axis_at))
    return loudness


def gaussian(stream_key, shape, spread, limit, pieces=(), held_as=jnp.bfloat16):
    gain = block_levels(stream_key, shape, pieces, -0.22, 0.18) if pieces else 1.0
    drawn = jax.random.normal(stream_key, shape, jnp.float32) * spread * gain
    return jnp.minimum(jnp.maximum(drawn, -limit), limit).astype(held_as)


def setup_inputs(seed: int = 0) -> dict:
    seeds = jax.random.split(jax.random.key(seed), 6)
    return {
        "spectra": gaussian(seeds[0], (2, 3, STATIONS, NF), 1.0, 6.0, ((2, 128), (3, 4))),
        "observed": gaussian(seeds[1], (PAIRS, 3, 3, NT), 1.0, 6.0, ((0, 512),)),
        "own_station": draw_own_station(jax.random.fold_in(seeds[5], 71), 0),
        "partner_station": draw_partner_station(jax.random.fold_in(seeds[5], 71), 0),
        "pair_count": draw_pair_count(jax.random.fold_in(seeds[5], 71), 0),
    }


def phase_table(freq_start, freq_count, time_start, time_count):
    freq_index = lax.iota(jnp.int32, freq_count) + freq_start
    time_index = lax.iota(jnp.int32, time_count) + time_start
    phase_num = (2 * freq_index + 1)[:, None] * time_index[None, :] % (2 * NT)
    return phase_num.astype(jnp.float32) * (math.pi / NT)

def lag_window():
    time_index = lax.iota(jnp.int32, NT)
    lag_size = jnp.minimum(time_index, NT - time_index)
    return ((lag_size >= NT // 32) & (lag_size < NT // 4)).astype(jnp.float32)

def cross_spectra(first_rows, second_rows):
    real_part = first_rows[:, 0, :, None] * second_rows[:, 0, None, :] + first_rows[:, 1, :, None] * second_rows[:, 1, None, :]
    imag_part = first_rows[:, 1, :, None] * second_rows[:, 0, None, :] - first_rows[:, 0, :, None] * second_rows[:, 1, None, :]
    return jnp.stack([real_part, imag_part], axis=3)

def pair_gradients(adjoint_rows, first_rows, second_rows):
    adj_real = adjoint_rows[:, :, :, 0]
    adj_imag = adjoint_rows[:, :, :, 1]
    own_real = lax.optimization_barrier(jnp.sum(adj_real * second_rows[:, 0, None] - adj_imag * second_rows[:, 1, None], axis=2))
    own_imag = lax.optimization_barrier(jnp.sum(adj_real * second_rows[:, 1, None] + adj_imag * second_rows[:, 0, None], axis=2))
    far_real = lax.optimization_barrier(jnp.sum(adj_real * first_rows[:, 0, :, None] + adj_imag * first_rows[:, 1, :, None], axis=1))
    far_imag = lax.optimization_barrier(jnp.sum(adj_real * first_rows[:, 1, :, None] - adj_imag * first_rows[:, 0, :, None], axis=1))
    return (jnp.stack([own_real, own_imag], axis=1), jnp.stack([far_real, far_imag], axis=1))

def reference(spectra, observed, own_station, partner_station, pair_count):
    spec_rows = jnp.transpose(spectra, (2, 0, 1, 3))
    phase = phase_table(0, NF, 0, NT)
    cos_full = jnp.cos(phase) / math.sqrt(NF)
    sin_full = jnp.sin(phase) / math.sqrt(NF)
    basis = jnp.concatenate([cos_full.astype(jnp.bfloat16), -sin_full.astype(jnp.bfloat16)], axis=0)
    window = lag_window()
    slot_total = BLOCKS * CAP
    observed_blocks = observed.reshape(BLOCKS, slot_total * 9, NT)
    block_ids = jnp.repeat(jnp.arange(BLOCKS, dtype=jnp.int32), CAP)

    def one_reader(grad_all, inputs):
        reader, own_block, partner_block, count_row, observed_rows = inputs
        own_ids = reader * STA_DEV + own_block.reshape(slot_total)
        far_ids = block_ids * STA_DEV + partner_block.reshape(slot_total)
        alive_mask = (jnp.arange(CAP, dtype=jnp.int32)[None, :] < count_row[:, None]).reshape(slot_total).astype(jnp.float32)
        first_rows = spec_rows[own_ids].astype(jnp.float32)
        second_rows = spec_rows[far_ids].astype(jnp.float32)
        cross = (cross_spectra(first_rows, second_rows) * alive_mask[:, None, None, None, None]).astype(jnp.bfloat16)
        correlation = jnp.dot(cross.reshape(slot_total * 9, 2 * NF), basis, preferred_element_type=jnp.float32)
        residual = ((correlation - observed_rows.astype(jnp.float32)) * jnp.repeat(alive_mask, 9)[:, None] * window[None, :]).astype(jnp.bfloat16)
        adjoint_rows = lax.dot_general(residual, basis, (((1,), (1,)), ((), ())), preferred_element_type=jnp.float32).astype(jnp.bfloat16)
        own_grad, far_grad = pair_gradients(adjoint_rows.reshape(slot_total, 3, 3, 2, NF).astype(jnp.float32), first_rows, second_rows)
        grad_all = grad_all.at[own_ids].add(own_grad).at[far_ids].add(far_grad)
        return (grad_all, None)
    grad_start = jnp.zeros((STATIONS, 2, 3, NF), jnp.float32)
    readers = jnp.arange(BLOCKS, dtype=jnp.int32)
    grad_all, unused = lax.scan(one_reader, grad_start, (readers, own_station, partner_station, pair_count, observed_blocks))
    output_scale = 1.0 / math.sqrt(2.0 * BLOCKS * CAP / STA_DEV)
    real_term = jnp.einsum('sak,kt->tas', grad_all[:, 0], cos_full, precision=lax.Precision.HIGHEST)
    imag_term = jnp.einsum('sak,kt->tas', grad_all[:, 1], sin_full, precision=lax.Precision.HIGHEST)
    return (real_term - imag_term) * output_scale
```

```python
import math

import jax
import jax.numpy as jnp
from jax import lax
from jax.sharding import PartitionSpec as P

NF = 512
NT = 1024


def phase_table(freq_start, freq_count, time_count):
    freq_index = lax.iota(jnp.int32, freq_count) + freq_start
    time_index = lax.iota(jnp.int32, time_count)
    phase_num = (2 * freq_index + 1)[:, None] * time_index[None, :] % (2 * NT)
    return phase_num.astype(jnp.float32) * (math.pi / NT)


def lag_window():
    time_index = lax.iota(jnp.int32, NT)
    lag_size = jnp.minimum(time_index, NT - time_index)
    return ((lag_size >= NT // 32) & (lag_size < NT // 4)).astype(jnp.float32)


def cross_spectra(first_rows, second_rows):
    real_part = (
        first_rows[:, 0, :, None] * second_rows[:, 0, None, :]
        + first_rows[:, 1, :, None] * second_rows[:, 1, None, :]
    )
    imag_part = (
        first_rows[:, 1, :, None] * second_rows[:, 0, None, :]
        - first_rows[:, 0, :, None] * second_rows[:, 1, None, :]
    )
    return jnp.stack([real_part, imag_part], axis=3)


def pair_gradients(adjoint_rows, first_rows, second_rows):
    adj_real = adjoint_rows[:, :, :, 0]
    adj_imag = adjoint_rows[:, :, :, 1]
    own_real = jnp.sum(
        adj_real * second_rows[:, 0, None] - adj_imag * second_rows[:, 1, None], axis=2
    )
    own_imag = jnp.sum(
        adj_real * second_rows[:, 1, None] + adj_imag * second_rows[:, 0, None], axis=2
    )
    far_real = jnp.sum(
        adj_real * first_rows[:, 0, :, None] + adj_imag * first_rows[:, 1, :, None], axis=1
    )
    far_imag = jnp.sum(
        adj_real * first_rows[:, 1, :, None] - adj_imag * first_rows[:, 0, :, None], axis=1
    )
    return (jnp.stack([own_real, own_imag], axis=1), jnp.stack([far_real, far_imag], axis=1))


def local(spectra, observed, own_station, partner_station, pair_count):
    block_total = lax.axis_size("blk")
    band_total = lax.axis_size("frq")
    per_block = spectra.shape[2]
    freq_dev = spectra.shape[3]
    slot_cap = own_station.shape[2]
    slot_total = block_total * slot_cap
    item_count = slot_total // band_total
    band_index = lax.axis_index("frq")
    spec_rows = jnp.transpose(spectra, (2, 0, 1, 3))
    own_ids = own_station[0].reshape(slot_total)
    partner_local = partner_station[0]
    partner_ids = partner_local.reshape(slot_total)
    alive_mask = (
        (lax.iota(jnp.int32, slot_cap)[None, :] < pair_count[0][:, None])
        .reshape(slot_total)
        .astype(jnp.float32)
    )
    own_rows = jnp.take(spec_rows, own_ids, axis=0)
    asked_ids = lax.all_to_all(partner_local, "blk", split_axis=0, concat_axis=0, tiled=True)
    asked_rows = jnp.take(spec_rows, asked_ids.reshape(slot_total), axis=0)
    rows_new = lax.all_to_all(
        asked_rows.reshape(block_total, slot_cap * 2 * 3 * freq_dev),
        "blk",
        split_axis=0,
        concat_axis=0,
        tiled=True,
    ).reshape(slot_total, 2, 3, freq_dev)
    cross_new = (
        cross_spectra(own_rows.astype(jnp.float32), rows_new.astype(jnp.float32))
        * alive_mask[:, None, None, None, None]
    ).astype(jnp.bfloat16)
    phase = phase_table(0, NF, NT)
    basis = jnp.concatenate(
        [
            (jnp.cos(phase) / math.sqrt(NF)).astype(jnp.bfloat16),
            -(jnp.sin(phase) / math.sqrt(NF)).astype(jnp.bfloat16),
        ],
        axis=0,
    )
    window = lag_window()
    alive_band = lax.dynamic_slice_in_dim(alive_mask, band_index * item_count, item_count)
    observed_rows = observed.reshape(item_count * 9, NT).astype(jnp.float32)
    station_iota = lax.iota(jnp.int32, per_block)
    sent = cross_new.reshape(band_total, item_count, 3, 3, 2, freq_dev)
    whole_band = lax.all_to_all(sent, "frq", split_axis=0, concat_axis=5, tiled=True)
    correlation = jnp.dot(
        whole_band.reshape(item_count * 9, 2 * NF), basis, preferred_element_type=jnp.float32
    )
    residual = (
        (correlation - observed_rows) * jnp.repeat(alive_band, 9)[:, None] * window[None, :]
    ).astype(jnp.bfloat16)
    adjoint_rows = (
        lax.dot_general(
            residual, basis, (((1,), (1,)), ((), ())), preferred_element_type=jnp.float32
        )
        .astype(jnp.bfloat16)
        .reshape(1, item_count, 3, 3, 2, NF)
    )
    returned = lax.all_to_all(adjoint_rows, "frq", split_axis=5, concat_axis=0, tiled=True).reshape(
        slot_total, 3, 3, 2, freq_dev
    )
    own_grad, far_grad = pair_gradients(
        returned.astype(jnp.float32), own_rows.astype(jnp.float32), rows_new.astype(jnp.float32)
    )
    own_onehot = (own_ids[None, :] == station_iota[:, None]).astype(jnp.float32)
    grad_local = jnp.dot(
        own_onehot,
        own_grad.reshape(slot_total, 6 * freq_dev),
        precision=lax.Precision.HIGHEST,
        preferred_element_type=jnp.float32,
    )
    far_block = far_grad.reshape(block_total, slot_cap, 2, 3, freq_dev)
    back_grad, back_ids = (
        lax.all_to_all(
            far_block.astype(jnp.bfloat16), "blk", split_axis=0, concat_axis=0, tiled=True
        ).astype(far_block.dtype),
        asked_ids,
    )
    back_onehot = (back_ids.reshape(slot_total)[None, :] == station_iota[:, None]).astype(
        jnp.float32
    )
    station_grad = grad_local + jnp.dot(
        back_onehot,
        back_grad.reshape(slot_total, 6 * freq_dev),
        precision=lax.Precision.HIGHEST,
        preferred_element_type=jnp.float32,
    )
    grad_matrix = jnp.transpose(
        station_grad.reshape(per_block, 2, 3, freq_dev), (1, 3, 2, 0)
    ).reshape(2 * freq_dev, 3 * per_block)
    output_scale = 1.0 / math.sqrt(2.0 * block_total * slot_cap / per_block)
    phase_part = phase_table(
        band_index * freq_dev, freq_dev, NT // band_total * lax.axis_size("frq")
    )
    basis_part = jnp.concatenate(
        [jnp.cos(phase_part) / math.sqrt(NF), -(jnp.sin(phase_part) / math.sqrt(NF))], axis=0
    )
    product = lax.dot_general(
        basis_part,
        grad_matrix,
        (((0,), (0,)), ((), ())),
        precision=lax.Precision.HIGHEST,
        preferred_element_type=jnp.float32,
    )
    return lax.psum_scatter(
        product.reshape(NT // band_total * lax.axis_size("frq"), 3, per_block) * output_scale,
        "frq",
        scatter_dimension=0,
        tiled=True,
    )


def solution(mesh):
    return jax.shard_map(
        local,
        mesh=mesh,
        in_specs=(
            P(None, None, "blk", "frq"),
            P(("blk", "frq"), None, None, None),
            P("blk", None, None),
            P("blk", None, None),
            P("blk", None),
        ),
        out_specs=P("frq", None, "blk"),
        check_vma=False,
    )
```

```python
import math

import jax
import jax.numpy as jnp
from jax import lax
from jax.sharding import PartitionSpec as P

NF = 512
NT = 1024


def phase_table(freq_start, freq_count, time_count):
    freq_index = lax.iota(jnp.int32, freq_count) + freq_start
    time_index = lax.iota(jnp.int32, time_count)
    phase_num = (2 * freq_index + 1)[:, None] * time_index[None, :] % (2 * NT)
    return phase_num.astype(jnp.float32) * (math.pi / NT)


def lag_window():
    time_index = lax.iota(jnp.int32, NT)
    lag_size = jnp.minimum(time_index, NT - time_index)
    return ((lag_size >= NT // 32) & (lag_size < NT // 4)).astype(jnp.float32)


def cross_spectra(first_rows, second_rows):
    real_part = (
        first_rows[:, 0, :, None] * second_rows[:, 0, None, :]
        + first_rows[:, 1, :, None] * second_rows[:, 1, None, :]
    )
    imag_part = (
        first_rows[:, 1, :, None] * second_rows[:, 0, None, :]
        - first_rows[:, 0, :, None] * second_rows[:, 1, None, :]
    )
    return jnp.stack([real_part, imag_part], axis=3)


def pair_gradients(adjoint_rows, first_rows, second_rows):
    adj_real = adjoint_rows[:, :, :, 0]
    adj_imag = adjoint_rows[:, :, :, 1]
    own_real = jnp.sum(
        adj_real * second_rows[:, 0, None] - adj_imag * second_rows[:, 1, None], axis=2
    )
    own_imag = jnp.sum(
        adj_real * second_rows[:, 1, None] + adj_imag * second_rows[:, 0, None], axis=2
    )
    far_real = jnp.sum(
        adj_real * first_rows[:, 0, :, None] + adj_imag * first_rows[:, 1, :, None], axis=1
    )
    far_imag = jnp.sum(
        adj_real * first_rows[:, 1, :, None] - adj_imag * first_rows[:, 0, :, None], axis=1
    )
    return (jnp.stack([own_real, own_imag], axis=1), jnp.stack([far_real, far_imag], axis=1))


def local(spectra, observed, own_station, partner_station, pair_count):
    block_total = lax.axis_size("blk")
    band_total = lax.axis_size("frq")
    per_block = spectra.shape[2]
    freq_dev = spectra.shape[3]
    slot_cap = own_station.shape[2]
    slot_total = block_total * slot_cap
    item_count = slot_total // band_total
    band_index = lax.axis_index("frq")
    spec_rows = jnp.transpose(spectra, (2, 0, 1, 3))
    own_ids = own_station[0].reshape(slot_total)
    partner_local = partner_station[0]
    partner_ids = partner_local.reshape(slot_total)
    alive_mask = (
        (lax.iota(jnp.int32, slot_cap)[None, :] < pair_count[0][:, None])
        .reshape(slot_total)
        .astype(jnp.float32)
    )
    own_rows = jnp.take(spec_rows, own_ids, axis=0)
    asked_ids = lax.all_to_all(partner_local, "blk", split_axis=0, concat_axis=0, tiled=True)
    asked_rows = jnp.take(spec_rows, asked_ids.reshape(slot_total), axis=0)
    rows_new = lax.all_to_all(
        asked_rows.reshape(block_total, slot_cap * 2 * 3 * freq_dev),
        "blk",
        split_axis=0,
        concat_axis=0,
        tiled=True,
    ).reshape(slot_total, 2, 3, freq_dev)
    cross_new = (
        cross_spectra(own_rows.astype(jnp.float32), rows_new.astype(jnp.float32))
        * alive_mask[:, None, None, None, None]
    ).astype(jnp.bfloat16)
    phase = phase_table(0, NF, NT)
    basis = jnp.concatenate(
        [
            (jnp.cos(phase) / math.sqrt(NF)).astype(jnp.bfloat16),
            -(jnp.sin(phase) / math.sqrt(NF)).astype(jnp.bfloat16),
        ],
        axis=0,
    )
    window = lag_window()
    alive_band = lax.dynamic_slice_in_dim(alive_mask, band_index * item_count, item_count)
    observed_rows = observed.reshape(item_count * 9, NT).astype(jnp.float32)
    station_iota = lax.iota(jnp.int32, per_block)
    sent = cross_new.reshape(band_total, item_count, 3, 3, 2, freq_dev)
    whole_band = lax.all_to_all(sent, "frq", split_axis=0, concat_axis=5, tiled=True)
    correlation = jnp.dot(
        whole_band.reshape(item_count * 9, 2 * NF), basis, preferred_element_type=jnp.float32
    )
    residual = (
        (correlation - observed_rows) * jnp.repeat(alive_band, 9)[:, None] * window[None, :]
    ).astype(jnp.bfloat16)
    adjoint_rows = (
        lax.dot_general(
            residual, basis, (((1,), (1,)), ((), ())), preferred_element_type=jnp.float32
        )
        .astype(jnp.bfloat16)
        .reshape(1, item_count, 3, 3, 2, NF)
    )
    returned = lax.all_to_all(adjoint_rows, "frq", split_axis=5, concat_axis=0, tiled=True).reshape(
        slot_total, 3, 3, 2, freq_dev
    )
    own_grad, far_grad = pair_gradients(
        returned.astype(jnp.float32), own_rows.astype(jnp.float32), rows_new.astype(jnp.float32)
    )
    own_onehot = (own_ids[None, :] == station_iota[:, None]).astype(jnp.float32)
    grad_local = jnp.dot(
        own_onehot,
        own_grad.reshape(slot_total, 6 * freq_dev),
        precision=lax.Precision.HIGHEST,
        preferred_element_type=jnp.float32,
    )
    far_block = far_grad.reshape(block_total, slot_cap, 2, 3, freq_dev)
    back_grad, back_ids = (
        lax.all_to_all(
            far_block.astype(jnp.bfloat16), "blk", split_axis=0, concat_axis=0, tiled=True
        ).astype(far_block.dtype),
        asked_ids,
    )
    back_onehot = (back_ids.reshape(slot_total)[None, :] == station_iota[:, None]).astype(
        jnp.float32
    )
    station_grad = grad_local + jnp.dot(
        back_onehot,
        back_grad.reshape(slot_total, 6 * freq_dev),
        precision=lax.Precision.HIGHEST,
        preferred_element_type=jnp.float32,
    )
    grad_matrix = jnp.transpose(
        station_grad.reshape(per_block, 2, 3, freq_dev), (1, 3, 2, 0)
    ).reshape(2 * freq_dev, 3 * per_block)
    output_scale = 1.0 / math.sqrt(2.0 * block_total * slot_cap / per_block)
    phase_part = phase_table(
        band_index * freq_dev, freq_dev, NT // band_total * lax.axis_size("frq")
    )
    basis_part = jnp.concatenate(
        [jnp.cos(phase_part) / math.sqrt(NF), -(jnp.sin(phase_part) / math.sqrt(NF))], axis=0
    )
    product = lax.dot_general(
        basis_part,
        grad_matrix,
        (((0,), (0,)), ((), ())),
        precision=lax.Precision.HIGHEST,
        preferred_element_type=jnp.float32,
    )
    lag_parts = lax.all_to_all(
        product.reshape(band_total, NT // band_total, 3, per_block) * output_scale,
        "frq",
        split_axis=0,
        concat_axis=0,
        tiled=True,
    )
    return jnp.sum(lag_parts, axis=0)


def solution(mesh):
    return jax.shard_map(
        local,
        mesh=mesh,
        in_specs=(
            P(None, None, "blk", "frq"),
            P(("blk", "frq"), None, None, None),
            P("blk", None, None),
            P("blk", None, None),
            P("blk", None),
        ),
        out_specs=P("frq", None, "blk"),
        check_vma=False,
    )
```

```python
import math

import jax
import jax.numpy as jnp
from jax import lax
from jax.sharding import PartitionSpec as P

NF = 512
NT = 1024


def phase_table(freq_start, freq_count, time_count):
    freq_index = lax.iota(jnp.int32, freq_count) + freq_start
    time_index = lax.iota(jnp.int32, time_count)
    phase_num = (2 * freq_index + 1)[:, None] * time_index[None, :] % (2 * NT)
    return phase_num.astype(jnp.float32) * (math.pi / NT)


def lag_window():
    time_index = lax.iota(jnp.int32, NT)
    lag_size = jnp.minimum(time_index, NT - time_index)
    return ((lag_size >= NT // 32) & (lag_size < NT // 4)).astype(jnp.float32)


def cross_spectra(first_rows, second_rows):
    real_part = (
        first_rows[:, 0, :, None] * second_rows[:, 0, None, :]
        + first_rows[:, 1, :, None] * second_rows[:, 1, None, :]
    )
    imag_part = (
        first_rows[:, 1, :, None] * second_rows[:, 0, None, :]
        - first_rows[:, 0, :, None] * second_rows[:, 1, None, :]
    )
    return jnp.stack([real_part, imag_part], axis=3)


def pair_gradients(adjoint_rows, first_rows, second_rows):
    adj_real = adjoint_rows[:, :, :, 0]
    adj_imag = adjoint_rows[:, :, :, 1]
    own_real = jnp.sum(
        adj_real * second_rows[:, 0, None] - adj_imag * second_rows[:, 1, None], axis=2
    )
    own_imag = jnp.sum(
        adj_real * second_rows[:, 1, None] + adj_imag * second_rows[:, 0, None], axis=2
    )
    far_real = jnp.sum(
        adj_real * first_rows[:, 0, :, None] + adj_imag * first_rows[:, 1, :, None], axis=1
    )
    far_imag = jnp.sum(
        adj_real * first_rows[:, 1, :, None] - adj_imag * first_rows[:, 0, :, None], axis=1
    )
    return (jnp.stack([own_real, own_imag], axis=1), jnp.stack([far_real, far_imag], axis=1))


def local(spectra, observed, own_station, partner_station, pair_count):
    block_total = lax.axis_size("blk")
    band_total = lax.axis_size("frq")
    per_block = spectra.shape[2]
    freq_dev = spectra.shape[3]
    slot_cap = own_station.shape[2]
    slot_total = block_total * slot_cap
    item_count = slot_total // band_total
    band_index = lax.axis_index("frq")
    spec_rows = jnp.transpose(spectra, (2, 0, 1, 3))
    own_ids = own_station[0].reshape(slot_total)
    partner_local = partner_station[0]
    partner_ids = partner_local.reshape(slot_total)
    alive_mask = (
        (lax.iota(jnp.int32, slot_cap)[None, :] < pair_count[0][:, None])
        .reshape(slot_total)
        .astype(jnp.float32)
    )
    own_rows = jnp.take(spec_rows, own_ids, axis=0)
    asked_ids = lax.all_to_all(partner_local, "blk", split_axis=0, concat_axis=0, tiled=True)
    asked_rows = jnp.take(spec_rows, asked_ids.reshape(slot_total), axis=0)
    rows_new = lax.all_to_all(
        asked_rows.reshape(block_total, slot_cap * 2 * 3 * freq_dev),
        "blk",
        split_axis=0,
        concat_axis=0,
        tiled=True,
    ).reshape(slot_total, 2, 3, freq_dev)
    cross_new = (
        cross_spectra(own_rows.astype(jnp.float32), rows_new.astype(jnp.float32))
        * alive_mask[:, None, None, None, None]
    ).astype(jnp.bfloat16)
    lag_low = NT // 32
    lag_high = NT // 4
    lag_index = jnp.concatenate(
        [
            lax.iota(jnp.int32, lag_high - lag_low) + lag_low,
            lax.iota(jnp.int32, lag_high - lag_low) + (NT - lag_high + 1),
        ]
    )
    phase = (2 * lax.iota(jnp.int32, NF) + 1)[:, None] * lag_index[None, :] % (2 * NT)
    phase = phase.astype(jnp.float32) * (math.pi / NT)
    basis = jnp.concatenate(
        [
            (jnp.cos(phase) / math.sqrt(NF)).astype(jnp.bfloat16),
            -(jnp.sin(phase) / math.sqrt(NF)).astype(jnp.bfloat16),
        ],
        axis=0,
    )
    window = lag_window()[lag_index]
    alive_band = lax.dynamic_slice_in_dim(alive_mask, band_index * item_count, item_count)
    observed_all = observed.reshape(item_count * 9, NT)
    observed_rows = jnp.concatenate(
        [
            observed_all[:, lag_low:lag_high],
            observed_all[:, NT - lag_high + 1 : NT - lag_low + 1],
        ],
        axis=1,
    ).astype(jnp.float32)
    station_iota = lax.iota(jnp.int32, per_block)
    sent = cross_new.reshape(band_total, item_count, 3, 3, 2, freq_dev)
    whole_band = lax.all_to_all(sent, "frq", split_axis=0, concat_axis=5, tiled=True)
    correlation = jnp.dot(
        whole_band.reshape(item_count * 9, 2 * NF), basis, preferred_element_type=jnp.float32
    )
    residual = (
        (correlation - observed_rows) * jnp.repeat(alive_band, 9)[:, None] * window[None, :]
    ).astype(jnp.bfloat16)
    adjoint_rows = (
        lax.dot_general(
            residual, basis, (((1,), (1,)), ((), ())), preferred_element_type=jnp.float32
        )
        .astype(jnp.bfloat16)
        .reshape(1, item_count, 3, 3, 2, NF)
    )
    returned = lax.all_to_all(adjoint_rows, "frq", split_axis=5, concat_axis=0, tiled=True).reshape(
        slot_total, 3, 3, 2, freq_dev
    )
    own_grad, far_grad = pair_gradients(
        returned.astype(jnp.float32), own_rows.astype(jnp.float32), rows_new.astype(jnp.float32)
    )
    own_onehot = (own_ids[None, :] == station_iota[:, None]).astype(jnp.float32)
    grad_local = jnp.dot(
        own_onehot,
        own_grad.reshape(slot_total, 6 * freq_dev),
        precision=lax.Precision.HIGHEST,
        preferred_element_type=jnp.float32,
    )
    far_block = far_grad.reshape(block_total, slot_cap, 2, 3, freq_dev)
    back_grad, back_ids = (
        lax.all_to_all(
            far_block.astype(jnp.bfloat16), "blk", split_axis=0, concat_axis=0, tiled=True
        ).astype(far_block.dtype),
        asked_ids,
    )
    back_onehot = (back_ids.reshape(slot_total)[None, :] == station_iota[:, None]).astype(
        jnp.float32
    )
    station_grad = grad_local + jnp.dot(
        back_onehot,
        back_grad.reshape(slot_total, 6 * freq_dev),
        precision=lax.Precision.HIGHEST,
        preferred_element_type=jnp.float32,
    )
    grad_matrix = jnp.transpose(
        station_grad.reshape(per_block, 2, 3, freq_dev), (1, 3, 2, 0)
    ).reshape(2 * freq_dev, 3 * per_block)
    output_scale = 1.0 / math.sqrt(2.0 * block_total * slot_cap / per_block)
    phase_part = phase_table(
        band_index * freq_dev, freq_dev, NT // band_total * lax.axis_size("frq")
    )
    basis_part = jnp.concatenate(
        [jnp.cos(phase_part) / math.sqrt(NF), -(jnp.sin(phase_part) / math.sqrt(NF))], axis=0
    )
    product = lax.dot_general(
        basis_part,
        grad_matrix,
        (((0,), (0,)), ((), ())),
        precision=lax.Precision.HIGHEST,
        preferred_element_type=jnp.float32,
    )
    lag_parts = lax.all_to_all(
        product.reshape(band_total, NT // band_total, 3, per_block) * output_scale,
        "frq",
        split_axis=0,
        concat_axis=0,
        tiled=True,
    )
    return jnp.sum(lag_parts, axis=0)


def solution(mesh):
    return jax.shard_map(
        local,
        mesh=mesh,
        in_specs=(
            P(None, None, "blk", "frq"),
            P(("blk", "frq"), None, None, None),
            P("blk", None, None),
            P("blk", None, None),
            P("blk", None),
        ),
        out_specs=P("frq", None, "blk"),
        check_vma=False,
    )
```

```python
import math

import jax
import jax.numpy as jnp
from jax import lax
from jax.sharding import PartitionSpec as P

NF = 512
NT = 1024


def phase_table(freq_start, freq_count, time_count):
    freq_index = lax.iota(jnp.int32, freq_count) + freq_start
    time_index = lax.iota(jnp.int32, time_count)
    phase_num = (2 * freq_index + 1)[:, None] * time_index[None, :] % (2 * NT)
    return phase_num.astype(jnp.float32) * (math.pi / NT)


def lag_window():
    time_index = lax.iota(jnp.int32, NT)
    lag_size = jnp.minimum(time_index, NT - time_index)
    return ((lag_size >= NT // 32) & (lag_size < NT // 4)).astype(jnp.float32)


def cross_spectra(first_rows, second_rows):
    real_part = (
        first_rows[:, 0, :, None] * second_rows[:, 0, None, :]
        + first_rows[:, 1, :, None] * second_rows[:, 1, None, :]
    )
    imag_part = (
        first_rows[:, 1, :, None] * second_rows[:, 0, None, :]
        - first_rows[:, 0, :, None] * second_rows[:, 1, None, :]
    )
    return jnp.stack([real_part, imag_part], axis=3)


def pair_gradients(adjoint_rows, first_rows, second_rows):
    adj_real = adjoint_rows[:, :, :, 0]
    adj_imag = adjoint_rows[:, :, :, 1]
    own_real = jnp.sum(
        adj_real * second_rows[:, 0, None] - adj_imag * second_rows[:, 1, None], axis=2
    )
    own_imag = jnp.sum(
        adj_real * second_rows[:, 1, None] + adj_imag * second_rows[:, 0, None], axis=2
    )
    far_real = jnp.sum(
        adj_real * first_rows[:, 0, :, None] + adj_imag * first_rows[:, 1, :, None], axis=1
    )
    far_imag = jnp.sum(
        adj_real * first_rows[:, 1, :, None] - adj_imag * first_rows[:, 0, :, None], axis=1
    )
    return (jnp.stack([own_real, own_imag], axis=1), jnp.stack([far_real, far_imag], axis=1))


def local(spectra, observed, own_station, partner_station, pair_count):
    block_total = lax.axis_size("blk")
    band_total = lax.axis_size("frq")
    per_block = spectra.shape[2]
    freq_dev = spectra.shape[3]
    slot_cap = own_station.shape[2]
    slot_total = block_total * slot_cap
    item_count = slot_total // band_total
    band_index = lax.axis_index("frq")
    spec_rows = jnp.transpose(spectra, (2, 0, 1, 3))
    own_ids = own_station[0].reshape(slot_total)
    partner_local = partner_station[0]
    partner_ids = partner_local.reshape(slot_total)
    alive_mask = (
        (lax.iota(jnp.int32, slot_cap)[None, :] < pair_count[0][:, None])
        .reshape(slot_total)
        .astype(jnp.float32)
    )
    asked_ids = lax.all_to_all(partner_local, "blk", split_axis=0, concat_axis=0, tiled=True)
    asked_rows = jnp.take(spec_rows, asked_ids.reshape(slot_total), axis=0)
    rows_new = lax.all_to_all(
        asked_rows.reshape(block_total, slot_cap * 2 * 3 * freq_dev),
        "blk",
        split_axis=0,
        concat_axis=0,
        tiled=True,
    ).reshape(band_total, item_count, 2, 3, freq_dev)
    own_table = jnp.broadcast_to(spec_rows[None], (band_total, per_block, 2, 3, freq_dev))
    sent = jnp.concatenate([rows_new, own_table], axis=1)
    whole_band = lax.all_to_all(sent, "frq", split_axis=0, concat_axis=0, tiled=True)
    whole_band = jnp.transpose(whole_band, (1, 2, 3, 0, 4)).reshape(
        item_count + per_block, 2, 3, NF
    )
    second_rows = whole_band[:item_count].astype(jnp.float32)
    own_group = lax.dynamic_slice_in_dim(own_ids, band_index * item_count, item_count)
    first_rows = jnp.take(whole_band[item_count:], own_group, axis=0).astype(jnp.float32)
    alive_band = lax.dynamic_slice_in_dim(alive_mask, band_index * item_count, item_count)
    cross = (cross_spectra(first_rows, second_rows) * alive_band[:, None, None, None, None]).astype(
        jnp.bfloat16
    )
    lag_low = NT // 32
    lag_high = NT // 4
    lag_index = jnp.concatenate(
        [
            lax.iota(jnp.int32, lag_high - lag_low) + lag_low,
            lax.iota(jnp.int32, lag_high - lag_low) + (NT - lag_high + 1),
        ]
    )
    phase = (2 * lax.iota(jnp.int32, NF) + 1)[:, None] * lag_index[None, :] % (2 * NT)
    phase = phase.astype(jnp.float32) * (math.pi / NT)
    basis = jnp.concatenate(
        [
            (jnp.cos(phase) / math.sqrt(NF)).astype(jnp.bfloat16),
            -(jnp.sin(phase) / math.sqrt(NF)).astype(jnp.bfloat16),
        ],
        axis=0,
    )
    window = lag_window()[lag_index]
    observed_all = observed.reshape(item_count * 9, NT)
    observed_rows = jnp.concatenate(
        [
            observed_all[:, lag_low:lag_high],
            observed_all[:, NT - lag_high + 1 : NT - lag_low + 1],
        ],
        axis=1,
    ).astype(jnp.float32)
    station_iota = lax.iota(jnp.int32, per_block)
    correlation = jnp.dot(
        cross.reshape(item_count * 9, 2 * NF), basis, preferred_element_type=jnp.float32
    )
    residual = (
        (correlation - observed_rows) * jnp.repeat(alive_band, 9)[:, None] * window[None, :]
    ).astype(jnp.bfloat16)
    adjoint_rows = (
        lax.dot_general(
            residual, basis, (((1,), (1,)), ((), ())), preferred_element_type=jnp.float32
        )
        .astype(jnp.bfloat16)
        .reshape(item_count, 3, 3, 2, NF)
    )
    own_grad, far_grad = pair_gradients(adjoint_rows.astype(jnp.float32), first_rows, second_rows)
    own_onehot = (own_group[None, :] == station_iota[:, None]).astype(jnp.float32)
    grad_group = jnp.dot(
        own_onehot,
        own_grad.reshape(item_count, 6 * NF),
        precision=lax.Precision.HIGHEST,
        preferred_element_type=jnp.float32,
    ).reshape(per_block, 2, 3, NF)
    grad_high = grad_group.astype(jnp.bfloat16)
    grad_low = (grad_group - grad_high.astype(jnp.float32)).astype(jnp.bfloat16)
    back_sent = jnp.concatenate([far_grad.astype(jnp.bfloat16), grad_high, grad_low], axis=0)
    back_sent = jnp.transpose(
        back_sent.reshape(item_count + 2 * per_block, 2, 3, band_total, freq_dev), (3, 0, 1, 2, 4)
    )
    band_back = lax.all_to_all(back_sent, "frq", split_axis=0, concat_axis=0, tiled=True)
    far_band = band_back[:, :item_count].reshape(block_total, slot_cap * 2 * 3 * freq_dev)
    grad_local = jnp.sum(
        band_back[:, item_count : item_count + per_block].astype(jnp.float32)
        + band_back[:, item_count + per_block :].astype(jnp.float32),
        axis=0,
    ).reshape(per_block, 6 * freq_dev)
    back_grad = lax.all_to_all(far_band, "blk", split_axis=0, concat_axis=0, tiled=True).astype(
        jnp.float32
    )
    back_onehot = (asked_ids.reshape(slot_total)[None, :] == station_iota[:, None]).astype(
        jnp.float32
    )
    station_grad = grad_local + jnp.dot(
        back_onehot,
        back_grad.reshape(slot_total, 6 * freq_dev),
        precision=lax.Precision.HIGHEST,
        preferred_element_type=jnp.float32,
    )
    grad_matrix = jnp.transpose(
        station_grad.reshape(per_block, 2, 3, freq_dev), (1, 3, 2, 0)
    ).reshape(2 * freq_dev, 3 * per_block)
    output_scale = 1.0 / math.sqrt(2.0 * block_total * slot_cap / per_block)
    phase_part = phase_table(
        band_index * freq_dev, freq_dev, NT // band_total * lax.axis_size("frq")
    )
    basis_part = jnp.concatenate(
        [jnp.cos(phase_part) / math.sqrt(NF), -(jnp.sin(phase_part) / math.sqrt(NF))], axis=0
    )
    product = lax.dot_general(
        basis_part,
        grad_matrix,
        (((0,), (0,)), ((), ())),
        precision=lax.Precision.HIGHEST,
        preferred_element_type=jnp.float32,
    )
    lag_parts = lax.all_to_all(
        product.reshape(band_total, NT // band_total, 3, per_block) * output_scale,
        "frq",
        split_axis=0,
        concat_axis=0,
        tiled=True,
    )
    return jnp.sum(lag_parts, axis=0)


def solution(mesh):
    return jax.shard_map(
        local,
        mesh=mesh,
        in_specs=(
            P(None, None, "blk", "frq"),
            P(("blk", "frq"), None, None, None),
            P("blk", None, None),
            P("blk", None, None),
            P("blk", None),
        ),
        out_specs=P("frq", None, "blk"),
        check_vma=False,
    )
```

```python
import math

import jax
import jax.numpy as jnp
from jax import lax
from jax.sharding import PartitionSpec as P

NF = 512
NT = 1024


def phase_table(freq_start, freq_count, time_count):
    freq_index = lax.iota(jnp.int32, freq_count) + freq_start
    time_index = lax.iota(jnp.int32, time_count)
    phase_num = (2 * freq_index + 1)[:, None] * time_index[None, :] % (2 * NT)
    return phase_num.astype(jnp.float32) * (math.pi / NT)


def lag_window():
    time_index = lax.iota(jnp.int32, NT)
    lag_size = jnp.minimum(time_index, NT - time_index)
    return ((lag_size >= NT // 32) & (lag_size < NT // 4)).astype(jnp.float32)


def cross_spectra(first_rows, second_rows):
    real_part = (
        first_rows[:, 0, :, None] * second_rows[:, 0, None, :]
        + first_rows[:, 1, :, None] * second_rows[:, 1, None, :]
    )
    imag_part = (
        first_rows[:, 1, :, None] * second_rows[:, 0, None, :]
        - first_rows[:, 0, :, None] * second_rows[:, 1, None, :]
    )
    return jnp.stack([real_part, imag_part], axis=3)


def pair_gradients(adjoint_rows, first_rows, second_rows):
    adj_real = adjoint_rows[:, :, :, 0]
    adj_imag = adjoint_rows[:, :, :, 1]
    own_real = jnp.sum(
        adj_real * second_rows[:, 0, None] - adj_imag * second_rows[:, 1, None], axis=2
    )
    own_imag = jnp.sum(
        adj_real * second_rows[:, 1, None] + adj_imag * second_rows[:, 0, None], axis=2
    )
    far_real = jnp.sum(
        adj_real * first_rows[:, 0, :, None] + adj_imag * first_rows[:, 1, :, None], axis=1
    )
    far_imag = jnp.sum(
        adj_real * first_rows[:, 1, :, None] - adj_imag * first_rows[:, 0, :, None], axis=1
    )
    return (jnp.stack([own_real, own_imag], axis=1), jnp.stack([far_real, far_imag], axis=1))


def local(spectra, observed, own_station, partner_station, pair_count):
    block_total = lax.axis_size("blk")
    band_total = lax.axis_size("frq")
    per_block = spectra.shape[2]
    freq_dev = spectra.shape[3]
    slot_cap = own_station.shape[2]
    slot_total = block_total * slot_cap
    item_count = slot_total // band_total
    band_index = lax.axis_index("frq")
    spec_rows = jnp.transpose(spectra, (2, 0, 1, 3))
    own_ids = own_station[0].reshape(slot_total)
    partner_local = partner_station[0]
    partner_ids = partner_local.reshape(slot_total)
    alive_mask = (
        (lax.iota(jnp.int32, slot_cap)[None, :] < pair_count[0][:, None])
        .reshape(slot_total)
        .astype(jnp.float32)
    )
    asked_ids = lax.all_to_all(partner_local, "blk", split_axis=0, concat_axis=0, tiled=True)
    asked_rows = jnp.take(spec_rows, asked_ids.reshape(slot_total), axis=0, mode="clip")
    rows_new = lax.all_to_all(
        asked_rows.reshape(block_total, slot_cap * 2 * 3 * freq_dev),
        "blk",
        split_axis=0,
        concat_axis=0,
        tiled=True,
    ).reshape(band_total, item_count, 2, 3, freq_dev)
    own_table = jnp.broadcast_to(spec_rows[None], (band_total, per_block, 2, 3, freq_dev))
    sent = jnp.concatenate([rows_new, own_table], axis=1)
    whole_band = lax.all_to_all(sent, "frq", split_axis=0, concat_axis=0, tiled=True)
    whole_band = jnp.transpose(whole_band, (1, 2, 3, 0, 4)).reshape(
        item_count + per_block, 2, 3, NF
    )
    second_rows = whole_band[:item_count].astype(jnp.float32)
    own_group = lax.dynamic_slice_in_dim(own_ids, band_index * item_count, item_count)
    first_rows = jnp.take(whole_band[item_count:], own_group, axis=0, mode="clip").astype(
        jnp.float32
    )
    alive_band = lax.dynamic_slice_in_dim(alive_mask, band_index * item_count, item_count)
    first_re = first_rows[:, 0, :, None]
    first_im = first_rows[:, 1, :, None]
    second_re = second_rows[:, 0, None]
    second_im = second_rows[:, 1, None]
    alive_col = alive_band[:, None, None, None]
    cross_re = ((first_re * second_re + first_im * second_im) * alive_col).astype(jnp.bfloat16)
    cross_im = ((first_im * second_re - first_re * second_im) * alive_col).astype(jnp.bfloat16)
    lag_low = NT // 32
    lag_high = NT // 4
    lag_index = jnp.concatenate(
        [
            lax.iota(jnp.int32, lag_high - lag_low) + lag_low,
            lax.iota(jnp.int32, lag_high - lag_low) + (NT - lag_high + 1),
        ]
    )
    phase = (2 * lax.iota(jnp.int32, NF) + 1)[:, None] * lag_index[None, :] % (2 * NT)
    phase = phase.astype(jnp.float32) * (math.pi / NT)
    basis_cos = (jnp.cos(phase) / math.sqrt(NF)).astype(jnp.bfloat16)
    basis_sin = (-(jnp.sin(phase) / math.sqrt(NF))).astype(jnp.bfloat16)
    window = lag_window()[lag_index]
    observed_all = observed.reshape(item_count * 9, NT)
    observed_rows = jnp.concatenate(
        [
            observed_all[:, lag_low:lag_high],
            observed_all[:, NT - lag_high + 1 : NT - lag_low + 1],
        ],
        axis=1,
    ).astype(jnp.float32)
    station_iota = lax.iota(jnp.int32, per_block)
    correlation = jnp.dot(
        cross_re.reshape(item_count * 9, NF), basis_cos, preferred_element_type=jnp.float32
    ) + jnp.dot(cross_im.reshape(item_count * 9, NF), basis_sin, preferred_element_type=jnp.float32)
    residual = (
        (correlation - observed_rows) * jnp.repeat(alive_band, 9)[:, None] * window[None, :]
    ).astype(jnp.bfloat16)

    def back_project(table):
        product = lax.dot_general(
            residual, table, (((1,), (1,)), ((), ())), preferred_element_type=jnp.float32
        )
        return lax.reduce_precision(product, exponent_bits=8, mantissa_bits=7).reshape(
            item_count, 3, 3, NF
        )

    adj_re = back_project(basis_cos)
    adj_im = back_project(basis_sin)
    own_re = jnp.sum(adj_re * second_re - adj_im * second_im, axis=2)
    own_im = jnp.sum(adj_re * second_im + adj_im * second_re, axis=2)
    far_re = jnp.sum(adj_re * first_re + adj_im * first_im, axis=1)
    far_im = jnp.sum(adj_re * first_im - adj_im * first_re, axis=1)
    far_grad = jnp.stack([far_re, far_im], axis=1)
    own_onehot = (own_group[None, :] == station_iota[:, None]).astype(jnp.float32)

    def station_sum(part):
        return jnp.dot(
            own_onehot,
            part.reshape(item_count, 3 * NF),
            precision=lax.Precision.HIGHEST,
            preferred_element_type=jnp.float32,
        ).reshape(per_block, 3, NF)

    grad_group = jnp.stack([station_sum(own_re), station_sum(own_im)], axis=1)
    grad_high = lax.reduce_precision(grad_group, exponent_bits=8, mantissa_bits=7)
    grad_low = (grad_group - grad_high).astype(jnp.bfloat16)
    grad_high = grad_high.astype(jnp.bfloat16)
    back_sent = jnp.concatenate([far_grad.astype(jnp.bfloat16), grad_high, grad_low], axis=0)
    back_sent = jnp.transpose(
        back_sent.reshape(item_count + 2 * per_block, 2, 3, band_total, freq_dev), (3, 0, 1, 2, 4)
    )
    band_back = lax.all_to_all(back_sent, "frq", split_axis=0, concat_axis=0, tiled=True)
    far_band = band_back[:, :item_count].reshape(block_total, slot_cap * 2 * 3 * freq_dev)
    grad_local = jnp.sum(
        band_back[:, item_count : item_count + per_block].astype(jnp.float32)
        + band_back[:, item_count + per_block :].astype(jnp.float32),
        axis=0,
    ).reshape(per_block, 6 * freq_dev)
    back_grad = lax.all_to_all(far_band, "blk", split_axis=0, concat_axis=0, tiled=True).astype(
        jnp.float32
    )
    back_onehot = (asked_ids.reshape(slot_total)[None, :] == station_iota[:, None]).astype(
        jnp.float32
    )
    station_grad = grad_local + jnp.dot(
        back_onehot,
        back_grad.reshape(slot_total, 6 * freq_dev),
        precision=lax.Precision.HIGHEST,
        preferred_element_type=jnp.float32,
    )
    grad_matrix = jnp.transpose(
        station_grad.reshape(per_block, 2, 3, freq_dev), (1, 3, 2, 0)
    ).reshape(2 * freq_dev, 3 * per_block)
    output_scale = 1.0 / math.sqrt(2.0 * block_total * slot_cap / per_block)
    phase_part = phase_table(
        band_index * freq_dev, freq_dev, NT // band_total * lax.axis_size("frq")
    )
    basis_part = jnp.concatenate(
        [jnp.cos(phase_part) / math.sqrt(NF), -(jnp.sin(phase_part) / math.sqrt(NF))], axis=0
    )
    product = lax.dot_general(
        basis_part,
        grad_matrix,
        (((0,), (0,)), ((), ())),
        precision=lax.Precision.HIGHEST,
        preferred_element_type=jnp.float32,
    )
    lag_parts = lax.all_to_all(
        product.reshape(band_total, NT // band_total, 3, per_block) * output_scale,
        "frq",
        split_axis=0,
        concat_axis=0,
        tiled=True,
    )
    return jnp.sum(lag_parts, axis=0)


def solution(mesh):
    return jax.shard_map(
        local,
        mesh=mesh,
        in_specs=(
            P(None, None, "blk", "frq"),
            P(("blk", "frq"), None, None, None),
            P("blk", None, None),
            P("blk", None, None),
            P("blk", None),
        ),
        out_specs=P("frq", None, "blk"),
        check_vma=False,
    )
```

```python
import math

import jax
import jax.numpy as jnp
from jax import lax
from jax.sharding import PartitionSpec as P

NF = 512
NT = 1024


def phase_table(freq_start, freq_count, time_count):
    freq_index = lax.iota(jnp.int32, freq_count) + freq_start
    time_index = lax.iota(jnp.int32, time_count)
    phase_num = (2 * freq_index + 1)[:, None] * time_index[None, :] % (2 * NT)
    return phase_num.astype(jnp.float32) * (math.pi / NT)


def lag_window():
    time_index = lax.iota(jnp.int32, NT)
    lag_size = jnp.minimum(time_index, NT - time_index)
    return ((lag_size >= NT // 32) & (lag_size < NT // 4)).astype(jnp.float32)


def cross_spectra(first_rows, second_rows):
    real_part = (
        first_rows[:, 0, :, None] * second_rows[:, 0, None, :]
        + first_rows[:, 1, :, None] * second_rows[:, 1, None, :]
    )
    imag_part = (
        first_rows[:, 1, :, None] * second_rows[:, 0, None, :]
        - first_rows[:, 0, :, None] * second_rows[:, 1, None, :]
    )
    return jnp.stack([real_part, imag_part], axis=3)


def pair_gradients(adjoint_rows, first_rows, second_rows):
    adj_real = adjoint_rows[:, :, :, 0]
    adj_imag = adjoint_rows[:, :, :, 1]
    own_real = jnp.sum(
        adj_real * second_rows[:, 0, None] - adj_imag * second_rows[:, 1, None], axis=2
    )
    own_imag = jnp.sum(
        adj_real * second_rows[:, 1, None] + adj_imag * second_rows[:, 0, None], axis=2
    )
    far_real = jnp.sum(
        adj_real * first_rows[:, 0, :, None] + adj_imag * first_rows[:, 1, :, None], axis=1
    )
    far_imag = jnp.sum(
        adj_real * first_rows[:, 1, :, None] - adj_imag * first_rows[:, 0, :, None], axis=1
    )
    return (jnp.stack([own_real, own_imag], axis=1), jnp.stack([far_real, far_imag], axis=1))


def local(spectra, observed, own_station, partner_station, pair_count):
    block_total = lax.axis_size("blk")
    band_total = lax.axis_size("frq")
    per_block = spectra.shape[2]
    freq_dev = spectra.shape[3]
    slot_cap = own_station.shape[2]
    slot_total = block_total * slot_cap
    item_count = slot_total // band_total
    band_index = lax.axis_index("frq")
    spec_rows = jnp.transpose(spectra, (2, 0, 1, 3))
    own_ids = own_station[0].reshape(slot_total)
    partner_local = partner_station[0]
    partner_ids = partner_local.reshape(slot_total)
    alive_mask = (
        (lax.iota(jnp.int32, slot_cap)[None, :] < pair_count[0][:, None])
        .reshape(slot_total)
        .astype(jnp.float32)
    )
    asked_ids = lax.all_to_all(partner_local, "blk", split_axis=0, concat_axis=0, tiled=True)
    asked_rows = jnp.take(spec_rows, asked_ids.reshape(slot_total), axis=0, mode="clip")
    rows_new = lax.all_to_all(
        asked_rows.reshape(block_total, slot_cap * 2 * 3 * freq_dev),
        "blk",
        split_axis=0,
        concat_axis=0,
        tiled=True,
    ).reshape(band_total, item_count, 2, 3, freq_dev)
    own_table = jnp.broadcast_to(spec_rows[None], (band_total, per_block, 2, 3, freq_dev))
    sent = jnp.concatenate([rows_new, own_table], axis=1)
    whole_band = lax.all_to_all(sent, "frq", split_axis=0, concat_axis=0, tiled=True)
    whole_band = jnp.transpose(whole_band, (2, 3, 1, 0, 4)).reshape(
        2, 3, item_count + per_block, NF
    )
    second_rows = whole_band[:, :, :item_count].astype(jnp.float32)
    own_group = lax.dynamic_slice_in_dim(own_ids, band_index * item_count, item_count)
    first_rows = jnp.take(
        whole_band[:, :, item_count:], own_group, axis=2, mode="clip"
    ).astype(jnp.float32)
    alive_band = lax.dynamic_slice_in_dim(alive_mask, band_index * item_count, item_count)
    first_re = first_rows[0][:, None]
    first_im = first_rows[1][:, None]
    second_re = second_rows[0][None]
    second_im = second_rows[1][None]
    alive_col = alive_band[None, None, :, None]
    cross = (
        jnp.concatenate(
            [
                first_re * second_re + first_im * second_im,
                first_im * second_re - first_re * second_im,
            ],
            axis=3,
        )
        * alive_col
    ).astype(jnp.bfloat16)
    lag_low = NT // 32
    lag_high = NT // 4
    lag_index = jnp.concatenate(
        [
            lax.iota(jnp.int32, lag_high - lag_low) + lag_low,
            lax.iota(jnp.int32, lag_high - lag_low) + (NT - lag_high + 1),
        ]
    )
    phase = (2 * lax.iota(jnp.int32, NF) + 1)[:, None] * lag_index[None, :] % (2 * NT)
    phase = phase.astype(jnp.float32) * (math.pi / NT)
    basis = jnp.concatenate(
        [
            (jnp.cos(phase) / math.sqrt(NF)).astype(jnp.bfloat16),
            -(jnp.sin(phase) / math.sqrt(NF)).astype(jnp.bfloat16),
        ],
        axis=0,
    )
    window = lag_window()[lag_index]
    observed_all = jnp.transpose(observed, (1, 2, 0, 3)).reshape(9 * item_count, NT)
    observed_rows = jnp.concatenate(
        [
            observed_all[:, lag_low:lag_high],
            observed_all[:, NT - lag_high + 1 : NT - lag_low + 1],
        ],
        axis=1,
    ).astype(jnp.float32)
    station_iota = lax.iota(jnp.int32, per_block)
    correlation = jnp.dot(
        cross.reshape(9 * item_count, 2 * NF), basis, preferred_element_type=jnp.float32
    )
    residual = (
        (correlation - observed_rows) * jnp.tile(alive_band, 9)[:, None] * window[None, :]
    ).astype(jnp.bfloat16)
    adjoint_rows = lax.reduce_precision(
        lax.dot_general(
            residual, basis, (((1,), (1,)), ((), ())), preferred_element_type=jnp.float32
        ),
        exponent_bits=8,
        mantissa_bits=7,
    ).reshape(3, 3, item_count, 2 * NF)
    adj_re = adjoint_rows[..., :NF]
    adj_im = adjoint_rows[..., NF:]
    own_re = jnp.sum(adj_re * second_re - adj_im * second_im, axis=1)
    own_im = jnp.sum(adj_re * second_im + adj_im * second_re, axis=1)
    far_re = jnp.sum(adj_re * first_re + adj_im * first_im, axis=0)
    far_im = jnp.sum(adj_re * first_im - adj_im * first_re, axis=0)
    own_onehot = (own_group[None, :] == station_iota[:, None]).astype(jnp.float32)
    grad_group = lax.dot_general(
        own_onehot,
        jnp.stack([own_re, own_im]),
        (((1,), (2,)), ((), ())),
        precision=lax.Precision.HIGHEST,
        preferred_element_type=jnp.float32,
    )
    grad_high = lax.reduce_precision(grad_group, exponent_bits=8, mantissa_bits=7)
    grad_low = (grad_group - grad_high).astype(jnp.bfloat16)
    far_grad = jnp.transpose(jnp.stack([far_re, far_im]), (2, 0, 1, 3)).astype(jnp.bfloat16)
    back_sent = jnp.concatenate([far_grad, grad_high.astype(jnp.bfloat16), grad_low], axis=0)
    back_sent = jnp.transpose(
        back_sent.reshape(item_count + 2 * per_block, 2, 3, band_total, freq_dev), (3, 0, 1, 2, 4)
    )
    band_back = lax.all_to_all(back_sent, "frq", split_axis=0, concat_axis=0, tiled=True)
    far_band = band_back[:, :item_count].reshape(block_total, slot_cap * 2 * 3 * freq_dev)
    grad_local = jnp.sum(
        band_back[:, item_count : item_count + per_block].astype(jnp.float32)
        + band_back[:, item_count + per_block :].astype(jnp.float32),
        axis=0,
    ).reshape(per_block, 6 * freq_dev)
    back_grad = lax.all_to_all(far_band, "blk", split_axis=0, concat_axis=0, tiled=True).astype(
        jnp.float32
    )
    back_onehot = (asked_ids.reshape(slot_total)[None, :] == station_iota[:, None]).astype(
        jnp.float32
    )
    station_grad = grad_local + jnp.dot(
        back_onehot,
        back_grad.reshape(slot_total, 6 * freq_dev),
        precision=lax.Precision.HIGHEST,
        preferred_element_type=jnp.float32,
    )
    grad_matrix = jnp.transpose(
        station_grad.reshape(per_block, 2, 3, freq_dev), (1, 3, 2, 0)
    ).reshape(2 * freq_dev, 3 * per_block)
    output_scale = 1.0 / math.sqrt(2.0 * block_total * slot_cap / per_block)
    phase_part = phase_table(
        band_index * freq_dev, freq_dev, NT // band_total * lax.axis_size("frq")
    )
    basis_part = jnp.concatenate(
        [jnp.cos(phase_part) / math.sqrt(NF), -(jnp.sin(phase_part) / math.sqrt(NF))], axis=0
    )
    product = lax.dot_general(
        basis_part,
        grad_matrix,
        (((0,), (0,)), ((), ())),
        precision=lax.Precision.HIGHEST,
        preferred_element_type=jnp.float32,
    )
    lag_parts = lax.all_to_all(
        product.reshape(band_total, NT // band_total, 3, per_block) * output_scale,
        "frq",
        split_axis=0,
        concat_axis=0,
        tiled=True,
    )
    return jnp.sum(lag_parts, axis=0)


def solution(mesh):
    return jax.shard_map(
        local,
        mesh=mesh,
        in_specs=(
            P(None, None, "blk", "frq"),
            P(("blk", "frq"), None, None, None),
            P("blk", None, None),
            P("blk", None, None),
            P("blk", None),
        ),
        out_specs=P("frq", None, "blk"),
        check_vma=False,
    )
```

```python
import math

import jax
import jax.numpy as jnp
from jax import lax
from jax.sharding import PartitionSpec as P

NF = 512
NT = 1024


def phase_table(freq_start, freq_count, time_count):
    freq_index = lax.iota(jnp.int32, freq_count) + freq_start
    time_index = lax.iota(jnp.int32, time_count)
    phase_num = (2 * freq_index + 1)[:, None] * time_index[None, :] % (2 * NT)
    return phase_num.astype(jnp.float32) * (math.pi / NT)


def lag_window():
    time_index = lax.iota(jnp.int32, NT)
    lag_size = jnp.minimum(time_index, NT - time_index)
    return ((lag_size >= NT // 32) & (lag_size < NT // 4)).astype(jnp.float32)


def cross_spectra(first_rows, second_rows):
    real_part = (
        first_rows[:, 0, :, None] * second_rows[:, 0, None, :]
        + first_rows[:, 1, :, None] * second_rows[:, 1, None, :]
    )
    imag_part = (
        first_rows[:, 1, :, None] * second_rows[:, 0, None, :]
        - first_rows[:, 0, :, None] * second_rows[:, 1, None, :]
    )
    return jnp.stack([real_part, imag_part], axis=3)


def pair_gradients(adjoint_rows, first_rows, second_rows):
    adj_real = adjoint_rows[:, :, :, 0]
    adj_imag = adjoint_rows[:, :, :, 1]
    own_real = jnp.sum(
        adj_real * second_rows[:, 0, None] - adj_imag * second_rows[:, 1, None], axis=2
    )
    own_imag = jnp.sum(
        adj_real * second_rows[:, 1, None] + adj_imag * second_rows[:, 0, None], axis=2
    )
    far_real = jnp.sum(
        adj_real * first_rows[:, 0, :, None] + adj_imag * first_rows[:, 1, :, None], axis=1
    )
    far_imag = jnp.sum(
        adj_real * first_rows[:, 1, :, None] - adj_imag * first_rows[:, 0, :, None], axis=1
    )
    return (jnp.stack([own_real, own_imag], axis=1), jnp.stack([far_real, far_imag], axis=1))


def blk_exchange(chunks):
    count, width = chunks.shape
    tile = 16 * 128
    padded = -(-width // tile) * tile
    wide = jnp.pad(chunks, ((0, 0), (0, padded - width))).reshape(count, padded // 128, 128)
    moved = lax.all_to_all(wide, "blk", split_axis=0, concat_axis=0, tiled=True)
    return moved.reshape(count, padded)[:, :width]


def local(spectra, observed, own_station, partner_station, pair_count):
    block_total = lax.axis_size("blk")
    band_total = lax.axis_size("frq")
    per_block = spectra.shape[2]
    freq_dev = spectra.shape[3]
    slot_cap = own_station.shape[2]
    slot_total = block_total * slot_cap
    item_count = slot_total // band_total
    band_index = lax.axis_index("frq")
    spec_rows = jnp.transpose(spectra, (2, 0, 1, 3))
    own_ids = own_station[0].reshape(slot_total)
    partner_local = partner_station[0]
    partner_ids = partner_local.reshape(slot_total)
    alive_mask = (
        (lax.iota(jnp.int32, slot_cap)[None, :] < pair_count[0][:, None])
        .reshape(slot_total)
        .astype(jnp.float32)
    )
    asked_ids = lax.all_to_all(partner_local, "blk", split_axis=0, concat_axis=0, tiled=True)
    asked_rows = jnp.take(spec_rows, asked_ids.reshape(slot_total), axis=0, mode="clip")
    rows_new = blk_exchange(asked_rows.reshape(block_total, -1)).reshape(
        band_total, item_count, 2, 3, freq_dev
    )
    own_table = jnp.broadcast_to(spec_rows[None], (band_total, per_block, 2, 3, freq_dev))
    sent = jnp.concatenate([rows_new, own_table], axis=1)
    whole_band = lax.all_to_all(sent, "frq", split_axis=0, concat_axis=0, tiled=True)
    whole_band = jnp.transpose(whole_band, (2, 3, 1, 0, 4)).reshape(
        2, 3, item_count + per_block, NF
    )
    second_rows = whole_band[:, :, :item_count].astype(jnp.float32)
    own_group = lax.dynamic_slice_in_dim(own_ids, band_index * item_count, item_count)
    first_rows = jnp.take(
        whole_band[:, :, item_count:], own_group, axis=2, mode="clip"
    ).astype(jnp.float32)
    alive_band = lax.dynamic_slice_in_dim(alive_mask, band_index * item_count, item_count)
    first_re = first_rows[0][:, None]
    first_im = first_rows[1][:, None]
    second_re = second_rows[0][None]
    second_im = second_rows[1][None]
    alive_col = alive_band[None, None, :, None]
    cross = (
        jnp.concatenate(
            [
                first_re * second_re + first_im * second_im,
                first_im * second_re - first_re * second_im,
            ],
            axis=3,
        )
        * alive_col
    ).astype(jnp.bfloat16)
    lag_low = NT // 32
    lag_high = NT // 4
    lag_index = jnp.concatenate(
        [
            lax.iota(jnp.int32, lag_high - lag_low) + lag_low,
            lax.iota(jnp.int32, lag_high - lag_low) + (NT - lag_high + 1),
        ]
    )
    phase = (2 * lax.iota(jnp.int32, NF) + 1)[:, None] * lag_index[None, :] % (2 * NT)
    phase = phase.astype(jnp.float32) * (math.pi / NT)
    basis = jnp.concatenate(
        [
            (jnp.cos(phase) / math.sqrt(NF)).astype(jnp.bfloat16),
            -(jnp.sin(phase) / math.sqrt(NF)).astype(jnp.bfloat16),
        ],
        axis=0,
    )
    window = lag_window()[lag_index]
    observed_all = jnp.transpose(observed, (1, 2, 0, 3)).reshape(9 * item_count, NT)
    observed_rows = jnp.concatenate(
        [
            observed_all[:, lag_low:lag_high],
            observed_all[:, NT - lag_high + 1 : NT - lag_low + 1],
        ],
        axis=1,
    ).astype(jnp.float32)
    station_iota = lax.iota(jnp.int32, per_block)
    correlation = jnp.dot(
        cross.reshape(9 * item_count, 2 * NF), basis, preferred_element_type=jnp.float32
    )
    residual = (
        (correlation - observed_rows) * jnp.tile(alive_band, 9)[:, None] * window[None, :]
    ).astype(jnp.bfloat16)
    adjoint_rows = lax.reduce_precision(
        lax.dot_general(
            residual, basis, (((1,), (1,)), ((), ())), preferred_element_type=jnp.float32
        ),
        exponent_bits=8,
        mantissa_bits=7,
    ).reshape(3, 3, item_count, 2 * NF)
    adj_re = adjoint_rows[..., :NF]
    adj_im = adjoint_rows[..., NF:]
    own_re = jnp.sum(adj_re * second_re - adj_im * second_im, axis=1)
    own_im = jnp.sum(adj_re * second_im + adj_im * second_re, axis=1)
    far_re = jnp.sum(adj_re * first_re + adj_im * first_im, axis=0)
    far_im = jnp.sum(adj_re * first_im - adj_im * first_re, axis=0)
    own_onehot = (own_group[None, :] == station_iota[:, None]).astype(jnp.float32)
    grad_group = lax.dot_general(
        own_onehot,
        jnp.stack([own_re, own_im]),
        (((1,), (2,)), ((), ())),
        precision=lax.Precision.HIGHEST,
        preferred_element_type=jnp.float32,
    )
    grad_high = lax.reduce_precision(grad_group, exponent_bits=8, mantissa_bits=7)
    grad_low = (grad_group - grad_high).astype(jnp.bfloat16)
    far_grad = jnp.transpose(jnp.stack([far_re, far_im]), (2, 0, 1, 3)).astype(jnp.bfloat16)
    back_sent = jnp.concatenate([far_grad, grad_high.astype(jnp.bfloat16), grad_low], axis=0)
    back_sent = jnp.transpose(
        back_sent.reshape(item_count + 2 * per_block, 2, 3, band_total, freq_dev), (3, 0, 1, 2, 4)
    )
    band_back = lax.all_to_all(back_sent, "frq", split_axis=0, concat_axis=0, tiled=True)
    far_band = band_back[:, :item_count].reshape(block_total, slot_cap * 2 * 3 * freq_dev)
    grad_local = jnp.sum(
        band_back[:, item_count : item_count + per_block].astype(jnp.float32)
        + band_back[:, item_count + per_block :].astype(jnp.float32),
        axis=0,
    ).reshape(per_block, 6 * freq_dev)
    back_grad = blk_exchange(far_band).astype(jnp.float32)
    back_onehot = (asked_ids.reshape(slot_total)[None, :] == station_iota[:, None]).astype(
        jnp.float32
    )
    station_grad = grad_local + jnp.dot(
        back_onehot,
        back_grad.reshape(slot_total, 6 * freq_dev),
        precision=lax.Precision.HIGHEST,
        preferred_element_type=jnp.float32,
    )
    grad_matrix = jnp.transpose(
        station_grad.reshape(per_block, 2, 3, freq_dev), (1, 3, 2, 0)
    ).reshape(2 * freq_dev, 3 * per_block)
    output_scale = 1.0 / math.sqrt(2.0 * block_total * slot_cap / per_block)
    phase_part = phase_table(
        band_index * freq_dev, freq_dev, NT // band_total * lax.axis_size("frq")
    )
    basis_part = jnp.concatenate(
        [jnp.cos(phase_part) / math.sqrt(NF), -(jnp.sin(phase_part) / math.sqrt(NF))], axis=0
    )
    product = lax.dot_general(
        basis_part,
        grad_matrix,
        (((0,), (0,)), ((), ())),
        precision=lax.Precision.HIGHEST,
        preferred_element_type=jnp.float32,
    )
    lag_parts = lax.all_to_all(
        product.reshape(band_total, NT // band_total, 3, per_block) * output_scale,
        "frq",
        split_axis=0,
        concat_axis=0,
        tiled=True,
    )
    return jnp.sum(lag_parts, axis=0)


def solution(mesh):
    return jax.shard_map(
        local,
        mesh=mesh,
        in_specs=(
            P(None, None, "blk", "frq"),
            P(("blk", "frq"), None, None, None),
            P("blk", None, None),
            P("blk", None, None),
            P("blk", None),
        ),
        out_specs=P("frq", None, "blk"),
        check_vma=False,
    )
```

```python
import math

import jax
import jax.numpy as jnp
from jax import lax
from jax.sharding import PartitionSpec as P

NF = 512
NT = 1024


def phase_table(freq_start, freq_count, time_count):
    freq_index = lax.iota(jnp.int32, freq_count) + freq_start
    time_index = lax.iota(jnp.int32, time_count)
    phase_num = (2 * freq_index + 1)[:, None] * time_index[None, :] % (2 * NT)
    return phase_num.astype(jnp.float32) * (math.pi / NT)


def lag_window():
    time_index = lax.iota(jnp.int32, NT)
    lag_size = jnp.minimum(time_index, NT - time_index)
    return ((lag_size >= NT // 32) & (lag_size < NT // 4)).astype(jnp.float32)


def cross_spectra(first_rows, second_rows):
    real_part = (
        first_rows[:, 0, :, None] * second_rows[:, 0, None, :]
        + first_rows[:, 1, :, None] * second_rows[:, 1, None, :]
    )
    imag_part = (
        first_rows[:, 1, :, None] * second_rows[:, 0, None, :]
        - first_rows[:, 0, :, None] * second_rows[:, 1, None, :]
    )
    return jnp.stack([real_part, imag_part], axis=3)


def pair_gradients(adjoint_rows, first_rows, second_rows):
    adj_real = adjoint_rows[:, :, :, 0]
    adj_imag = adjoint_rows[:, :, :, 1]
    own_real = jnp.sum(
        adj_real * second_rows[:, 0, None] - adj_imag * second_rows[:, 1, None], axis=2
    )
    own_imag = jnp.sum(
        adj_real * second_rows[:, 1, None] + adj_imag * second_rows[:, 0, None], axis=2
    )
    far_real = jnp.sum(
        adj_real * first_rows[:, 0, :, None] + adj_imag * first_rows[:, 1, :, None], axis=1
    )
    far_imag = jnp.sum(
        adj_real * first_rows[:, 1, :, None] - adj_imag * first_rows[:, 0, :, None], axis=1
    )
    return (jnp.stack([own_real, own_imag], axis=1), jnp.stack([far_real, far_imag], axis=1))


def blk_exchange(chunks):
    count, width = chunks.shape
    tile = 16 * 128
    padded = -(-width // tile) * tile
    wide = jnp.pad(chunks, ((0, 0), (0, padded - width))).reshape(count, padded // 128, 128)
    moved = lax.all_to_all(wide, "blk", split_axis=0, concat_axis=0, tiled=True)
    return moved.reshape(count, padded)[:, :width]


def local(spectra, observed, own_station, partner_station, pair_count):
    block_total = lax.axis_size("blk")
    band_total = lax.axis_size("frq")
    per_block = spectra.shape[2]
    freq_dev = spectra.shape[3]
    slot_cap = own_station.shape[2]
    slot_total = block_total * slot_cap
    item_count = slot_total // band_total
    band_index = lax.axis_index("frq")
    spec_rows = jnp.transpose(spectra, (2, 0, 1, 3))
    own_ids = own_station[0].reshape(slot_total)
    partner_local = partner_station[0]
    partner_ids = partner_local.reshape(slot_total)
    alive_mask = (
        (lax.iota(jnp.int32, slot_cap)[None, :] < pair_count[0][:, None])
        .reshape(slot_total)
        .astype(jnp.float32)
    )
    asked_ids = lax.all_to_all(partner_local, "blk", split_axis=0, concat_axis=0, tiled=True)
    asked_rows = jnp.take(spec_rows, asked_ids.reshape(slot_total), axis=0, mode="clip")
    rows_new = blk_exchange(asked_rows.reshape(block_total, -1)).reshape(
        band_total, item_count, 2, 3, freq_dev
    )
    own_table = jnp.broadcast_to(spec_rows[None], (band_total, per_block, 2, 3, freq_dev))
    sent = jnp.concatenate([rows_new, own_table], axis=1)
    whole_band = lax.all_to_all(sent, "frq", split_axis=0, concat_axis=0, tiled=True)
    whole_band = jnp.transpose(whole_band, (2, 3, 1, 0, 4)).reshape(
        2, 3, item_count + per_block, NF
    )
    second_rows = whole_band[:, :, :item_count].astype(jnp.float32)
    own_group = lax.dynamic_slice_in_dim(own_ids, band_index * item_count, item_count)
    first_rows = jnp.take(
        whole_band[:, :, item_count:], own_group, axis=2, mode="clip"
    ).astype(jnp.float32)
    alive_band = lax.dynamic_slice_in_dim(alive_mask, band_index * item_count, item_count)
    first_re = first_rows[0][:, None]
    first_im = first_rows[1][:, None]
    second_re = second_rows[0][None]
    second_im = second_rows[1][None]
    alive_col = alive_band[None, None, :, None]
    cross = (
        jnp.concatenate(
            [
                first_re * second_re + first_im * second_im,
                first_im * second_re - first_re * second_im,
            ],
            axis=3,
        )
        * alive_col
    ).astype(jnp.bfloat16)
    lag_low = NT // 32
    lag_high = NT // 4
    lag_index = jnp.concatenate(
        [
            lax.iota(jnp.int32, lag_high - lag_low) + lag_low,
            lax.iota(jnp.int32, lag_high - lag_low) + (NT - lag_high + 1),
        ]
    )
    phase = (2 * lax.iota(jnp.int32, NF) + 1)[:, None] * lag_index[None, :] % (2 * NT)
    phase = phase.astype(jnp.float32) * (math.pi / NT)
    basis = jnp.concatenate(
        [
            (jnp.cos(phase) / math.sqrt(NF)).astype(jnp.bfloat16),
            -(jnp.sin(phase) / math.sqrt(NF)).astype(jnp.bfloat16),
        ],
        axis=0,
    )
    window = lag_window()[lag_index]
    observed_all = jnp.transpose(observed, (1, 2, 0, 3)).reshape(9 * item_count, NT)
    observed_rows = jnp.concatenate(
        [
            observed_all[:, lag_low:lag_high],
            observed_all[:, NT - lag_high + 1 : NT - lag_low + 1],
        ],
        axis=1,
    ).astype(jnp.float32)
    station_iota = lax.iota(jnp.int32, per_block)
    correlation = jnp.dot(
        cross.reshape(9 * item_count, 2 * NF), basis, preferred_element_type=jnp.float32
    )
    residual = (
        (correlation - observed_rows) * jnp.tile(alive_band, 9)[:, None] * window[None, :]
    ).astype(jnp.bfloat16)
    adjoint_rows = lax.reduce_precision(
        lax.dot_general(
            residual, basis, (((1,), (1,)), ((), ())), preferred_element_type=jnp.float32
        ),
        exponent_bits=8,
        mantissa_bits=7,
    ).reshape(3, 3, item_count, 2 * NF)
    adj_re = adjoint_rows[..., :NF]
    adj_im = adjoint_rows[..., NF:]
    own_re = jnp.sum(adj_re * second_re - adj_im * second_im, axis=1)
    own_im = jnp.sum(adj_re * second_im + adj_im * second_re, axis=1)
    far_re = jnp.sum(adj_re * first_re + adj_im * first_im, axis=0)
    far_im = jnp.sum(adj_re * first_im - adj_im * first_re, axis=0)
    own_onehot = (own_group[None, :] == station_iota[:, None]).astype(jnp.float32)
    grad_group = lax.dot_general(
        own_onehot,
        jnp.stack([own_re, own_im]),
        (((1,), (2,)), ((), ())),
        precision=lax.Precision.HIGHEST,
        preferred_element_type=jnp.float32,
    )
    output_scale = 1.0 / math.sqrt(2.0 * block_total * slot_cap / per_block)
    phase_full = phase_table(0, NF, NT)
    cos_full = jnp.cos(phase_full) / math.sqrt(NF)
    sin_full = jnp.sin(phase_full) / math.sqrt(NF)
    own_matrix = jnp.transpose(grad_group, (1, 3, 2, 0)).reshape(2 * NF, 3 * per_block)
    product_own = lax.dot_general(
        jnp.concatenate([cos_full, -sin_full], axis=0),
        own_matrix,
        (((0,), (0,)), ((), ())),
        precision=lax.Precision.HIGHEST,
        preferred_element_type=jnp.float32,
    )
    far_grad = jnp.transpose(jnp.stack([far_re, far_im]), (2, 0, 1, 3)).astype(jnp.bfloat16)
    back_sent = jnp.transpose(
        far_grad.reshape(item_count, 2, 3, band_total, freq_dev), (3, 0, 1, 2, 4)
    )
    band_back = lax.all_to_all(back_sent, "frq", split_axis=0, concat_axis=0, tiled=True)
    far_band = band_back.reshape(block_total, slot_cap * 2 * 3 * freq_dev)
    back_grad = blk_exchange(far_band).astype(jnp.float32)
    back_onehot = (asked_ids.reshape(slot_total)[None, :] == station_iota[:, None]).astype(
        jnp.float32
    )
    station_grad = jnp.dot(
        back_onehot,
        back_grad.reshape(slot_total, 6 * freq_dev),
        precision=lax.Precision.HIGHEST,
        preferred_element_type=jnp.float32,
    )
    grad_matrix = jnp.transpose(
        station_grad.reshape(per_block, 2, 3, freq_dev), (1, 3, 2, 0)
    ).reshape(2 * freq_dev, 3 * per_block)
    basis_part = jnp.concatenate(
        [
            lax.dynamic_slice_in_dim(cos_full, band_index * freq_dev, freq_dev),
            -lax.dynamic_slice_in_dim(sin_full, band_index * freq_dev, freq_dev),
        ],
        axis=0,
    )
    product = product_own + lax.dot_general(
        basis_part,
        grad_matrix,
        (((0,), (0,)), ((), ())),
        precision=lax.Precision.HIGHEST,
        preferred_element_type=jnp.float32,
    )
    lag_parts = lax.all_to_all(
        product.reshape(band_total, NT // band_total, 3, per_block) * output_scale,
        "frq",
        split_axis=0,
        concat_axis=0,
        tiled=True,
    )
    return jnp.sum(lag_parts, axis=0)


def solution(mesh):
    return jax.shard_map(
        local,
        mesh=mesh,
        in_specs=(
            P(None, None, "blk", "frq"),
            P(("blk", "frq"), None, None, None),
            P("blk", None, None),
            P("blk", None, None),
            P("blk", None),
        ),
        out_specs=P("frq", None, "blk"),
        check_vma=False,
    )
```

```python
import math

import jax
import jax.numpy as jnp
from jax import lax
from jax.sharding import PartitionSpec as P

NF = 512
NT = 1024


def phase_table(freq_start, freq_count, time_count):
    freq_index = lax.iota(jnp.int32, freq_count) + freq_start
    time_index = lax.iota(jnp.int32, time_count)
    phase_num = (2 * freq_index + 1)[:, None] * time_index[None, :] % (2 * NT)
    return phase_num.astype(jnp.float32) * (math.pi / NT)


def lag_window():
    time_index = lax.iota(jnp.int32, NT)
    lag_size = jnp.minimum(time_index, NT - time_index)
    return ((lag_size >= NT // 32) & (lag_size < NT // 4)).astype(jnp.float32)


def cross_spectra(first_rows, second_rows):
    real_part = (
        first_rows[:, 0, :, None] * second_rows[:, 0, None, :]
        + first_rows[:, 1, :, None] * second_rows[:, 1, None, :]
    )
    imag_part = (
        first_rows[:, 1, :, None] * second_rows[:, 0, None, :]
        - first_rows[:, 0, :, None] * second_rows[:, 1, None, :]
    )
    return jnp.stack([real_part, imag_part], axis=3)


def pair_gradients(adjoint_rows, first_rows, second_rows):
    adj_real = adjoint_rows[:, :, :, 0]
    adj_imag = adjoint_rows[:, :, :, 1]
    own_real = jnp.sum(
        adj_real * second_rows[:, 0, None] - adj_imag * second_rows[:, 1, None], axis=2
    )
    own_imag = jnp.sum(
        adj_real * second_rows[:, 1, None] + adj_imag * second_rows[:, 0, None], axis=2
    )
    far_real = jnp.sum(
        adj_real * first_rows[:, 0, :, None] + adj_imag * first_rows[:, 1, :, None], axis=1
    )
    far_imag = jnp.sum(
        adj_real * first_rows[:, 1, :, None] - adj_imag * first_rows[:, 0, :, None], axis=1
    )
    return (jnp.stack([own_real, own_imag], axis=1), jnp.stack([far_real, far_imag], axis=1))


def blk_exchange(chunks):
    count, width = chunks.shape
    tile = 16 * 128
    padded = -(-width // tile) * tile
    wide = jnp.pad(chunks, ((0, 0), (0, padded - width))).reshape(count, padded // 128, 128)
    moved = lax.all_to_all(wide, "blk", split_axis=0, concat_axis=0, tiled=True)
    return moved.reshape(count, padded)[:, :width]


def local(spectra, observed, own_station, partner_station, pair_count):
    block_total = lax.axis_size("blk")
    band_total = lax.axis_size("frq")
    per_block = spectra.shape[2]
    freq_dev = spectra.shape[3]
    slot_cap = own_station.shape[2]
    slot_total = block_total * slot_cap
    item_count = slot_total // band_total
    band_index = lax.axis_index("frq")
    spec_rows = jnp.transpose(spectra, (2, 0, 1, 3))
    own_ids = own_station[0].reshape(slot_total)
    partner_local = partner_station[0]
    partner_ids = partner_local.reshape(slot_total)
    alive_mask = (
        (lax.iota(jnp.int32, slot_cap)[None, :] < pair_count[0][:, None])
        .reshape(slot_total)
        .astype(jnp.float32)
    )
    asked_ids = lax.all_to_all(partner_local, "blk", split_axis=0, concat_axis=0, tiled=True)
    asked_rows = jnp.take(spec_rows, asked_ids.reshape(slot_total), axis=0, mode="clip")
    rows_new = blk_exchange(asked_rows.reshape(block_total, -1)).reshape(
        band_total, item_count, 2, 3, freq_dev
    )
    own_table = jnp.broadcast_to(spec_rows[None], (band_total, per_block, 2, 3, freq_dev))
    sent = jnp.concatenate([rows_new, own_table], axis=1)
    whole_band = lax.all_to_all(sent, "frq", split_axis=0, concat_axis=0, tiled=True)
    whole_band = jnp.transpose(whole_band, (2, 3, 1, 0, 4)).reshape(
        2, 3, item_count + per_block, NF
    )
    second_rows = whole_band[:, :, :item_count].astype(jnp.float32)
    own_group = lax.dynamic_slice_in_dim(own_ids, band_index * item_count, item_count)
    first_rows = jnp.take(
        whole_band[:, :, item_count:], own_group, axis=2, mode="clip"
    ).astype(jnp.float32)
    alive_band = lax.dynamic_slice_in_dim(alive_mask, band_index * item_count, item_count)
    first_re = first_rows[0][:, None]
    first_im = first_rows[1][:, None]
    second_re = second_rows[0][None]
    second_im = second_rows[1][None]
    alive_col = alive_band[None, None, :, None]
    cross = (
        jnp.concatenate(
            [
                first_re * second_re + first_im * second_im,
                first_im * second_re - first_re * second_im,
            ],
            axis=3,
        )
        * alive_col
    ).astype(jnp.bfloat16)
    lag_low = NT // 32
    lag_high = NT // 4
    lag_index = jnp.concatenate(
        [
            lax.iota(jnp.int32, lag_high - lag_low) + lag_low,
            lax.iota(jnp.int32, lag_high - lag_low) + (NT - lag_high + 1),
        ]
    )
    phase = (2 * lax.iota(jnp.int32, NF) + 1)[:, None] * lag_index[None, :] % (2 * NT)
    phase = phase.astype(jnp.float32) * (math.pi / NT)
    basis = jnp.concatenate(
        [
            (jnp.cos(phase) / math.sqrt(NF)).astype(jnp.bfloat16),
            -(jnp.sin(phase) / math.sqrt(NF)).astype(jnp.bfloat16),
        ],
        axis=0,
    )
    window = lag_window()[lag_index]
    observed_all = jnp.transpose(observed, (1, 2, 0, 3)).reshape(9 * item_count, NT)
    observed_rows = jnp.concatenate(
        [
            observed_all[:, lag_low:lag_high],
            observed_all[:, NT - lag_high + 1 : NT - lag_low + 1],
        ],
        axis=1,
    ).astype(jnp.float32)
    station_iota = lax.iota(jnp.int32, per_block)
    correlation = jnp.dot(
        cross.reshape(9 * item_count, 2 * NF), basis, preferred_element_type=jnp.float32
    )
    residual = (
        (correlation - observed_rows) * jnp.tile(alive_band, 9)[:, None] * window[None, :]
    ).astype(jnp.bfloat16)
    adjoint_rows = lax.reduce_precision(
        lax.dot_general(
            residual, basis, (((1,), (1,)), ((), ())), preferred_element_type=jnp.float32
        ),
        exponent_bits=8,
        mantissa_bits=7,
    ).reshape(3, 3, item_count, 2 * NF)
    adj_re = adjoint_rows[..., :NF]
    adj_im = adjoint_rows[..., NF:]
    own_re = jnp.sum(adj_re * second_re - adj_im * second_im, axis=1)
    own_im = jnp.sum(adj_re * second_im + adj_im * second_re, axis=1)
    far_re = jnp.sum(adj_re * first_re + adj_im * first_im, axis=0)
    far_im = jnp.sum(adj_re * first_im - adj_im * first_re, axis=0)
    own_onehot = (own_group[None, :] == station_iota[:, None]).astype(jnp.float32)
    grad_group = lax.dot_general(
        own_onehot,
        jnp.stack([own_re, own_im]),
        (((1,), (2,)), ((), ())),
        precision=lax.Precision.HIGHEST,
        preferred_element_type=jnp.float32,
    )
    output_scale = 1.0 / math.sqrt(2.0 * block_total * slot_cap / per_block)
    phase_full = phase_table(0, NF, NT)
    cos_full = jnp.cos(phase_full) / math.sqrt(NF)
    sin_full = jnp.sin(phase_full) / math.sqrt(NF)
    own_matrix = jnp.transpose(grad_group, (1, 3, 2, 0)).reshape(2 * NF, 3 * per_block)
    product_own = lax.dot_general(
        jnp.concatenate([cos_full, -sin_full], axis=0),
        own_matrix,
        (((0,), (0,)), ((), ())),
        precision=lax.Precision.HIGHEST,
        preferred_element_type=jnp.float32,
    )
    product_own = lax.optimization_barrier(product_own)
    far_grad = jnp.transpose(jnp.stack([far_re, far_im]), (2, 0, 1, 3)).astype(jnp.bfloat16)
    back_sent = jnp.transpose(
        far_grad.reshape(item_count, 2, 3, band_total, freq_dev), (3, 0, 1, 2, 4)
    )
    band_back = lax.all_to_all(back_sent, "frq", split_axis=0, concat_axis=0, tiled=True)
    far_band = band_back.reshape(block_total, slot_cap * 2 * 3 * freq_dev)
    back_grad = blk_exchange(far_band).astype(jnp.float32)
    back_onehot = (asked_ids.reshape(slot_total)[None, :] == station_iota[:, None]).astype(
        jnp.float32
    )
    station_grad = jnp.dot(
        back_onehot,
        back_grad.reshape(slot_total, 6 * freq_dev),
        precision=lax.Precision.HIGHEST,
        preferred_element_type=jnp.float32,
    )
    grad_matrix = jnp.transpose(
        station_grad.reshape(per_block, 2, 3, freq_dev), (1, 3, 2, 0)
    ).reshape(2 * freq_dev, 3 * per_block)
    basis_part = jnp.concatenate(
        [
            lax.dynamic_slice_in_dim(cos_full, band_index * freq_dev, freq_dev),
            -lax.dynamic_slice_in_dim(sin_full, band_index * freq_dev, freq_dev),
        ],
        axis=0,
    )
    product = product_own + lax.dot_general(
        basis_part,
        grad_matrix,
        (((0,), (0,)), ((), ())),
        precision=lax.Precision.HIGHEST,
        preferred_element_type=jnp.float32,
    )
    lag_parts = lax.all_to_all(
        product.reshape(band_total, NT // band_total, 3, per_block) * output_scale,
        "frq",
        split_axis=0,
        concat_axis=0,
        tiled=True,
    )
    return jnp.sum(lag_parts, axis=0)


def solution(mesh):
    return jax.shard_map(
        local,
        mesh=mesh,
        in_specs=(
            P(None, None, "blk", "frq"),
            P(("blk", "frq"), None, None, None),
            P("blk", None, None),
            P("blk", None, None),
            P("blk", None),
        ),
        out_specs=P("frq", None, "blk"),
        check_vma=False,
    )
```

```python
import math

import jax
import jax.numpy as jnp
from jax import lax
from jax.sharding import PartitionSpec as P

NF = 512
NT = 1024


def phase_table(freq_start, freq_count, time_count):
    freq_index = lax.iota(jnp.int32, freq_count) + freq_start
    time_index = lax.iota(jnp.int32, time_count)
    phase_num = (2 * freq_index + 1)[:, None] * time_index[None, :] % (2 * NT)
    return phase_num.astype(jnp.float32) * (math.pi / NT)


def lag_window():
    time_index = lax.iota(jnp.int32, NT)
    lag_size = jnp.minimum(time_index, NT - time_index)
    return ((lag_size >= NT // 32) & (lag_size < NT // 4)).astype(jnp.float32)


def cross_spectra(first_rows, second_rows):
    real_part = (
        first_rows[:, 0, :, None] * second_rows[:, 0, None, :]
        + first_rows[:, 1, :, None] * second_rows[:, 1, None, :]
    )
    imag_part = (
        first_rows[:, 1, :, None] * second_rows[:, 0, None, :]
        - first_rows[:, 0, :, None] * second_rows[:, 1, None, :]
    )
    return jnp.stack([real_part, imag_part], axis=3)


def pair_gradients(adjoint_rows, first_rows, second_rows):
    adj_real = adjoint_rows[:, :, :, 0]
    adj_imag = adjoint_rows[:, :, :, 1]
    own_real = jnp.sum(
        adj_real * second_rows[:, 0, None] - adj_imag * second_rows[:, 1, None], axis=2
    )
    own_imag = jnp.sum(
        adj_real * second_rows[:, 1, None] + adj_imag * second_rows[:, 0, None], axis=2
    )
    far_real = jnp.sum(
        adj_real * first_rows[:, 0, :, None] + adj_imag * first_rows[:, 1, :, None], axis=1
    )
    far_imag = jnp.sum(
        adj_real * first_rows[:, 1, :, None] - adj_imag * first_rows[:, 0, :, None], axis=1
    )
    return (jnp.stack([own_real, own_imag], axis=1), jnp.stack([far_real, far_imag], axis=1))


def blk_exchange(chunks):
    count, width = chunks.shape
    tile = 16 * 128
    padded = -(-width // tile) * tile
    wide = jnp.pad(chunks, ((0, 0), (0, padded - width))).reshape(count, padded // 128, 128)
    moved = lax.all_to_all(wide, "blk", split_axis=0, concat_axis=0, tiled=True)
    return moved.reshape(count, padded)[:, :width]


def local(spectra, observed, own_station, partner_station, pair_count):
    block_total = lax.axis_size("blk")
    band_total = lax.axis_size("frq")
    per_block = spectra.shape[2]
    freq_dev = spectra.shape[3]
    slot_cap = own_station.shape[2]
    slot_total = block_total * slot_cap
    item_count = slot_total // band_total
    band_index = lax.axis_index("frq")
    spec_rows = jnp.transpose(spectra, (2, 0, 1, 3))
    own_ids = own_station[0].reshape(slot_total)
    partner_local = partner_station[0]
    partner_ids = partner_local.reshape(slot_total)
    alive_mask = (
        (lax.iota(jnp.int32, slot_cap)[None, :] < pair_count[0][:, None])
        .reshape(slot_total)
        .astype(jnp.float32)
    )
    asked_ids = lax.all_to_all(partner_local, "blk", split_axis=0, concat_axis=0, tiled=True)
    asked_rows = jnp.take(spec_rows, asked_ids.reshape(slot_total), axis=0, mode="clip")
    rows_new = blk_exchange(asked_rows.reshape(block_total, -1)).reshape(
        band_total, item_count, 2, 3, freq_dev
    )
    lag_low = NT // 32
    lag_high = NT // 4
    lag_index = jnp.concatenate(
        [
            lax.iota(jnp.int32, lag_high - lag_low) + lag_low,
            lax.iota(jnp.int32, lag_high - lag_low) + (NT - lag_high + 1),
        ]
    )
    phase = (2 * lax.iota(jnp.int32, NF) + 1)[:, None] * lag_index[None, :] % (2 * NT)
    phase = phase.astype(jnp.float32) * (math.pi / NT)
    basis = jnp.concatenate(
        [
            (jnp.cos(phase) / math.sqrt(NF)).astype(jnp.bfloat16),
            -(jnp.sin(phase) / math.sqrt(NF)).astype(jnp.bfloat16),
        ],
        axis=0,
    )
    lag_size = jnp.minimum(lag_index, NT - lag_index)
    window = ((lag_size >= lag_low) & (lag_size < lag_high)).astype(jnp.float32)
    observed_all = jnp.transpose(observed, (1, 2, 0, 3)).reshape(9 * item_count, NT)
    observed_rows = jnp.concatenate(
        [
            observed_all[:, lag_low:lag_high],
            observed_all[:, NT - lag_high + 1 : NT - lag_low + 1],
        ],
        axis=1,
    ).astype(jnp.float32)
    basis, observed_rows, window, rows_new = lax.optimization_barrier(
        (basis, observed_rows, window, rows_new)
    )
    own_table = jnp.broadcast_to(spec_rows[None], (band_total, per_block, 2, 3, freq_dev))
    sent = jnp.concatenate([rows_new, own_table], axis=1)
    whole_band = lax.all_to_all(sent, "frq", split_axis=0, concat_axis=0, tiled=True)
    whole_band = jnp.transpose(whole_band, (2, 3, 1, 0, 4)).reshape(
        2, 3, item_count + per_block, NF
    )
    second_rows = whole_band[:, :, :item_count].astype(jnp.float32)
    own_group = lax.dynamic_slice_in_dim(own_ids, band_index * item_count, item_count)
    first_rows = jnp.take(
        whole_band[:, :, item_count:], own_group, axis=2, mode="clip"
    ).astype(jnp.float32)
    alive_band = lax.dynamic_slice_in_dim(alive_mask, band_index * item_count, item_count)
    first_re = first_rows[0][:, None]
    first_im = first_rows[1][:, None]
    second_re = second_rows[0][None]
    second_im = second_rows[1][None]
    alive_col = alive_band[None, None, :, None]
    cross = (
        jnp.concatenate(
            [
                first_re * second_re + first_im * second_im,
                first_im * second_re - first_re * second_im,
            ],
            axis=3,
        )
        * alive_col
    ).astype(jnp.bfloat16)
    station_iota = lax.iota(jnp.int32, per_block)
    correlation = jnp.dot(
        cross.reshape(9 * item_count, 2 * NF), basis, preferred_element_type=jnp.float32
    )
    residual = (
        (correlation - observed_rows) * jnp.tile(alive_band, 9)[:, None] * window[None, :]
    ).astype(jnp.bfloat16)
    adjoint_rows = lax.reduce_precision(
        lax.dot_general(
            residual, basis, (((1,), (1,)), ((), ())), preferred_element_type=jnp.float32
        ),
        exponent_bits=8,
        mantissa_bits=7,
    ).reshape(3, 3, item_count, 2 * NF)
    adj_re = adjoint_rows[..., :NF]
    adj_im = adjoint_rows[..., NF:]
    own_re = jnp.sum(adj_re * second_re - adj_im * second_im, axis=1)
    own_im = jnp.sum(adj_re * second_im + adj_im * second_re, axis=1)
    far_re = jnp.sum(adj_re * first_re + adj_im * first_im, axis=0)
    far_im = jnp.sum(adj_re * first_im - adj_im * first_re, axis=0)
    own_onehot = (own_group[None, :] == station_iota[:, None]).astype(jnp.float32)
    grad_group = lax.dot_general(
        own_onehot,
        jnp.stack([own_re, own_im]),
        (((1,), (2,)), ((), ())),
        precision=lax.Precision.HIGHEST,
        preferred_element_type=jnp.float32,
    )
    output_scale = 1.0 / math.sqrt(2.0 * block_total * slot_cap / per_block)
    phase_full = phase_table(0, NF, NT)
    cos_full = jnp.cos(phase_full) / math.sqrt(NF)
    sin_full = jnp.sin(phase_full) / math.sqrt(NF)
    own_matrix = jnp.transpose(grad_group, (1, 3, 2, 0)).reshape(2 * NF, 3 * per_block)
    product_own = lax.dot_general(
        jnp.concatenate([cos_full, -sin_full], axis=0),
        own_matrix,
        (((0,), (0,)), ((), ())),
        precision=lax.Precision.HIGHEST,
        preferred_element_type=jnp.float32,
    )
    product_own = lax.optimization_barrier(product_own)
    far_grad = jnp.transpose(jnp.stack([far_re, far_im]), (2, 0, 1, 3)).astype(jnp.bfloat16)
    back_sent = jnp.transpose(
        far_grad.reshape(item_count, 2, 3, band_total, freq_dev), (3, 0, 1, 2, 4)
    )
    band_back = lax.all_to_all(back_sent, "frq", split_axis=0, concat_axis=0, tiled=True)
    far_band = band_back.reshape(block_total, slot_cap * 2 * 3 * freq_dev)
    back_grad = blk_exchange(far_band).astype(jnp.float32)
    back_onehot = (asked_ids.reshape(slot_total)[None, :] == station_iota[:, None]).astype(
        jnp.float32
    )
    station_grad = jnp.dot(
        back_onehot,
        back_grad.reshape(slot_total, 6 * freq_dev),
        precision=lax.Precision.HIGHEST,
        preferred_element_type=jnp.float32,
    )
    grad_matrix = jnp.transpose(
        station_grad.reshape(per_block, 2, 3, freq_dev), (1, 3, 2, 0)
    ).reshape(2 * freq_dev, 3 * per_block)
    basis_part = jnp.concatenate(
        [
            lax.dynamic_slice_in_dim(cos_full, band_index * freq_dev, freq_dev),
            -lax.dynamic_slice_in_dim(sin_full, band_index * freq_dev, freq_dev),
        ],
        axis=0,
    )
    product = product_own + lax.dot_general(
        basis_part,
        grad_matrix,
        (((0,), (0,)), ((), ())),
        precision=lax.Precision.HIGHEST,
        preferred_element_type=jnp.float32,
    )
    lag_parts = lax.all_to_all(
        product.reshape(band_total, NT // band_total, 3, per_block) * output_scale,
        "frq",
        split_axis=0,
        concat_axis=0,
        tiled=True,
    )
    return jnp.sum(lag_parts, axis=0)


def solution(mesh):
    return jax.shard_map(
        local,
        mesh=mesh,
        in_specs=(
            P(None, None, "blk", "frq"),
            P(("blk", "frq"), None, None, None),
            P("blk", None, None),
            P("blk", None, None),
            P("blk", None),
        ),
        out_specs=P("frq", None, "blk"),
        check_vma=False,
    )
```

```python
import math

import jax
import jax.numpy as jnp
from jax import lax
from jax.sharding import PartitionSpec as P

NF = 512
NT = 1024


def phase_table(freq_start, freq_count, time_count):
    freq_index = lax.iota(jnp.int32, freq_count) + freq_start
    time_index = lax.iota(jnp.int32, time_count)
    phase_num = (2 * freq_index + 1)[:, None] * time_index[None, :] % (2 * NT)
    return phase_num.astype(jnp.float32) * (math.pi / NT)


def lag_window():
    time_index = lax.iota(jnp.int32, NT)
    lag_size = jnp.minimum(time_index, NT - time_index)
    return ((lag_size >= NT // 32) & (lag_size < NT // 4)).astype(jnp.float32)


def cross_spectra(first_rows, second_rows):
    real_part = (
        first_rows[:, 0, :, None] * second_rows[:, 0, None, :]
        + first_rows[:, 1, :, None] * second_rows[:, 1, None, :]
    )
    imag_part = (
        first_rows[:, 1, :, None] * second_rows[:, 0, None, :]
        - first_rows[:, 0, :, None] * second_rows[:, 1, None, :]
    )
    return jnp.stack([real_part, imag_part], axis=3)


def pair_gradients(adjoint_rows, first_rows, second_rows):
    adj_real = adjoint_rows[:, :, :, 0]
    adj_imag = adjoint_rows[:, :, :, 1]
    own_real = jnp.sum(
        adj_real * second_rows[:, 0, None] - adj_imag * second_rows[:, 1, None], axis=2
    )
    own_imag = jnp.sum(
        adj_real * second_rows[:, 1, None] + adj_imag * second_rows[:, 0, None], axis=2
    )
    far_real = jnp.sum(
        adj_real * first_rows[:, 0, :, None] + adj_imag * first_rows[:, 1, :, None], axis=1
    )
    far_imag = jnp.sum(
        adj_real * first_rows[:, 1, :, None] - adj_imag * first_rows[:, 0, :, None], axis=1
    )
    return (jnp.stack([own_real, own_imag], axis=1), jnp.stack([far_real, far_imag], axis=1))


def blk_exchange(chunks):
    count, width = chunks.shape
    tile = 16 * 128
    padded = -(-width // tile) * tile
    wide = jnp.pad(chunks, ((0, 0), (0, padded - width))).reshape(count, padded // 128, 128)
    moved = lax.all_to_all(wide, "blk", split_axis=0, concat_axis=0, tiled=True)
    return moved.reshape(count, padded)[:, :width]


def local(spectra, observed, own_station, partner_station, pair_count):
    block_total = lax.axis_size("blk")
    band_total = lax.axis_size("frq")
    per_block = spectra.shape[2]
    freq_dev = spectra.shape[3]
    slot_cap = own_station.shape[2]
    slot_total = block_total * slot_cap
    item_count = slot_total // band_total
    band_index = lax.axis_index("frq")
    spec_rows = jnp.transpose(spectra, (2, 0, 1, 3))
    own_ids = own_station[0].reshape(slot_total)
    partner_local = partner_station[0]
    partner_ids = partner_local.reshape(slot_total)
    alive_mask = (
        (lax.iota(jnp.int32, slot_cap)[None, :] < pair_count[0][:, None])
        .reshape(slot_total)
        .astype(jnp.float32)
    )
    asked_ids = lax.all_to_all(partner_local, "blk", split_axis=0, concat_axis=0, tiled=True)
    own_table = lax.all_to_all(
        jnp.broadcast_to(spec_rows[None], (band_total, per_block, 2, 3, freq_dev)),
        "frq",
        split_axis=0,
        concat_axis=0,
        tiled=True,
    )
    own_table = jnp.transpose(own_table, (2, 3, 1, 0, 4)).reshape(2, 3, per_block, NF)
    own_group = lax.dynamic_slice_in_dim(own_ids, band_index * item_count, item_count)
    first_rows = jnp.take(own_table, own_group, axis=2, mode="clip").astype(jnp.float32)
    first_rows, asked_ids = lax.optimization_barrier((first_rows, asked_ids))
    asked_rows = jnp.take(spec_rows, asked_ids.reshape(slot_total), axis=0, mode="clip")
    rows_new = blk_exchange(asked_rows.reshape(block_total, -1)).reshape(
        band_total, item_count, 2, 3, freq_dev
    )
    lag_low = NT // 32
    lag_high = NT // 4
    lag_index = jnp.concatenate(
        [
            lax.iota(jnp.int32, lag_high - lag_low) + lag_low,
            lax.iota(jnp.int32, lag_high - lag_low) + (NT - lag_high + 1),
        ]
    )
    phase = (2 * lax.iota(jnp.int32, NF) + 1)[:, None] * lag_index[None, :] % (2 * NT)
    phase = phase.astype(jnp.float32) * (math.pi / NT)
    basis = jnp.concatenate(
        [
            (jnp.cos(phase) / math.sqrt(NF)).astype(jnp.bfloat16),
            -(jnp.sin(phase) / math.sqrt(NF)).astype(jnp.bfloat16),
        ],
        axis=0,
    )
    lag_size = jnp.minimum(lag_index, NT - lag_index)
    window = ((lag_size >= lag_low) & (lag_size < lag_high)).astype(jnp.float32)
    observed_all = jnp.transpose(observed, (1, 2, 0, 3)).reshape(9 * item_count, NT)
    observed_rows = jnp.concatenate(
        [
            observed_all[:, lag_low:lag_high],
            observed_all[:, NT - lag_high + 1 : NT - lag_low + 1],
        ],
        axis=1,
    ).astype(jnp.float32)
    basis, observed_rows, window, rows_new = lax.optimization_barrier(
        (basis, observed_rows, window, rows_new)
    )
    whole_band = lax.all_to_all(rows_new, "frq", split_axis=0, concat_axis=0, tiled=True)
    second_rows = (
        jnp.transpose(whole_band, (2, 3, 1, 0, 4)).reshape(2, 3, item_count, NF).astype(jnp.float32)
    )
    alive_band = lax.dynamic_slice_in_dim(alive_mask, band_index * item_count, item_count)
    first_re = first_rows[0][:, None]
    first_im = first_rows[1][:, None]
    second_re = second_rows[0][None]
    second_im = second_rows[1][None]
    alive_col = alive_band[None, None, :, None]
    cross = (
        jnp.concatenate(
            [
                first_re * second_re + first_im * second_im,
                first_im * second_re - first_re * second_im,
            ],
            axis=3,
        )
        * alive_col
    ).astype(jnp.bfloat16)
    station_iota = lax.iota(jnp.int32, per_block)
    correlation = jnp.dot(
        cross.reshape(9 * item_count, 2 * NF), basis, preferred_element_type=jnp.float32
    )
    residual = (
        (correlation - observed_rows) * jnp.tile(alive_band, 9)[:, None] * window[None, :]
    ).astype(jnp.bfloat16)
    adjoint_rows = lax.reduce_precision(
        lax.dot_general(
            residual, basis, (((1,), (1,)), ((), ())), preferred_element_type=jnp.float32
        ),
        exponent_bits=8,
        mantissa_bits=7,
    ).reshape(3, 3, item_count, 2 * NF)
    adj_re = adjoint_rows[..., :NF]
    adj_im = adjoint_rows[..., NF:]
    own_re = jnp.sum(adj_re * second_re - adj_im * second_im, axis=1)
    own_im = jnp.sum(adj_re * second_im + adj_im * second_re, axis=1)
    far_re = jnp.sum(adj_re * first_re + adj_im * first_im, axis=0)
    far_im = jnp.sum(adj_re * first_im - adj_im * first_re, axis=0)
    own_onehot = (own_group[None, :] == station_iota[:, None]).astype(jnp.float32)
    grad_group = lax.dot_general(
        own_onehot,
        jnp.stack([own_re, own_im]),
        (((1,), (2,)), ((), ())),
        precision=lax.Precision.HIGHEST,
        preferred_element_type=jnp.float32,
    )
    output_scale = 1.0 / math.sqrt(2.0 * block_total * slot_cap / per_block)
    phase_full = phase_table(0, NF, NT)
    cos_full = jnp.cos(phase_full) / math.sqrt(NF)
    sin_full = jnp.sin(phase_full) / math.sqrt(NF)
    own_matrix = jnp.transpose(grad_group, (1, 3, 2, 0)).reshape(2 * NF, 3 * per_block)
    product_own = lax.dot_general(
        jnp.concatenate([cos_full, -sin_full], axis=0),
        own_matrix,
        (((0,), (0,)), ((), ())),
        precision=lax.Precision.HIGHEST,
        preferred_element_type=jnp.float32,
    )
    product_own = lax.optimization_barrier(product_own)
    far_grad = jnp.transpose(jnp.stack([far_re, far_im]), (2, 0, 1, 3)).astype(jnp.bfloat16)
    back_sent = jnp.transpose(
        far_grad.reshape(item_count, 2, 3, band_total, freq_dev), (3, 0, 1, 2, 4)
    )
    band_back = lax.all_to_all(back_sent, "frq", split_axis=0, concat_axis=0, tiled=True)
    far_band = band_back.reshape(block_total, slot_cap * 2 * 3 * freq_dev)
    back_grad = blk_exchange(far_band).astype(jnp.float32)
    back_onehot = (asked_ids.reshape(slot_total)[None, :] == station_iota[:, None]).astype(
        jnp.float32
    )
    station_grad = jnp.dot(
        back_onehot,
        back_grad.reshape(slot_total, 6 * freq_dev),
        precision=lax.Precision.HIGHEST,
        preferred_element_type=jnp.float32,
    )
    grad_matrix = jnp.transpose(
        station_grad.reshape(per_block, 2, 3, freq_dev), (1, 3, 2, 0)
    ).reshape(2 * freq_dev, 3 * per_block)
    basis_part = jnp.concatenate(
        [
            lax.dynamic_slice_in_dim(cos_full, band_index * freq_dev, freq_dev),
            -lax.dynamic_slice_in_dim(sin_full, band_index * freq_dev, freq_dev),
        ],
        axis=0,
    )
    product = product_own + lax.dot_general(
        basis_part,
        grad_matrix,
        (((0,), (0,)), ((), ())),
        precision=lax.Precision.HIGHEST,
        preferred_element_type=jnp.float32,
    )
    lag_parts = lax.all_to_all(
        product.reshape(band_total, NT // band_total, 3, per_block) * output_scale,
        "frq",
        split_axis=0,
        concat_axis=0,
        tiled=True,
    )
    return jnp.sum(lag_parts, axis=0)


def solution(mesh):
    return jax.shard_map(
        local,
        mesh=mesh,
        in_specs=(
            P(None, None, "blk", "frq"),
            P(("blk", "frq"), None, None, None),
            P("blk", None, None),
            P("blk", None, None),
            P("blk", None),
        ),
        out_specs=P("frq", None, "blk"),
        check_vma=False,
    )
```

```python
import math

import jax
import jax.numpy as jnp
from jax import lax
from jax.sharding import PartitionSpec as P

NF = 512
NT = 1024


def phase_table(freq_start, freq_count, time_count):
    freq_index = lax.iota(jnp.int32, freq_count) + freq_start
    time_index = lax.iota(jnp.int32, time_count)
    phase_num = (2 * freq_index + 1)[:, None] * time_index[None, :] % (2 * NT)
    return phase_num.astype(jnp.float32) * (math.pi / NT)


def lag_window():
    time_index = lax.iota(jnp.int32, NT)
    lag_size = jnp.minimum(time_index, NT - time_index)
    return ((lag_size >= NT // 32) & (lag_size < NT // 4)).astype(jnp.float32)


def cross_spectra(first_rows, second_rows):
    real_part = (
        first_rows[:, 0, :, None] * second_rows[:, 0, None, :]
        + first_rows[:, 1, :, None] * second_rows[:, 1, None, :]
    )
    imag_part = (
        first_rows[:, 1, :, None] * second_rows[:, 0, None, :]
        - first_rows[:, 0, :, None] * second_rows[:, 1, None, :]
    )
    return jnp.stack([real_part, imag_part], axis=3)


def pair_gradients(adjoint_rows, first_rows, second_rows):
    adj_real = adjoint_rows[:, :, :, 0]
    adj_imag = adjoint_rows[:, :, :, 1]
    own_real = jnp.sum(
        adj_real * second_rows[:, 0, None] - adj_imag * second_rows[:, 1, None], axis=2
    )
    own_imag = jnp.sum(
        adj_real * second_rows[:, 1, None] + adj_imag * second_rows[:, 0, None], axis=2
    )
    far_real = jnp.sum(
        adj_real * first_rows[:, 0, :, None] + adj_imag * first_rows[:, 1, :, None], axis=1
    )
    far_imag = jnp.sum(
        adj_real * first_rows[:, 1, :, None] - adj_imag * first_rows[:, 0, :, None], axis=1
    )
    return (jnp.stack([own_real, own_imag], axis=1), jnp.stack([far_real, far_imag], axis=1))


def blk_exchange(chunks):
    count, width = chunks.shape
    moved = lax.all_to_all(
        chunks.reshape(count, width // 128, 128), "blk", split_axis=0, concat_axis=0, tiled=True
    )
    return moved.reshape(count, width)


def local(spectra, observed, own_station, partner_station, pair_count):
    block_total = lax.axis_size("blk")
    band_total = lax.axis_size("frq")
    per_block = spectra.shape[2]
    freq_dev = spectra.shape[3]
    slot_cap = own_station.shape[2]
    slot_total = block_total * slot_cap
    item_count = slot_total // band_total
    band_index = lax.axis_index("frq")
    spec_rows = jnp.transpose(spectra, (2, 0, 1, 3))
    own_ids = own_station[0].reshape(slot_total)
    partner_local = partner_station[0]
    partner_ids = partner_local.reshape(slot_total)
    alive_mask = (
        (lax.iota(jnp.int32, slot_cap)[None, :] < pair_count[0][:, None])
        .reshape(slot_total)
        .astype(jnp.float32)
    )
    asked_ids = lax.all_to_all(partner_local, "blk", split_axis=0, concat_axis=0, tiled=True)
    asked_rows = jnp.take(spec_rows, asked_ids.reshape(slot_total), axis=0, mode="clip")
    rows_new = blk_exchange(asked_rows.reshape(block_total, -1)).reshape(
        band_total, item_count, 2, 3, freq_dev
    )
    lag_low = NT // 32
    lag_high = NT // 4
    lag_index = jnp.concatenate(
        [
            lax.iota(jnp.int32, lag_high - lag_low) + lag_low,
            lax.iota(jnp.int32, lag_high - lag_low) + (NT - lag_high + 1),
        ]
    )
    phase = (2 * lax.iota(jnp.int32, NF) + 1)[:, None] * lag_index[None, :] % (2 * NT)
    phase = phase.astype(jnp.float32) * (math.pi / NT)
    basis = jnp.concatenate(
        [
            (jnp.cos(phase) / math.sqrt(NF)).astype(jnp.bfloat16),
            -(jnp.sin(phase) / math.sqrt(NF)).astype(jnp.bfloat16),
        ],
        axis=0,
    )
    lag_size = jnp.minimum(lag_index, NT - lag_index)
    window = ((lag_size >= lag_low) & (lag_size < lag_high)).astype(jnp.float32)
    observed_all = jnp.transpose(observed, (1, 2, 0, 3)).reshape(9 * item_count, NT)
    observed_rows = jnp.concatenate(
        [
            observed_all[:, lag_low:lag_high],
            observed_all[:, NT - lag_high + 1 : NT - lag_low + 1],
        ],
        axis=1,
    ).astype(jnp.float32)
    basis, observed_rows, window, rows_new = lax.optimization_barrier(
        (basis, observed_rows, window, rows_new)
    )
    own_table = jnp.broadcast_to(spec_rows[None], (band_total, per_block, 2, 3, freq_dev))
    sent = jnp.concatenate([rows_new, own_table], axis=1)
    whole_band = lax.all_to_all(sent, "frq", split_axis=0, concat_axis=0, tiled=True)
    whole_band = jnp.transpose(whole_band, (2, 3, 1, 0, 4)).reshape(
        2, 3, item_count + per_block, NF
    )
    second_rows = whole_band[:, :, :item_count].astype(jnp.float32)
    own_group = lax.dynamic_slice_in_dim(own_ids, band_index * item_count, item_count)
    first_rows = jnp.take(
        whole_band[:, :, item_count:], own_group, axis=2, mode="clip"
    ).astype(jnp.float32)
    alive_band = lax.dynamic_slice_in_dim(alive_mask, band_index * item_count, item_count)
    first_re = first_rows[0][:, None]
    first_im = first_rows[1][:, None]
    second_re = second_rows[0][None]
    second_im = second_rows[1][None]
    alive_col = alive_band[None, None, :, None]
    cross = (
        jnp.concatenate(
            [
                first_re * second_re + first_im * second_im,
                first_im * second_re - first_re * second_im,
            ],
            axis=3,
        )
        * alive_col
    ).astype(jnp.bfloat16)
    station_iota = lax.iota(jnp.int32, per_block)
    correlation = jnp.dot(
        cross.reshape(9 * item_count, 2 * NF), basis, preferred_element_type=jnp.float32
    )
    residual = (
        (correlation - observed_rows) * jnp.tile(alive_band, 9)[:, None] * window[None, :]
    ).astype(jnp.bfloat16)
    adjoint_rows = lax.reduce_precision(
        lax.dot_general(
            residual, basis, (((1,), (1,)), ((), ())), preferred_element_type=jnp.float32
        ),
        exponent_bits=8,
        mantissa_bits=7,
    ).reshape(3, 3, item_count, 2 * NF)
    adj_re = adjoint_rows[..., :NF]
    adj_im = adjoint_rows[..., NF:]
    own_re = jnp.sum(adj_re * second_re - adj_im * second_im, axis=1)
    own_im = jnp.sum(adj_re * second_im + adj_im * second_re, axis=1)
    far_re = jnp.sum(adj_re * first_re + adj_im * first_im, axis=0)
    far_im = jnp.sum(adj_re * first_im - adj_im * first_re, axis=0)
    own_onehot = (own_group[None, :] == station_iota[:, None]).astype(jnp.float32)
    grad_group = lax.dot_general(
        own_onehot,
        jnp.stack([own_re, own_im]),
        (((1,), (2,)), ((), ())),
        precision=lax.Precision.HIGHEST,
        preferred_element_type=jnp.float32,
    )
    output_scale = 1.0 / math.sqrt(2.0 * block_total * slot_cap / per_block)
    phase_full = phase_table(0, NF, NT)
    cos_full = jnp.cos(phase_full) / math.sqrt(NF)
    sin_full = jnp.sin(phase_full) / math.sqrt(NF)
    own_matrix = jnp.transpose(grad_group, (1, 3, 2, 0)).reshape(2 * NF, 3 * per_block)
    product_own = lax.dot_general(
        jnp.concatenate([cos_full, -sin_full], axis=0),
        own_matrix,
        (((0,), (0,)), ((), ())),
        precision=lax.Precision.HIGHEST,
        preferred_element_type=jnp.float32,
    )
    product_own = lax.optimization_barrier(product_own)
    far_grad = jnp.transpose(jnp.stack([far_re, far_im]), (2, 0, 1, 3)).astype(jnp.bfloat16)
    back_sent = jnp.transpose(
        far_grad.reshape(item_count, 2, 3, band_total, freq_dev), (3, 0, 1, 2, 4)
    )
    band_back = lax.all_to_all(back_sent, "frq", split_axis=0, concat_axis=0, tiled=True)
    far_band = band_back.reshape(block_total, slot_cap * 2 * 3 * freq_dev)
    back_grad = blk_exchange(far_band).astype(jnp.float32)
    back_onehot = (asked_ids.reshape(slot_total)[None, :] == station_iota[:, None]).astype(
        jnp.float32
    )
    station_grad = jnp.dot(
        back_onehot,
        back_grad.reshape(slot_total, 6 * freq_dev),
        precision=lax.Precision.HIGHEST,
        preferred_element_type=jnp.float32,
    )
    grad_matrix = jnp.transpose(
        station_grad.reshape(per_block, 2, 3, freq_dev), (1, 3, 2, 0)
    ).reshape(2 * freq_dev, 3 * per_block)
    basis_part = jnp.concatenate(
        [
            lax.dynamic_slice_in_dim(cos_full, band_index * freq_dev, freq_dev),
            -lax.dynamic_slice_in_dim(sin_full, band_index * freq_dev, freq_dev),
        ],
        axis=0,
    )
    product = product_own + lax.dot_general(
        basis_part,
        grad_matrix,
        (((0,), (0,)), ((), ())),
        precision=lax.Precision.HIGHEST,
        preferred_element_type=jnp.float32,
    )
    lag_parts = lax.all_to_all(
        product.reshape(band_total, NT // band_total, 3, per_block) * output_scale,
        "frq",
        split_axis=0,
        concat_axis=0,
        tiled=True,
    )
    return jnp.sum(lag_parts, axis=0)


def solution(mesh):
    return jax.shard_map(
        local,
        mesh=mesh,
        in_specs=(
            P(None, None, "blk", "frq"),
            P(("blk", "frq"), None, None, None),
            P("blk", None, None),
            P("blk", None, None),
            P("blk", None),
        ),
        out_specs=P("frq", None, "blk"),
        check_vma=False,
    )
```

```python
import math

import jax
import jax.numpy as jnp
from jax import lax
from jax.sharding import PartitionSpec as P

NF = 512
NT = 1024


def phase_table(freq_start, freq_count, time_count):
    freq_index = lax.iota(jnp.int32, freq_count) + freq_start
    time_index = lax.iota(jnp.int32, time_count)
    phase_num = (2 * freq_index + 1)[:, None] * time_index[None, :] % (2 * NT)
    return phase_num.astype(jnp.float32) * (math.pi / NT)


def lag_window():
    time_index = lax.iota(jnp.int32, NT)
    lag_size = jnp.minimum(time_index, NT - time_index)
    return ((lag_size >= NT // 32) & (lag_size < NT // 4)).astype(jnp.float32)


def cross_spectra(first_rows, second_rows):
    real_part = (
        first_rows[:, 0, :, None] * second_rows[:, 0, None, :]
        + first_rows[:, 1, :, None] * second_rows[:, 1, None, :]
    )
    imag_part = (
        first_rows[:, 1, :, None] * second_rows[:, 0, None, :]
        - first_rows[:, 0, :, None] * second_rows[:, 1, None, :]
    )
    return jnp.stack([real_part, imag_part], axis=3)


def pair_gradients(adjoint_rows, first_rows, second_rows):
    adj_real = adjoint_rows[:, :, :, 0]
    adj_imag = adjoint_rows[:, :, :, 1]
    own_real = jnp.sum(
        adj_real * second_rows[:, 0, None] - adj_imag * second_rows[:, 1, None], axis=2
    )
    own_imag = jnp.sum(
        adj_real * second_rows[:, 1, None] + adj_imag * second_rows[:, 0, None], axis=2
    )
    far_real = jnp.sum(
        adj_real * first_rows[:, 0, :, None] + adj_imag * first_rows[:, 1, :, None], axis=1
    )
    far_imag = jnp.sum(
        adj_real * first_rows[:, 1, :, None] - adj_imag * first_rows[:, 0, :, None], axis=1
    )
    return (jnp.stack([own_real, own_imag], axis=1), jnp.stack([far_real, far_imag], axis=1))


def blk_exchange(chunks):
    count, width = chunks.shape
    moved = lax.all_to_all(
        chunks.reshape(count, width // 128, 128), "blk", split_axis=0, concat_axis=0, tiled=True
    )
    return moved.reshape(count, width)


def local(spectra, observed, own_station, partner_station, pair_count):
    block_total = lax.axis_size("blk")
    band_total = lax.axis_size("frq")
    per_block = spectra.shape[2]
    freq_dev = spectra.shape[3]
    slot_cap = own_station.shape[2]
    slot_total = block_total * slot_cap
    item_count = slot_total // band_total
    band_index = lax.axis_index("frq")
    spec_rows = jnp.transpose(spectra, (2, 0, 1, 3))
    own_ids = own_station[0].reshape(slot_total)
    partner_local = partner_station[0]
    partner_ids = partner_local.reshape(slot_total)
    alive_mask = (
        (lax.iota(jnp.int32, slot_cap)[None, :] < pair_count[0][:, None])
        .reshape(slot_total)
        .astype(jnp.float32)
    )
    asked_ids = lax.all_to_all(partner_local, "blk", split_axis=0, concat_axis=0, tiled=True)
    asked_onehot = (
        asked_ids.reshape(slot_total)[:, None] == lax.iota(jnp.int32, per_block)[None, :]
    ).astype(spectra.dtype)
    asked_rows = jnp.dot(
        asked_onehot, spec_rows.reshape(per_block, -1), preferred_element_type=jnp.float32
    ).astype(spectra.dtype)
    rows_new = blk_exchange(asked_rows.reshape(block_total, -1)).reshape(
        band_total, item_count, 2, 3, freq_dev
    )
    lag_low = NT // 32
    lag_high = NT // 4
    lag_index = jnp.concatenate(
        [
            lax.iota(jnp.int32, lag_high - lag_low) + lag_low,
            lax.iota(jnp.int32, lag_high - lag_low) + (NT - lag_high + 1),
        ]
    )
    phase = (2 * lax.iota(jnp.int32, NF) + 1)[:, None] * lag_index[None, :] % (2 * NT)
    phase = phase.astype(jnp.float32) * (math.pi / NT)
    basis = jnp.concatenate(
        [
            (jnp.cos(phase) / math.sqrt(NF)).astype(jnp.bfloat16),
            -(jnp.sin(phase) / math.sqrt(NF)).astype(jnp.bfloat16),
        ],
        axis=0,
    )
    lag_size = jnp.minimum(lag_index, NT - lag_index)
    window = ((lag_size >= lag_low) & (lag_size < lag_high)).astype(jnp.float32)
    observed_all = jnp.transpose(observed, (1, 2, 0, 3)).reshape(9 * item_count, NT)
    observed_rows = jnp.concatenate(
        [
            observed_all[:, lag_low:lag_high],
            observed_all[:, NT - lag_high + 1 : NT - lag_low + 1],
        ],
        axis=1,
    ).astype(jnp.float32)
    basis, observed_rows, window, rows_new = lax.optimization_barrier(
        (basis, observed_rows, window, rows_new)
    )
    own_table = jnp.broadcast_to(spec_rows[None], (band_total, per_block, 2, 3, freq_dev))
    sent = jnp.concatenate([rows_new, own_table], axis=1)
    whole_band = lax.all_to_all(sent, "frq", split_axis=0, concat_axis=0, tiled=True)
    whole_band = jnp.transpose(whole_band, (2, 3, 1, 0, 4)).reshape(
        2, 3, item_count + per_block, NF
    )
    second_rows = whole_band[:, :, :item_count].astype(jnp.float32)
    own_group = lax.dynamic_slice_in_dim(own_ids, band_index * item_count, item_count)
    group_onehot = (own_group[:, None] == lax.iota(jnp.int32, per_block)[None, :]).astype(
        whole_band.dtype
    )
    first_rows = jnp.einsum(
        "pn,rcnk->rcpk",
        group_onehot,
        whole_band[:, :, item_count:],
        preferred_element_type=jnp.float32,
    )
    alive_band = lax.dynamic_slice_in_dim(alive_mask, band_index * item_count, item_count)
    first_re = first_rows[0][:, None]
    first_im = first_rows[1][:, None]
    second_re = second_rows[0][None]
    second_im = second_rows[1][None]
    alive_col = alive_band[None, None, :, None]
    cross = (
        jnp.concatenate(
            [
                first_re * second_re + first_im * second_im,
                first_im * second_re - first_re * second_im,
            ],
            axis=3,
        )
        * alive_col
    ).astype(jnp.bfloat16)
    station_iota = lax.iota(jnp.int32, per_block)
    correlation = jnp.dot(
        cross.reshape(9 * item_count, 2 * NF), basis, preferred_element_type=jnp.float32
    )
    residual = (
        (correlation - observed_rows) * jnp.tile(alive_band, 9)[:, None] * window[None, :]
    ).astype(jnp.bfloat16)
    adjoint_rows = lax.reduce_precision(
        lax.dot_general(
            residual, basis, (((1,), (1,)), ((), ())), preferred_element_type=jnp.float32
        ),
        exponent_bits=8,
        mantissa_bits=7,
    ).reshape(3, 3, item_count, 2 * NF)
    adj_re = adjoint_rows[..., :NF]
    adj_im = adjoint_rows[..., NF:]
    own_re = jnp.sum(adj_re * second_re - adj_im * second_im, axis=1)
    own_im = jnp.sum(adj_re * second_im + adj_im * second_re, axis=1)
    far_re = jnp.sum(adj_re * first_re + adj_im * first_im, axis=0)
    far_im = jnp.sum(adj_re * first_im - adj_im * first_re, axis=0)
    own_onehot = (own_group[None, :] == station_iota[:, None]).astype(jnp.float32)
    grad_group = lax.dot_general(
        own_onehot,
        jnp.stack([own_re, own_im]),
        (((1,), (2,)), ((), ())),
        precision=lax.Precision.HIGHEST,
        preferred_element_type=jnp.float32,
    )
    output_scale = 1.0 / math.sqrt(2.0 * block_total * slot_cap / per_block)
    phase_full = phase_table(0, NF, NT)
    cos_full = jnp.cos(phase_full) / math.sqrt(NF)
    sin_full = jnp.sin(phase_full) / math.sqrt(NF)
    own_matrix = jnp.transpose(grad_group, (1, 3, 2, 0)).reshape(2 * NF, 3 * per_block)
    product_own = lax.dot_general(
        jnp.concatenate([cos_full, -sin_full], axis=0),
        own_matrix,
        (((0,), (0,)), ((), ())),
        precision=lax.Precision.HIGHEST,
        preferred_element_type=jnp.float32,
    )
    product_own = lax.optimization_barrier(product_own)
    far_grad = jnp.transpose(jnp.stack([far_re, far_im]), (2, 0, 1, 3)).astype(jnp.bfloat16)
    back_sent = jnp.transpose(
        far_grad.reshape(item_count, 2, 3, band_total, freq_dev), (3, 0, 1, 2, 4)
    )
    band_back = lax.all_to_all(back_sent, "frq", split_axis=0, concat_axis=0, tiled=True)
    far_band = band_back.reshape(block_total, slot_cap * 2 * 3 * freq_dev)
    back_grad = blk_exchange(far_band).astype(jnp.float32)
    back_onehot = (asked_ids.reshape(slot_total)[None, :] == station_iota[:, None]).astype(
        jnp.float32
    )
    station_grad = jnp.dot(
        back_onehot,
        back_grad.reshape(slot_total, 6 * freq_dev),
        precision=lax.Precision.HIGHEST,
        preferred_element_type=jnp.float32,
    )
    grad_matrix = jnp.transpose(
        station_grad.reshape(per_block, 2, 3, freq_dev), (1, 3, 2, 0)
    ).reshape(2 * freq_dev, 3 * per_block)
    basis_part = jnp.concatenate(
        [
            lax.dynamic_slice_in_dim(cos_full, band_index * freq_dev, freq_dev),
            -lax.dynamic_slice_in_dim(sin_full, band_index * freq_dev, freq_dev),
        ],
        axis=0,
    )
    product = product_own + lax.dot_general(
        basis_part,
        grad_matrix,
        (((0,), (0,)), ((), ())),
        precision=lax.Precision.HIGHEST,
        preferred_element_type=jnp.float32,
    )
    lag_parts = lax.all_to_all(
        product.reshape(band_total, NT // band_total, 3, per_block) * output_scale,
        "frq",
        split_axis=0,
        concat_axis=0,
        tiled=True,
    )
    return jnp.sum(lag_parts, axis=0)


def solution(mesh):
    return jax.shard_map(
        local,
        mesh=mesh,
        in_specs=(
            P(None, None, "blk", "frq"),
            P(("blk", "frq"), None, None, None),
            P("blk", None, None),
            P("blk", None, None),
            P("blk", None),
        ),
        out_specs=P("frq", None, "blk"),
        check_vma=False,
    )
```

```python
import math

import jax
import jax.numpy as jnp
from jax import lax
from jax.sharding import PartitionSpec as P

NF = 512
NT = 1024


def phase_table(freq_start, freq_count, time_count):
    freq_index = lax.iota(jnp.int32, freq_count) + freq_start
    time_index = lax.iota(jnp.int32, time_count)
    phase_num = (2 * freq_index + 1)[:, None] * time_index[None, :] % (2 * NT)
    return phase_num.astype(jnp.float32) * (math.pi / NT)


def lag_window():
    time_index = lax.iota(jnp.int32, NT)
    lag_size = jnp.minimum(time_index, NT - time_index)
    return ((lag_size >= NT // 32) & (lag_size < NT // 4)).astype(jnp.float32)


def cross_spectra(first_rows, second_rows):
    real_part = (
        first_rows[:, 0, :, None] * second_rows[:, 0, None, :]
        + first_rows[:, 1, :, None] * second_rows[:, 1, None, :]
    )
    imag_part = (
        first_rows[:, 1, :, None] * second_rows[:, 0, None, :]
        - first_rows[:, 0, :, None] * second_rows[:, 1, None, :]
    )
    return jnp.stack([real_part, imag_part], axis=3)


def pair_gradients(adjoint_rows, first_rows, second_rows):
    adj_real = adjoint_rows[:, :, :, 0]
    adj_imag = adjoint_rows[:, :, :, 1]
    own_real = jnp.sum(
        adj_real * second_rows[:, 0, None] - adj_imag * second_rows[:, 1, None], axis=2
    )
    own_imag = jnp.sum(
        adj_real * second_rows[:, 1, None] + adj_imag * second_rows[:, 0, None], axis=2
    )
    far_real = jnp.sum(
        adj_real * first_rows[:, 0, :, None] + adj_imag * first_rows[:, 1, :, None], axis=1
    )
    far_imag = jnp.sum(
        adj_real * first_rows[:, 1, :, None] - adj_imag * first_rows[:, 0, :, None], axis=1
    )
    return (jnp.stack([own_real, own_imag], axis=1), jnp.stack([far_real, far_imag], axis=1))


def blk_exchange(chunks):
    count, width = chunks.shape
    moved = lax.all_to_all(
        chunks.reshape(count, 4, width // 4), "blk", split_axis=0, concat_axis=0, tiled=True
    )
    return moved.reshape(count, width)


def local(spectra, observed, own_station, partner_station, pair_count):
    block_total = lax.axis_size("blk")
    band_total = lax.axis_size("frq")
    per_block = spectra.shape[2]
    freq_dev = spectra.shape[3]
    slot_cap = own_station.shape[2]
    slot_total = block_total * slot_cap
    item_count = slot_total // band_total
    band_index = lax.axis_index("frq")
    spec_rows = jnp.transpose(spectra, (2, 0, 1, 3))
    own_ids = own_station[0].reshape(slot_total)
    partner_local = partner_station[0]
    partner_ids = partner_local.reshape(slot_total)
    alive_mask = (
        (lax.iota(jnp.int32, slot_cap)[None, :] < pair_count[0][:, None])
        .reshape(slot_total)
        .astype(jnp.float32)
    )
    asked_ids = lax.all_to_all(partner_local, "blk", split_axis=0, concat_axis=0, tiled=True)
    asked_onehot = (
        asked_ids.reshape(slot_total)[:, None] == lax.iota(jnp.int32, per_block)[None, :]
    ).astype(spectra.dtype)
    asked_rows = jnp.dot(
        asked_onehot, spec_rows.reshape(per_block, -1), preferred_element_type=jnp.float32
    ).astype(spectra.dtype)
    rows_new = blk_exchange(asked_rows.reshape(block_total, -1)).reshape(
        band_total, item_count, 2, 3, freq_dev
    )
    lag_low = NT // 32
    lag_high = NT // 4
    lag_index = jnp.concatenate(
        [
            lax.iota(jnp.int32, lag_high - lag_low) + lag_low,
            lax.iota(jnp.int32, lag_high - lag_low) + (NT - lag_high + 1),
        ]
    )
    phase = (2 * lax.iota(jnp.int32, NF) + 1)[:, None] * lag_index[None, :] % (2 * NT)
    phase = phase.astype(jnp.float32) * (math.pi / NT)
    basis = jnp.concatenate(
        [
            (jnp.cos(phase) / math.sqrt(NF)).astype(jnp.bfloat16),
            -(jnp.sin(phase) / math.sqrt(NF)).astype(jnp.bfloat16),
        ],
        axis=0,
    )
    lag_size = jnp.minimum(lag_index, NT - lag_index)
    window = ((lag_size >= lag_low) & (lag_size < lag_high)).astype(jnp.float32)
    observed_all = jnp.transpose(observed, (1, 2, 0, 3)).reshape(9 * item_count, NT)
    observed_rows = jnp.concatenate(
        [
            observed_all[:, lag_low:lag_high],
            observed_all[:, NT - lag_high + 1 : NT - lag_low + 1],
        ],
        axis=1,
    ).astype(jnp.float32)
    basis, observed_rows, window, rows_new = lax.optimization_barrier(
        (basis, observed_rows, window, rows_new)
    )
    own_table = jnp.broadcast_to(spec_rows[None], (band_total, per_block, 2, 3, freq_dev))
    sent = jnp.concatenate([rows_new, own_table], axis=1)
    whole_band = lax.all_to_all(sent, "frq", split_axis=0, concat_axis=0, tiled=True)
    whole_band = jnp.transpose(whole_band, (2, 3, 1, 0, 4)).reshape(
        2, 3, item_count + per_block, NF
    )
    second_rows = whole_band[:, :, :item_count].astype(jnp.float32)
    own_group = lax.dynamic_slice_in_dim(own_ids, band_index * item_count, item_count)
    group_onehot = (own_group[:, None] == lax.iota(jnp.int32, per_block)[None, :]).astype(
        whole_band.dtype
    )
    first_rows = jnp.einsum(
        "pn,rcnk->rcpk",
        group_onehot,
        whole_band[:, :, item_count:],
        preferred_element_type=jnp.float32,
    )
    alive_band = lax.dynamic_slice_in_dim(alive_mask, band_index * item_count, item_count)
    first_re = first_rows[0][:, None]
    first_im = first_rows[1][:, None]
    second_re = second_rows[0][None]
    second_im = second_rows[1][None]
    alive_col = alive_band[None, None, :, None]
    cross = (
        jnp.concatenate(
            [
                first_re * second_re + first_im * second_im,
                first_im * second_re - first_re * second_im,
            ],
            axis=3,
        )
        * alive_col
    ).astype(jnp.bfloat16)
    station_iota = lax.iota(jnp.int32, per_block)
    correlation = jnp.dot(
        cross.reshape(9 * item_count, 2 * NF), basis, preferred_element_type=jnp.float32
    )
    residual = (
        (correlation - observed_rows) * jnp.tile(alive_band, 9)[:, None] * window[None, :]
    ).astype(jnp.bfloat16)
    adjoint_rows = lax.reduce_precision(
        lax.dot_general(
            residual, basis, (((1,), (1,)), ((), ())), preferred_element_type=jnp.float32
        ),
        exponent_bits=8,
        mantissa_bits=7,
    ).reshape(3, 3, item_count, 2 * NF)
    adj_re = adjoint_rows[..., :NF]
    adj_im = adjoint_rows[..., NF:]
    own_re = jnp.sum(adj_re * second_re - adj_im * second_im, axis=1)
    own_im = jnp.sum(adj_re * second_im + adj_im * second_re, axis=1)
    far_re = jnp.sum(adj_re * first_re + adj_im * first_im, axis=0)
    far_im = jnp.sum(adj_re * first_im - adj_im * first_re, axis=0)
    own_onehot = (own_group[None, :] == station_iota[:, None]).astype(jnp.float32)
    grad_group = lax.dot_general(
        own_onehot,
        jnp.stack([own_re, own_im]),
        (((1,), (2,)), ((), ())),
        precision=lax.Precision.HIGHEST,
        preferred_element_type=jnp.float32,
    )
    output_scale = 1.0 / math.sqrt(2.0 * block_total * slot_cap / per_block)
    phase_full = phase_table(0, NF, NT)
    cos_full = jnp.cos(phase_full) / math.sqrt(NF)
    sin_full = jnp.sin(phase_full) / math.sqrt(NF)
    own_matrix = jnp.transpose(grad_group, (1, 3, 2, 0)).reshape(2 * NF, 3 * per_block)
    product_own = lax.dot_general(
        jnp.concatenate([cos_full, -sin_full], axis=0),
        own_matrix,
        (((0,), (0,)), ((), ())),
        precision=lax.Precision.HIGHEST,
        preferred_element_type=jnp.float32,
    )
    product_own = lax.optimization_barrier(product_own)
    far_grad = jnp.transpose(jnp.stack([far_re, far_im]), (2, 0, 1, 3)).astype(jnp.bfloat16)
    back_sent = jnp.transpose(
        far_grad.reshape(item_count, 2, 3, band_total, freq_dev), (3, 0, 1, 2, 4)
    )
    band_back = lax.all_to_all(back_sent, "frq", split_axis=0, concat_axis=0, tiled=True)
    far_band = band_back.reshape(block_total, slot_cap * 2 * 3 * freq_dev)
    back_grad = blk_exchange(far_band).astype(jnp.float32)
    back_onehot = (asked_ids.reshape(slot_total)[None, :] == station_iota[:, None]).astype(
        jnp.float32
    )
    station_grad = jnp.dot(
        back_onehot,
        back_grad.reshape(slot_total, 6 * freq_dev),
        precision=lax.Precision.HIGHEST,
        preferred_element_type=jnp.float32,
    )
    grad_matrix = jnp.transpose(
        station_grad.reshape(per_block, 2, 3, freq_dev), (1, 3, 2, 0)
    ).reshape(2 * freq_dev, 3 * per_block)
    basis_part = jnp.concatenate(
        [
            lax.dynamic_slice_in_dim(cos_full, band_index * freq_dev, freq_dev),
            -lax.dynamic_slice_in_dim(sin_full, band_index * freq_dev, freq_dev),
        ],
        axis=0,
    )
    product = product_own + lax.dot_general(
        basis_part,
        grad_matrix,
        (((0,), (0,)), ((), ())),
        precision=lax.Precision.HIGHEST,
        preferred_element_type=jnp.float32,
    )
    lag_parts = lax.all_to_all(
        product.reshape(band_total, NT // band_total, 3, per_block) * output_scale,
        "frq",
        split_axis=0,
        concat_axis=0,
        tiled=True,
    )
    return jnp.sum(lag_parts, axis=0)


def solution(mesh):
    return jax.shard_map(
        local,
        mesh=mesh,
        in_specs=(
            P(None, None, "blk", "frq"),
            P(("blk", "frq"), None, None, None),
            P("blk", None, None),
            P("blk", None, None),
            P("blk", None),
        ),
        out_specs=P("frq", None, "blk"),
        check_vma=False,
    )
```

```python
import math

import jax
import jax.numpy as jnp
from jax import lax
from jax.sharding import PartitionSpec as P

NF = 512
NT = 1024


def phase_table(freq_start, freq_count, time_count):
    freq_index = lax.iota(jnp.int32, freq_count) + freq_start
    time_index = lax.iota(jnp.int32, time_count)
    phase_num = (2 * freq_index + 1)[:, None] * time_index[None, :] % (2 * NT)
    return phase_num.astype(jnp.float32) * (math.pi / NT)


def lag_window():
    time_index = lax.iota(jnp.int32, NT)
    lag_size = jnp.minimum(time_index, NT - time_index)
    return ((lag_size >= NT // 32) & (lag_size < NT // 4)).astype(jnp.float32)


def cross_spectra(first_rows, second_rows):
    real_part = (
        first_rows[:, 0, :, None] * second_rows[:, 0, None, :]
        + first_rows[:, 1, :, None] * second_rows[:, 1, None, :]
    )
    imag_part = (
        first_rows[:, 1, :, None] * second_rows[:, 0, None, :]
        - first_rows[:, 0, :, None] * second_rows[:, 1, None, :]
    )
    return jnp.stack([real_part, imag_part], axis=3)


def pair_gradients(adjoint_rows, first_rows, second_rows):
    adj_real = adjoint_rows[:, :, :, 0]
    adj_imag = adjoint_rows[:, :, :, 1]
    own_real = jnp.sum(
        adj_real * second_rows[:, 0, None] - adj_imag * second_rows[:, 1, None], axis=2
    )
    own_imag = jnp.sum(
        adj_real * second_rows[:, 1, None] + adj_imag * second_rows[:, 0, None], axis=2
    )
    far_real = jnp.sum(
        adj_real * first_rows[:, 0, :, None] + adj_imag * first_rows[:, 1, :, None], axis=1
    )
    far_imag = jnp.sum(
        adj_real * first_rows[:, 1, :, None] - adj_imag * first_rows[:, 0, :, None], axis=1
    )
    return (jnp.stack([own_real, own_imag], axis=1), jnp.stack([far_real, far_imag], axis=1))


def blk_exchange(chunks):
    count, width = chunks.shape
    moved = lax.all_to_all(
        chunks.reshape(count, 4, width // 4), "blk", split_axis=0, concat_axis=0, tiled=True
    )
    return moved.reshape(count, width)


def local(spectra, observed, own_station, partner_station, pair_count):
    block_total = lax.axis_size("blk")
    band_total = lax.axis_size("frq")
    per_block = spectra.shape[2]
    freq_dev = spectra.shape[3]
    slot_cap = own_station.shape[2]
    slot_total = block_total * slot_cap
    item_count = slot_total // band_total
    band_index = lax.axis_index("frq")
    spec_rows = jnp.transpose(spectra, (2, 0, 1, 3))
    own_ids = own_station[0].reshape(slot_total)
    partner_local = partner_station[0]
    partner_ids = partner_local.reshape(slot_total)
    alive_mask = (
        (lax.iota(jnp.int32, slot_cap)[None, :] < pair_count[0][:, None])
        .reshape(slot_total)
        .astype(jnp.float32)
    )
    asked_ids = lax.all_to_all(partner_local, "blk", split_axis=0, concat_axis=0, tiled=True)
    asked_onehot = (
        asked_ids.reshape(slot_total)[:, None] == lax.iota(jnp.int32, per_block)[None, :]
    ).astype(spectra.dtype)
    asked_rows = jnp.dot(
        asked_onehot, spec_rows.reshape(per_block, -1), preferred_element_type=jnp.float32
    ).astype(spectra.dtype)
    rows_new = blk_exchange(asked_rows.reshape(block_total, -1)).reshape(
        band_total, item_count, 2, 3, freq_dev
    )
    lag_low = NT // 32
    lag_high = NT // 4
    lag_index = jnp.concatenate(
        [
            lax.iota(jnp.int32, lag_high - lag_low) + lag_low,
            lax.iota(jnp.int32, lag_high - lag_low) + (NT - lag_high + 1),
        ]
    )
    phase = (2 * lax.iota(jnp.int32, NF) + 1)[:, None] * lag_index[None, :] % (2 * NT)
    phase = phase.astype(jnp.float32) * (math.pi / NT)
    basis = jnp.concatenate(
        [
            (jnp.cos(phase) / math.sqrt(NF)).astype(jnp.bfloat16),
            -(jnp.sin(phase) / math.sqrt(NF)).astype(jnp.bfloat16),
        ],
        axis=0,
    )
    lag_size = jnp.minimum(lag_index, NT - lag_index)
    window = ((lag_size >= lag_low) & (lag_size < lag_high)).astype(jnp.float32)
    observed_all = jnp.transpose(observed, (1, 2, 0, 3)).reshape(9 * item_count, NT)
    observed_rows = jnp.concatenate(
        [
            observed_all[:, lag_low:lag_high],
            observed_all[:, NT - lag_high + 1 : NT - lag_low + 1],
        ],
        axis=1,
    ).astype(jnp.float32)
    basis, observed_rows, window, rows_new = lax.optimization_barrier(
        (basis, observed_rows, window, rows_new)
    )
    own_table = jnp.broadcast_to(spec_rows[None], (band_total, per_block, 2, 3, freq_dev))
    sent = jnp.concatenate([rows_new, own_table], axis=1)
    whole_band = lax.all_to_all(sent, "frq", split_axis=0, concat_axis=0, tiled=True)
    whole_band = jnp.transpose(whole_band, (2, 3, 1, 0, 4)).reshape(
        2, 3, item_count + per_block, NF
    )
    second_rows = whole_band[:, :, :item_count].astype(jnp.float32)
    own_group = lax.dynamic_slice_in_dim(own_ids, band_index * item_count, item_count)
    group_onehot = (own_group[:, None] == lax.iota(jnp.int32, per_block)[None, :]).astype(
        whole_band.dtype
    )
    first_rows = jnp.einsum(
        "pn,rcnk->rcpk",
        group_onehot,
        whole_band[:, :, item_count:],
        preferred_element_type=jnp.float32,
    )
    alive_band = lax.dynamic_slice_in_dim(alive_mask, band_index * item_count, item_count)
    first_re = first_rows[0][:, None]
    first_im = first_rows[1][:, None]
    second_re = second_rows[0][None]
    second_im = second_rows[1][None]
    alive_col = alive_band[None, None, :, None]
    cross = (
        jnp.concatenate(
            [
                first_re * second_re + first_im * second_im,
                first_im * second_re - first_re * second_im,
            ],
            axis=3,
        )
        * alive_col
    ).astype(jnp.bfloat16)
    station_iota = lax.iota(jnp.int32, per_block)
    correlation = jnp.dot(
        cross.reshape(9 * item_count, 2 * NF), basis, preferred_element_type=jnp.float32
    )
    residual = (
        (correlation - observed_rows) * jnp.tile(alive_band, 9)[:, None] * window[None, :]
    ).astype(jnp.bfloat16)
    adjoint_rows = lax.reduce_precision(
        lax.dot_general(
            residual, basis, (((1,), (1,)), ((), ())), preferred_element_type=jnp.float32
        ),
        exponent_bits=8,
        mantissa_bits=7,
    ).reshape(3, 3, item_count, 2 * NF)
    adj_re = adjoint_rows[..., :NF]
    adj_im = adjoint_rows[..., NF:]
    own_re = jnp.sum(adj_re * second_re - adj_im * second_im, axis=1)
    own_im = jnp.sum(adj_re * second_im + adj_im * second_re, axis=1)
    far_re = jnp.sum(adj_re * first_re + adj_im * first_im, axis=0)
    far_im = jnp.sum(adj_re * first_im - adj_im * first_re, axis=0)
    own_onehot = (own_group[None, :] == station_iota[:, None]).astype(jnp.float32)
    grad_group = lax.dot_general(
        own_onehot,
        jnp.stack([own_re, own_im]),
        (((1,), (2,)), ((), ())),
        precision=lax.Precision.HIGHEST,
        preferred_element_type=jnp.float32,
    )
    output_scale = 1.0 / math.sqrt(2.0 * block_total * slot_cap / per_block)
    phase_full = phase_table(0, NF, NT)
    cos_full = jnp.cos(phase_full) / math.sqrt(NF)
    sin_full = jnp.sin(phase_full) / math.sqrt(NF)
    own_matrix = jnp.transpose(grad_group, (1, 3, 2, 0)).reshape(2 * NF, 3 * per_block)
    product_own = lax.dot_general(
        jnp.concatenate([cos_full, -sin_full], axis=0),
        own_matrix,
        (((0,), (0,)), ((), ())),
        precision=lax.Precision.HIGHEST,
        preferred_element_type=jnp.float32,
    )
    product_own = lax.optimization_barrier(product_own)
    far_grad = jnp.transpose(jnp.stack([far_re, far_im]), (2, 0, 1, 3)).astype(jnp.bfloat16)
    back_sent = jnp.transpose(
        far_grad.reshape(item_count, 2, 3, band_total, freq_dev), (3, 0, 1, 2, 4)
    ).reshape(band_total, item_count // slot_cap, 4, slot_cap * 2 * 3 * freq_dev // 4)
    band_back = lax.all_to_all(back_sent, "frq", split_axis=0, concat_axis=0, tiled=True)
    far_band = band_back.reshape(block_total, slot_cap * 2 * 3 * freq_dev)
    back_grad = blk_exchange(far_band).astype(jnp.float32)
    back_onehot = (asked_ids.reshape(slot_total)[None, :] == station_iota[:, None]).astype(
        jnp.float32
    )
    station_grad = jnp.dot(
        back_onehot,
        back_grad.reshape(slot_total, 6 * freq_dev),
        precision=lax.Precision.HIGHEST,
        preferred_element_type=jnp.float32,
    )
    grad_matrix = jnp.transpose(
        station_grad.reshape(per_block, 2, 3, freq_dev), (1, 3, 2, 0)
    ).reshape(2 * freq_dev, 3 * per_block)
    basis_part = jnp.concatenate(
        [
            lax.dynamic_slice_in_dim(cos_full, band_index * freq_dev, freq_dev),
            -lax.dynamic_slice_in_dim(sin_full, band_index * freq_dev, freq_dev),
        ],
        axis=0,
    )
    product = product_own + lax.dot_general(
        basis_part,
        grad_matrix,
        (((0,), (0,)), ((), ())),
        precision=lax.Precision.HIGHEST,
        preferred_element_type=jnp.float32,
    )
    lag_parts = lax.all_to_all(
        product.reshape(band_total, NT // band_total, 3, per_block) * output_scale,
        "frq",
        split_axis=0,
        concat_axis=0,
        tiled=True,
    )
    return jnp.sum(lag_parts, axis=0)


def solution(mesh):
    return jax.shard_map(
        local,
        mesh=mesh,
        in_specs=(
            P(None, None, "blk", "frq"),
            P(("blk", "frq"), None, None, None),
            P("blk", None, None),
            P("blk", None, None),
            P("blk", None),
        ),
        out_specs=P("frq", None, "blk"),
        check_vma=False,
    )
```

```python
import math

import jax
import jax.numpy as jnp
from jax import lax
from jax.sharding import PartitionSpec as P

NF = 512
NT = 1024


def phase_table(freq_start, freq_count, time_count):
    freq_index = lax.iota(jnp.int32, freq_count) + freq_start
    time_index = lax.iota(jnp.int32, time_count)
    phase_num = (2 * freq_index + 1)[:, None] * time_index[None, :] % (2 * NT)
    return phase_num.astype(jnp.float32) * (math.pi / NT)


def lag_window():
    time_index = lax.iota(jnp.int32, NT)
    lag_size = jnp.minimum(time_index, NT - time_index)
    return ((lag_size >= NT // 32) & (lag_size < NT // 4)).astype(jnp.float32)


def cross_spectra(first_rows, second_rows):
    real_part = (
        first_rows[:, 0, :, None] * second_rows[:, 0, None, :]
        + first_rows[:, 1, :, None] * second_rows[:, 1, None, :]
    )
    imag_part = (
        first_rows[:, 1, :, None] * second_rows[:, 0, None, :]
        - first_rows[:, 0, :, None] * second_rows[:, 1, None, :]
    )
    return jnp.stack([real_part, imag_part], axis=3)


def pair_gradients(adjoint_rows, first_rows, second_rows):
    adj_real = adjoint_rows[:, :, :, 0]
    adj_imag = adjoint_rows[:, :, :, 1]
    own_real = jnp.sum(
        adj_real * second_rows[:, 0, None] - adj_imag * second_rows[:, 1, None], axis=2
    )
    own_imag = jnp.sum(
        adj_real * second_rows[:, 1, None] + adj_imag * second_rows[:, 0, None], axis=2
    )
    far_real = jnp.sum(
        adj_real * first_rows[:, 0, :, None] + adj_imag * first_rows[:, 1, :, None], axis=1
    )
    far_imag = jnp.sum(
        adj_real * first_rows[:, 1, :, None] - adj_imag * first_rows[:, 0, :, None], axis=1
    )
    return (jnp.stack([own_real, own_imag], axis=1), jnp.stack([far_real, far_imag], axis=1))


def blk_exchange(chunks):
    count, width = chunks.shape
    moved = lax.all_to_all(
        chunks.reshape(count, 4, width // 4), "blk", split_axis=0, concat_axis=0, tiled=True
    )
    return moved.reshape(count, width)


def local(spectra, observed, own_station, partner_station, pair_count):
    block_total = lax.axis_size("blk")
    band_total = lax.axis_size("frq")
    per_block = spectra.shape[2]
    freq_dev = spectra.shape[3]
    slot_cap = own_station.shape[2]
    slot_total = block_total * slot_cap
    item_count = slot_total // band_total
    band_index = lax.axis_index("frq")
    spec_rows = jnp.transpose(spectra, (2, 0, 1, 3))
    own_ids = own_station[0].reshape(slot_total)
    partner_local = partner_station[0]
    partner_ids = partner_local.reshape(slot_total)
    alive_mask = (
        (lax.iota(jnp.int32, slot_cap)[None, :] < pair_count[0][:, None])
        .reshape(slot_total)
        .astype(jnp.float32)
    )
    asked_ids = lax.all_to_all(partner_local, "blk", split_axis=0, concat_axis=0, tiled=True)
    asked_onehot = (
        asked_ids.reshape(slot_total)[:, None] == lax.iota(jnp.int32, per_block)[None, :]
    ).astype(spectra.dtype)
    asked_rows = jnp.dot(
        asked_onehot, spec_rows.reshape(per_block, -1), preferred_element_type=jnp.float32
    ).astype(spectra.dtype)
    rows_new = blk_exchange(asked_rows.reshape(block_total, -1)).reshape(
        band_total, item_count // slot_cap, 4, -1
    )
    lag_low = NT // 32
    lag_high = NT // 4
    lag_index = jnp.concatenate(
        [
            lax.iota(jnp.int32, lag_high - lag_low) + lag_low,
            lax.iota(jnp.int32, lag_high - lag_low) + (NT - lag_high + 1),
        ]
    )
    phase = (2 * lax.iota(jnp.int32, NF) + 1)[:, None] * lag_index[None, :] % (2 * NT)
    phase = phase.astype(jnp.float32) * (math.pi / NT)
    basis = jnp.concatenate(
        [
            (jnp.cos(phase) / math.sqrt(NF)).astype(jnp.bfloat16),
            -(jnp.sin(phase) / math.sqrt(NF)).astype(jnp.bfloat16),
        ],
        axis=0,
    )
    lag_size = jnp.minimum(lag_index, NT - lag_index)
    window = ((lag_size >= lag_low) & (lag_size < lag_high)).astype(jnp.float32)
    observed_all = jnp.transpose(observed, (1, 2, 0, 3)).reshape(9 * item_count, NT)
    observed_rows = jnp.concatenate(
        [
            observed_all[:, lag_low:lag_high],
            observed_all[:, NT - lag_high + 1 : NT - lag_low + 1],
        ],
        axis=1,
    ).astype(jnp.float32)
    basis, observed_rows, window, rows_new = lax.optimization_barrier(
        (basis, observed_rows, window, rows_new)
    )
    own_table = jnp.broadcast_to(
        spec_rows.reshape(1, per_block // 2, 4, -1), (band_total, per_block // 2, 4, 3 * freq_dev)
    )
    sent = jnp.concatenate([rows_new, own_table], axis=1)
    whole_band = lax.all_to_all(sent, "frq", split_axis=0, concat_axis=0, tiled=True)
    split_at = item_count // slot_cap
    whole_band = jnp.concatenate(
        [
            whole_band[:, :split_at].reshape(band_total, item_count, 2, 3, freq_dev),
            whole_band[:, split_at:].reshape(band_total, per_block, 2, 3, freq_dev),
        ],
        axis=1,
    )
    whole_band = jnp.transpose(whole_band, (2, 3, 1, 0, 4)).reshape(
        2, 3, item_count + per_block, NF
    )
    second_rows = whole_band[:, :, :item_count].astype(jnp.float32)
    own_group = lax.dynamic_slice_in_dim(own_ids, band_index * item_count, item_count)
    group_onehot = (own_group[:, None] == lax.iota(jnp.int32, per_block)[None, :]).astype(
        whole_band.dtype
    )
    first_rows = jnp.einsum(
        "pn,rcnk->rcpk",
        group_onehot,
        whole_band[:, :, item_count:],
        preferred_element_type=jnp.float32,
    )
    alive_band = lax.dynamic_slice_in_dim(alive_mask, band_index * item_count, item_count)
    first_re = first_rows[0][:, None]
    first_im = first_rows[1][:, None]
    second_re = second_rows[0][None]
    second_im = second_rows[1][None]
    alive_col = alive_band[None, None, :, None]
    cross = (
        jnp.concatenate(
            [
                first_re * second_re + first_im * second_im,
                first_im * second_re - first_re * second_im,
            ],
            axis=3,
        )
        * alive_col
    ).astype(jnp.bfloat16)
    station_iota = lax.iota(jnp.int32, per_block)
    correlation = jnp.dot(
        cross.reshape(9 * item_count, 2 * NF), basis, preferred_element_type=jnp.float32
    )
    residual = (
        (correlation - observed_rows) * jnp.tile(alive_band, 9)[:, None] * window[None, :]
    ).astype(jnp.bfloat16)
    adjoint_rows = lax.reduce_precision(
        lax.dot_general(
            residual, basis, (((1,), (1,)), ((), ())), preferred_element_type=jnp.float32
        ),
        exponent_bits=8,
        mantissa_bits=7,
    ).reshape(3, 3, item_count, 2 * NF)
    adj_re = adjoint_rows[..., :NF]
    adj_im = adjoint_rows[..., NF:]
    own_re = jnp.sum(adj_re * second_re - adj_im * second_im, axis=1)
    own_im = jnp.sum(adj_re * second_im + adj_im * second_re, axis=1)
    far_re = jnp.sum(adj_re * first_re + adj_im * first_im, axis=0)
    far_im = jnp.sum(adj_re * first_im - adj_im * first_re, axis=0)
    own_onehot = (own_group[None, :] == station_iota[:, None]).astype(jnp.float32)
    grad_group = lax.dot_general(
        own_onehot,
        jnp.stack([own_re, own_im]),
        (((1,), (2,)), ((), ())),
        precision=lax.Precision.HIGHEST,
        preferred_element_type=jnp.float32,
    )
    output_scale = 1.0 / math.sqrt(2.0 * block_total * slot_cap / per_block)
    phase_full = phase_table(0, NF, NT)
    cos_full = jnp.cos(phase_full) / math.sqrt(NF)
    sin_full = jnp.sin(phase_full) / math.sqrt(NF)
    own_matrix = jnp.transpose(grad_group, (1, 3, 2, 0)).reshape(2 * NF, 3 * per_block)
    product_own = lax.dot_general(
        jnp.concatenate([cos_full, -sin_full], axis=0),
        own_matrix,
        (((0,), (0,)), ((), ())),
        precision=lax.Precision.HIGHEST,
        preferred_element_type=jnp.float32,
    )
    product_own = lax.optimization_barrier(product_own)
    far_grad = jnp.transpose(jnp.stack([far_re, far_im]), (2, 0, 1, 3)).astype(jnp.bfloat16)
    back_sent = jnp.transpose(
        far_grad.reshape(item_count, 2, 3, band_total, freq_dev), (3, 0, 1, 2, 4)
    ).reshape(band_total, item_count // slot_cap, 4, slot_cap * 2 * 3 * freq_dev // 4)
    band_back = lax.all_to_all(back_sent, "frq", split_axis=0, concat_axis=0, tiled=True)
    far_band = band_back.reshape(block_total, slot_cap * 2 * 3 * freq_dev)
    back_grad = blk_exchange(far_band).astype(jnp.float32)
    back_onehot = (asked_ids.reshape(slot_total)[None, :] == station_iota[:, None]).astype(
        jnp.float32
    )
    station_grad = jnp.dot(
        back_onehot,
        back_grad.reshape(slot_total, 6 * freq_dev),
        precision=lax.Precision.HIGHEST,
        preferred_element_type=jnp.float32,
    )
    grad_matrix = jnp.transpose(
        station_grad.reshape(per_block, 2, 3, freq_dev), (1, 3, 2, 0)
    ).reshape(2 * freq_dev, 3 * per_block)
    basis_part = jnp.concatenate(
        [
            lax.dynamic_slice_in_dim(cos_full, band_index * freq_dev, freq_dev),
            -lax.dynamic_slice_in_dim(sin_full, band_index * freq_dev, freq_dev),
        ],
        axis=0,
    )
    product = product_own + lax.dot_general(
        basis_part,
        grad_matrix,
        (((0,), (0,)), ((), ())),
        precision=lax.Precision.HIGHEST,
        preferred_element_type=jnp.float32,
    )
    lag_parts = lax.all_to_all(
        product.reshape(band_total, NT // band_total, 3, per_block) * output_scale,
        "frq",
        split_axis=0,
        concat_axis=0,
        tiled=True,
    )
    return jnp.sum(lag_parts, axis=0)


def solution(mesh):
    return jax.shard_map(
        local,
        mesh=mesh,
        in_specs=(
            P(None, None, "blk", "frq"),
            P(("blk", "frq"), None, None, None),
            P("blk", None, None),
            P("blk", None, None),
            P("blk", None),
        ),
        out_specs=P("frq", None, "blk"),
        check_vma=False,
    )
```

```python
import math

import jax
import jax.numpy as jnp
from jax import lax
from jax.sharding import PartitionSpec as P

NF = 512
NT = 1024


def phase_table(freq_start, freq_count, time_count):
    freq_index = lax.iota(jnp.int32, freq_count) + freq_start
    time_index = lax.iota(jnp.int32, time_count)
    phase_num = (2 * freq_index + 1)[:, None] * time_index[None, :] % (2 * NT)
    return phase_num.astype(jnp.float32) * (math.pi / NT)


def lag_window():
    time_index = lax.iota(jnp.int32, NT)
    lag_size = jnp.minimum(time_index, NT - time_index)
    return ((lag_size >= NT // 32) & (lag_size < NT // 4)).astype(jnp.float32)


def cross_spectra(first_rows, second_rows):
    real_part = (
        first_rows[:, 0, :, None] * second_rows[:, 0, None, :]
        + first_rows[:, 1, :, None] * second_rows[:, 1, None, :]
    )
    imag_part = (
        first_rows[:, 1, :, None] * second_rows[:, 0, None, :]
        - first_rows[:, 0, :, None] * second_rows[:, 1, None, :]
    )
    return jnp.stack([real_part, imag_part], axis=3)


def pair_gradients(adjoint_rows, first_rows, second_rows):
    adj_real = adjoint_rows[:, :, :, 0]
    adj_imag = adjoint_rows[:, :, :, 1]
    own_real = jnp.sum(
        adj_real * second_rows[:, 0, None] - adj_imag * second_rows[:, 1, None], axis=2
    )
    own_imag = jnp.sum(
        adj_real * second_rows[:, 1, None] + adj_imag * second_rows[:, 0, None], axis=2
    )
    far_real = jnp.sum(
        adj_real * first_rows[:, 0, :, None] + adj_imag * first_rows[:, 1, :, None], axis=1
    )
    far_imag = jnp.sum(
        adj_real * first_rows[:, 1, :, None] - adj_imag * first_rows[:, 0, :, None], axis=1
    )
    return (jnp.stack([own_real, own_imag], axis=1), jnp.stack([far_real, far_imag], axis=1))


def blk_exchange(chunks):
    count, width = chunks.shape
    moved = lax.all_to_all(
        chunks.reshape(count, 4, width // 4), "blk", split_axis=0, concat_axis=0, tiled=True
    )
    return moved.reshape(count, width)


def local(spectra, observed, own_station, partner_station, pair_count):
    block_total = lax.axis_size("blk")
    band_total = lax.axis_size("frq")
    per_block = spectra.shape[2]
    freq_dev = spectra.shape[3]
    slot_cap = own_station.shape[2]
    slot_total = block_total * slot_cap
    item_count = slot_total // band_total
    band_index = lax.axis_index("frq")
    spec_rows = jnp.transpose(spectra, (2, 0, 1, 3))
    own_ids = own_station[0].reshape(slot_total)
    partner_local = partner_station[0]
    partner_ids = partner_local.reshape(slot_total)
    alive_mask = (
        (lax.iota(jnp.int32, slot_cap)[None, :] < pair_count[0][:, None])
        .reshape(slot_total)
        .astype(jnp.float32)
    )
    asked_ids = lax.all_to_all(
        jnp.pad(partner_local[:, None, :], ((0, 0), (0, 0), (0, 128 - slot_cap))),
        "blk",
        split_axis=0,
        concat_axis=0,
        tiled=True,
    )[:, 0, :slot_cap]
    asked_onehot = (
        asked_ids.reshape(slot_total)[:, None] == lax.iota(jnp.int32, per_block)[None, :]
    ).astype(spectra.dtype)
    asked_rows = jnp.dot(
        asked_onehot, spec_rows.reshape(per_block, -1), preferred_element_type=jnp.float32
    ).astype(spectra.dtype)
    rows_new = blk_exchange(asked_rows.reshape(block_total, -1)).reshape(
        band_total, item_count, 2, 3, freq_dev
    )
    lag_low = NT // 32
    lag_high = NT // 4
    lag_index = jnp.concatenate(
        [
            lax.iota(jnp.int32, lag_high - lag_low) + lag_low,
            lax.iota(jnp.int32, lag_high - lag_low) + (NT - lag_high + 1),
        ]
    )
    phase = (2 * lax.iota(jnp.int32, NF) + 1)[:, None] * lag_index[None, :] % (2 * NT)
    phase = phase.astype(jnp.float32) * (math.pi / NT)
    basis = jnp.concatenate(
        [
            (jnp.cos(phase) / math.sqrt(NF)).astype(jnp.bfloat16),
            -(jnp.sin(phase) / math.sqrt(NF)).astype(jnp.bfloat16),
        ],
        axis=0,
    )
    lag_size = jnp.minimum(lag_index, NT - lag_index)
    window = ((lag_size >= lag_low) & (lag_size < lag_high)).astype(jnp.float32)
    observed_all = jnp.transpose(observed, (1, 2, 0, 3)).reshape(9 * item_count, NT)
    observed_rows = jnp.concatenate(
        [
            observed_all[:, lag_low:lag_high],
            observed_all[:, NT - lag_high + 1 : NT - lag_low + 1],
        ],
        axis=1,
    ).astype(jnp.float32)
    basis, observed_rows, window, rows_new = lax.optimization_barrier(
        (basis, observed_rows, window, rows_new)
    )
    own_table = jnp.broadcast_to(spec_rows[None], (band_total, per_block, 2, 3, freq_dev))
    sent = jnp.concatenate([rows_new, own_table], axis=1)
    whole_band = lax.all_to_all(sent, "frq", split_axis=0, concat_axis=0, tiled=True)
    whole_band = jnp.transpose(whole_band, (2, 3, 1, 0, 4)).reshape(
        2, 3, item_count + per_block, NF
    )
    second_rows = whole_band[:, :, :item_count].astype(jnp.float32)
    own_group = lax.dynamic_slice_in_dim(own_ids, band_index * item_count, item_count)
    group_onehot = (own_group[:, None] == lax.iota(jnp.int32, per_block)[None, :]).astype(
        whole_band.dtype
    )
    first_rows = jnp.einsum(
        "pn,rcnk->rcpk",
        group_onehot,
        whole_band[:, :, item_count:],
        preferred_element_type=jnp.float32,
    )
    alive_band = lax.dynamic_slice_in_dim(alive_mask, band_index * item_count, item_count)
    first_re = first_rows[0][:, None]
    first_im = first_rows[1][:, None]
    second_re = second_rows[0][None]
    second_im = second_rows[1][None]
    alive_col = alive_band[None, None, :, None]
    cross = (
        jnp.concatenate(
            [
                first_re * second_re + first_im * second_im,
                first_im * second_re - first_re * second_im,
            ],
            axis=3,
        )
        * alive_col
    ).astype(jnp.bfloat16)
    station_iota = lax.iota(jnp.int32, per_block)
    correlation = jnp.dot(
        cross.reshape(9 * item_count, 2 * NF), basis, preferred_element_type=jnp.float32
    )
    residual = (
        (correlation - observed_rows) * jnp.tile(alive_band, 9)[:, None] * window[None, :]
    ).astype(jnp.bfloat16)
    adjoint_rows = lax.reduce_precision(
        lax.dot_general(
            residual, basis, (((1,), (1,)), ((), ())), preferred_element_type=jnp.float32
        ),
        exponent_bits=8,
        mantissa_bits=7,
    ).reshape(3, 3, item_count, 2 * NF)
    adj_re = adjoint_rows[..., :NF]
    adj_im = adjoint_rows[..., NF:]
    own_re = jnp.sum(adj_re * second_re - adj_im * second_im, axis=1)
    own_im = jnp.sum(adj_re * second_im + adj_im * second_re, axis=1)
    far_re = jnp.sum(adj_re * first_re + adj_im * first_im, axis=0)
    far_im = jnp.sum(adj_re * first_im - adj_im * first_re, axis=0)
    own_onehot = (own_group[None, :] == station_iota[:, None]).astype(jnp.float32)
    grad_group = lax.dot_general(
        own_onehot,
        jnp.stack([own_re, own_im]),
        (((1,), (2,)), ((), ())),
        precision=lax.Precision.HIGHEST,
        preferred_element_type=jnp.float32,
    )
    output_scale = 1.0 / math.sqrt(2.0 * block_total * slot_cap / per_block)
    phase_full = phase_table(0, NF, NT)
    cos_full = jnp.cos(phase_full) / math.sqrt(NF)
    sin_full = jnp.sin(phase_full) / math.sqrt(NF)
    own_matrix = jnp.transpose(grad_group, (1, 3, 2, 0)).reshape(2 * NF, 3 * per_block)
    product_own = lax.dot_general(
        jnp.concatenate([cos_full, -sin_full], axis=0),
        own_matrix,
        (((0,), (0,)), ((), ())),
        precision=lax.Precision.HIGHEST,
        preferred_element_type=jnp.float32,
    )
    product_own = lax.optimization_barrier(product_own)
    far_grad = jnp.transpose(jnp.stack([far_re, far_im]), (2, 0, 1, 3)).astype(jnp.bfloat16)
    back_sent = jnp.transpose(
        far_grad.reshape(item_count, 2, 3, band_total, freq_dev), (3, 0, 1, 2, 4)
    ).reshape(band_total, item_count // slot_cap, 4, slot_cap * 2 * 3 * freq_dev // 4)
    band_back = lax.all_to_all(back_sent, "frq", split_axis=0, concat_axis=0, tiled=True)
    far_band = band_back.reshape(block_total, slot_cap * 2 * 3 * freq_dev)
    back_grad = blk_exchange(far_band).astype(jnp.float32)
    back_onehot = (asked_ids.reshape(slot_total)[None, :] == station_iota[:, None]).astype(
        jnp.float32
    )
    station_grad = jnp.dot(
        back_onehot,
        back_grad.reshape(slot_total, 6 * freq_dev),
        precision=lax.Precision.HIGHEST,
        preferred_element_type=jnp.float32,
    )
    grad_matrix = jnp.transpose(
        station_grad.reshape(per_block, 2, 3, freq_dev), (1, 3, 2, 0)
    ).reshape(2 * freq_dev, 3 * per_block)
    basis_part = jnp.concatenate(
        [
            lax.dynamic_slice_in_dim(cos_full, band_index * freq_dev, freq_dev),
            -lax.dynamic_slice_in_dim(sin_full, band_index * freq_dev, freq_dev),
        ],
        axis=0,
    )
    product = product_own + lax.dot_general(
        basis_part,
        grad_matrix,
        (((0,), (0,)), ((), ())),
        precision=lax.Precision.HIGHEST,
        preferred_element_type=jnp.float32,
    )
    lag_parts = lax.all_to_all(
        product.reshape(band_total, NT // band_total, 3, per_block) * output_scale,
        "frq",
        split_axis=0,
        concat_axis=0,
        tiled=True,
    )
    return jnp.sum(lag_parts, axis=0)


def solution(mesh):
    return jax.shard_map(
        local,
        mesh=mesh,
        in_specs=(
            P(None, None, "blk", "frq"),
            P(("blk", "frq"), None, None, None),
            P("blk", None, None),
            P("blk", None, None),
            P("blk", None),
        ),
        out_specs=P("frq", None, "blk"),
        check_vma=False,
    )
```

```python
import math

import jax
import jax.numpy as jnp
from jax import lax
from jax.sharding import PartitionSpec as P

NF = 512
NT = 1024


def phase_table(freq_start, freq_count, time_count):
    freq_index = lax.iota(jnp.int32, freq_count) + freq_start
    time_index = lax.iota(jnp.int32, time_count)
    phase_num = (2 * freq_index + 1)[:, None] * time_index[None, :] % (2 * NT)
    return phase_num.astype(jnp.float32) * (math.pi / NT)


def lag_window():
    time_index = lax.iota(jnp.int32, NT)
    lag_size = jnp.minimum(time_index, NT - time_index)
    return ((lag_size >= NT // 32) & (lag_size < NT // 4)).astype(jnp.float32)


def cross_spectra(first_rows, second_rows):
    real_part = (
        first_rows[:, 0, :, None] * second_rows[:, 0, None, :]
        + first_rows[:, 1, :, None] * second_rows[:, 1, None, :]
    )
    imag_part = (
        first_rows[:, 1, :, None] * second_rows[:, 0, None, :]
        - first_rows[:, 0, :, None] * second_rows[:, 1, None, :]
    )
    return jnp.stack([real_part, imag_part], axis=3)


def pair_gradients(adjoint_rows, first_rows, second_rows):
    adj_real = adjoint_rows[:, :, :, 0]
    adj_imag = adjoint_rows[:, :, :, 1]
    own_real = jnp.sum(
        adj_real * second_rows[:, 0, None] - adj_imag * second_rows[:, 1, None], axis=2
    )
    own_imag = jnp.sum(
        adj_real * second_rows[:, 1, None] + adj_imag * second_rows[:, 0, None], axis=2
    )
    far_real = jnp.sum(
        adj_real * first_rows[:, 0, :, None] + adj_imag * first_rows[:, 1, :, None], axis=1
    )
    far_imag = jnp.sum(
        adj_real * first_rows[:, 1, :, None] - adj_imag * first_rows[:, 0, :, None], axis=1
    )
    return (jnp.stack([own_real, own_imag], axis=1), jnp.stack([far_real, far_imag], axis=1))


def blk_exchange(chunks):
    count, width = chunks.shape
    moved = lax.all_to_all(
        chunks.reshape(count, 4, width // 4), "blk", split_axis=0, concat_axis=0, tiled=True
    )
    return moved.reshape(count, width)


def local(spectra, observed, own_station, partner_station, pair_count):
    block_total = lax.axis_size("blk")
    band_total = lax.axis_size("frq")
    per_block = spectra.shape[2]
    freq_dev = spectra.shape[3]
    slot_cap = own_station.shape[2]
    slot_total = block_total * slot_cap
    item_count = slot_total // band_total
    band_index = lax.axis_index("frq")
    spec_rows = jnp.transpose(spectra, (2, 0, 1, 3))
    own_ids = own_station[0].reshape(slot_total)
    partner_local = partner_station[0]
    partner_ids = partner_local.reshape(slot_total)
    alive_mask = (
        (lax.iota(jnp.int32, slot_cap)[None, :] < pair_count[0][:, None])
        .reshape(slot_total)
        .astype(jnp.float32)
    )
    asked_ids = lax.all_to_all(
        jnp.pad(partner_local[:, None, :], ((0, 0), (0, 0), (0, 128 - slot_cap))),
        "blk",
        split_axis=0,
        concat_axis=0,
        tiled=True,
    )[:, 0, :slot_cap]
    asked_onehot = (
        asked_ids.reshape(slot_total)[:, None] == lax.iota(jnp.int32, per_block)[None, :]
    ).astype(spectra.dtype)
    asked_rows = jnp.dot(
        asked_onehot, spec_rows.reshape(per_block, -1), preferred_element_type=jnp.float32
    ).astype(spectra.dtype)
    rows_new = blk_exchange(asked_rows.reshape(block_total, -1)).reshape(
        band_total, item_count, 2, 3, freq_dev
    )
    lag_low = NT // 32
    lag_high = NT // 4
    lag_index = jnp.concatenate(
        [
            lax.iota(jnp.int32, lag_high - lag_low) + lag_low,
            lax.iota(jnp.int32, lag_high - lag_low) + (NT - lag_high + 1),
        ]
    )
    phase = (2 * lax.iota(jnp.int32, NF) + 1)[:, None] * lag_index[None, :] % (2 * NT)
    phase = phase.astype(jnp.float32) * (math.pi / NT)
    basis = jnp.concatenate(
        [
            (jnp.cos(phase) / math.sqrt(NF)).astype(jnp.bfloat16),
            -(jnp.sin(phase) / math.sqrt(NF)).astype(jnp.bfloat16),
        ],
        axis=0,
    )
    lag_size = jnp.minimum(lag_index, NT - lag_index)
    window = ((lag_size >= lag_low) & (lag_size < lag_high)).astype(jnp.float32)
    observed_all = jnp.transpose(observed, (1, 2, 0, 3)).reshape(9 * item_count, NT)
    observed_rows = jnp.concatenate(
        [
            observed_all[:, lag_low:lag_high],
            observed_all[:, NT - lag_high + 1 : NT - lag_low + 1],
        ],
        axis=1,
    ).astype(jnp.float32)
    basis, observed_rows, window, rows_new = lax.optimization_barrier(
        (basis, observed_rows, window, rows_new)
    )
    own_table = jnp.broadcast_to(spec_rows[None], (band_total, per_block, 2, 3, freq_dev))
    sent = jnp.concatenate([rows_new, own_table], axis=1)
    whole_band = lax.all_to_all(sent, "frq", split_axis=0, concat_axis=0, tiled=True)
    whole_band = jnp.transpose(whole_band, (2, 3, 1, 0, 4)).reshape(
        2, 3, item_count + per_block, NF
    )
    second_rows = whole_band[:, :, :item_count].astype(jnp.float32)
    own_group = lax.dynamic_slice_in_dim(own_ids, band_index * item_count, item_count)
    group_onehot = (own_group[:, None] == lax.iota(jnp.int32, per_block)[None, :]).astype(
        whole_band.dtype
    )
    first_rows = jnp.einsum(
        "pn,rcnk->rcpk",
        group_onehot,
        whole_band[:, :, item_count:],
        preferred_element_type=jnp.float32,
    )
    alive_band = lax.dynamic_slice_in_dim(alive_mask, band_index * item_count, item_count)
    first_re = first_rows[0][:, None]
    first_im = first_rows[1][:, None]
    second_re = second_rows[0][None]
    second_im = second_rows[1][None]
    alive_col = alive_band[None, None, :, None]
    cross = (
        jnp.concatenate(
            [
                first_re * second_re + first_im * second_im,
                first_im * second_re - first_re * second_im,
            ],
            axis=3,
        )
        * alive_col
    ).astype(jnp.bfloat16)
    station_iota = lax.iota(jnp.int32, per_block)
    correlation = jnp.dot(
        cross.reshape(9 * item_count, 2 * NF), basis, preferred_element_type=jnp.float32
    )
    residual = (
        (correlation - observed_rows) * jnp.tile(alive_band, 9)[:, None] * window[None, :]
    ).astype(jnp.bfloat16)
    adjoint_rows = lax.reduce_precision(
        lax.dot_general(
            residual, basis, (((1,), (1,)), ((), ())), preferred_element_type=jnp.float32
        ),
        exponent_bits=8,
        mantissa_bits=7,
    ).reshape(3, 3, item_count, 2 * NF)
    adj_re = adjoint_rows[..., :NF]
    adj_im = adjoint_rows[..., NF:]
    own_re = jnp.sum(adj_re * second_re - adj_im * second_im, axis=1)
    own_im = jnp.sum(adj_re * second_im + adj_im * second_re, axis=1)
    far_re = jnp.sum(adj_re * first_re + adj_im * first_im, axis=0)
    far_im = jnp.sum(adj_re * first_im - adj_im * first_re, axis=0)
    own_onehot = (own_group[None, :] == station_iota[:, None]).astype(jnp.float32)
    grad_group = lax.dot_general(
        own_onehot,
        jnp.stack([own_re, own_im]),
        (((1,), (2,)), ((), ())),
        precision=lax.Precision.HIGHEST,
        preferred_element_type=jnp.float32,
    )
    output_scale = 1.0 / math.sqrt(2.0 * block_total * slot_cap / per_block)
    phase_full = phase_table(0, NF, NT)
    cos_full = jnp.cos(phase_full) / math.sqrt(NF)
    sin_full = jnp.sin(phase_full) / math.sqrt(NF)
    own_matrix = jnp.transpose(grad_group, (1, 3, 2, 0)).reshape(2 * NF, 3 * per_block)
    product_own = lax.dot_general(
        jnp.concatenate([cos_full, -sin_full], axis=0).reshape(2 * NF, band_total, -1),
        own_matrix,
        (((0,), (0,)), ((), ())),
        precision=lax.Precision.HIGHEST,
        preferred_element_type=jnp.float32,
    )
    product_own = lax.optimization_barrier(product_own)
    far_grad = jnp.transpose(jnp.stack([far_re, far_im]), (2, 0, 1, 3)).astype(jnp.bfloat16)
    back_sent = jnp.transpose(
        far_grad.reshape(item_count, 2, 3, band_total, freq_dev), (3, 0, 1, 2, 4)
    ).reshape(band_total, item_count // slot_cap, 4, slot_cap * 2 * 3 * freq_dev // 4)
    band_back = lax.all_to_all(back_sent, "frq", split_axis=0, concat_axis=0, tiled=True)
    far_band = band_back.reshape(block_total, slot_cap * 2 * 3 * freq_dev)
    back_grad = blk_exchange(far_band).astype(jnp.float32)
    back_onehot = (asked_ids.reshape(slot_total)[None, :] == station_iota[:, None]).astype(
        jnp.float32
    )
    station_grad = jnp.dot(
        back_onehot,
        back_grad.reshape(slot_total, 6 * freq_dev),
        precision=lax.Precision.HIGHEST,
        preferred_element_type=jnp.float32,
    )
    grad_matrix = jnp.transpose(
        station_grad.reshape(per_block, 2, 3, freq_dev), (1, 3, 2, 0)
    ).reshape(2 * freq_dev, 3 * per_block)
    basis_part = jnp.concatenate(
        [
            lax.dynamic_slice_in_dim(cos_full, band_index * freq_dev, freq_dev),
            -lax.dynamic_slice_in_dim(sin_full, band_index * freq_dev, freq_dev),
        ],
        axis=0,
    )
    product = product_own + lax.dot_general(
        basis_part.reshape(2 * freq_dev, band_total, -1),
        grad_matrix,
        (((0,), (0,)), ((), ())),
        precision=lax.Precision.HIGHEST,
        preferred_element_type=jnp.float32,
    )
    lag_parts = lax.all_to_all(
        product.reshape(band_total, NT // band_total, 3, per_block) * output_scale,
        "frq",
        split_axis=0,
        concat_axis=0,
        tiled=True,
    )
    return jnp.sum(lag_parts, axis=0)


def solution(mesh):
    return jax.shard_map(
        local,
        mesh=mesh,
        in_specs=(
            P(None, None, "blk", "frq"),
            P(("blk", "frq"), None, None, None),
            P("blk", None, None),
            P("blk", None, None),
            P("blk", None),
        ),
        out_specs=P("frq", None, "blk"),
        check_vma=False,
    )
```

```python
import math

import jax
import jax.numpy as jnp
from jax import lax
from jax.sharding import PartitionSpec as P

NF = 512
NT = 1024


def phase_table(freq_start, freq_count, time_count):
    freq_index = lax.iota(jnp.int32, freq_count) + freq_start
    time_index = lax.iota(jnp.int32, time_count)
    phase_num = (2 * freq_index + 1)[:, None] * time_index[None, :] % (2 * NT)
    return phase_num.astype(jnp.float32) * (math.pi / NT)


def lag_window():
    time_index = lax.iota(jnp.int32, NT)
    lag_size = jnp.minimum(time_index, NT - time_index)
    return ((lag_size >= NT // 32) & (lag_size < NT // 4)).astype(jnp.float32)


def cross_spectra(first_rows, second_rows):
    real_part = (
        first_rows[:, 0, :, None] * second_rows[:, 0, None, :]
        + first_rows[:, 1, :, None] * second_rows[:, 1, None, :]
    )
    imag_part = (
        first_rows[:, 1, :, None] * second_rows[:, 0, None, :]
        - first_rows[:, 0, :, None] * second_rows[:, 1, None, :]
    )
    return jnp.stack([real_part, imag_part], axis=3)


def pair_gradients(adjoint_rows, first_rows, second_rows):
    adj_real = adjoint_rows[:, :, :, 0]
    adj_imag = adjoint_rows[:, :, :, 1]
    own_real = jnp.sum(
        adj_real * second_rows[:, 0, None] - adj_imag * second_rows[:, 1, None], axis=2
    )
    own_imag = jnp.sum(
        adj_real * second_rows[:, 1, None] + adj_imag * second_rows[:, 0, None], axis=2
    )
    far_real = jnp.sum(
        adj_real * first_rows[:, 0, :, None] + adj_imag * first_rows[:, 1, :, None], axis=1
    )
    far_imag = jnp.sum(
        adj_real * first_rows[:, 1, :, None] - adj_imag * first_rows[:, 0, :, None], axis=1
    )
    return (jnp.stack([own_real, own_imag], axis=1), jnp.stack([far_real, far_imag], axis=1))


def blk_exchange(chunks):
    count, width = chunks.shape
    moved = lax.all_to_all(
        chunks.reshape(count, 4, width // 4), "blk", split_axis=0, concat_axis=0, tiled=True
    )
    return moved.reshape(count, width)


def local(spectra, observed, own_station, partner_station, pair_count):
    block_total = lax.axis_size("blk")
    band_total = lax.axis_size("frq")
    per_block = spectra.shape[2]
    freq_dev = spectra.shape[3]
    slot_cap = own_station.shape[2]
    slot_total = block_total * slot_cap
    item_count = slot_total // band_total
    band_index = lax.axis_index("frq")
    spec_rows = jnp.transpose(spectra, (2, 0, 1, 3))
    own_ids = own_station[0].reshape(slot_total)
    partner_local = partner_station[0]
    partner_ids = partner_local.reshape(slot_total)
    alive_mask = (
        (lax.iota(jnp.int32, slot_cap)[None, :] < pair_count[0][:, None])
        .reshape(slot_total)
        .astype(jnp.float32)
    )
    asked_ids = lax.all_to_all(
        jnp.pad(partner_local[:, None, :], ((0, 0), (0, 0), (0, 128 - slot_cap))),
        "blk",
        split_axis=0,
        concat_axis=0,
        tiled=True,
    )[:, 0, :slot_cap]
    asked_onehot = (
        asked_ids.reshape(slot_total)[:, None] == lax.iota(jnp.int32, per_block)[None, :]
    ).astype(spectra.dtype)
    asked_rows = jnp.dot(
        asked_onehot, spec_rows.reshape(per_block, -1), preferred_element_type=jnp.float32
    ).astype(spectra.dtype)
    rows_new = blk_exchange(asked_rows.reshape(block_total, -1)).reshape(
        band_total, item_count, 2, 3, freq_dev
    )
    lag_low = NT // 32
    lag_high = NT // 4
    lag_index = jnp.concatenate(
        [
            lax.iota(jnp.int32, lag_high - lag_low) + lag_low,
            lax.iota(jnp.int32, lag_high - lag_low) + (NT - lag_high + 1),
        ]
    )
    phase = (2 * lax.iota(jnp.int32, NF) + 1)[:, None] * lag_index[None, :] % (2 * NT)
    phase = phase.astype(jnp.float32) * (math.pi / NT)
    basis = jnp.concatenate(
        [
            (jnp.cos(phase) / math.sqrt(NF)).astype(jnp.bfloat16),
            -(jnp.sin(phase) / math.sqrt(NF)).astype(jnp.bfloat16),
        ],
        axis=0,
    )
    lag_size = jnp.minimum(lag_index, NT - lag_index)
    window = ((lag_size >= lag_low) & (lag_size < lag_high)).astype(jnp.float32)
    observed_all = jnp.transpose(observed, (1, 2, 0, 3)).reshape(9 * item_count, NT)
    observed_rows = jnp.concatenate(
        [
            observed_all[:, lag_low:lag_high],
            observed_all[:, NT - lag_high + 1 : NT - lag_low + 1],
        ],
        axis=1,
    ).astype(jnp.float32)
    basis, observed_rows, window, rows_new = lax.optimization_barrier(
        (basis, observed_rows, window, rows_new)
    )
    own_table = jnp.broadcast_to(spec_rows[None], (band_total, per_block, 2, 3, freq_dev))
    sent = jnp.concatenate([rows_new, own_table], axis=1)
    whole_band = lax.all_to_all(sent, "frq", split_axis=0, concat_axis=0, tiled=True)
    whole_band = jnp.transpose(whole_band, (2, 3, 1, 0, 4)).reshape(
        2, 3, item_count + per_block, NF
    )
    second_rows = whole_band[:, :, :item_count].astype(jnp.float32)
    own_group = lax.dynamic_slice_in_dim(own_ids, band_index * item_count, item_count)
    group_onehot = (own_group[:, None] == lax.iota(jnp.int32, per_block)[None, :]).astype(
        whole_band.dtype
    )
    first_rows = jnp.einsum(
        "pn,rcnk->rcpk",
        group_onehot,
        whole_band[:, :, item_count:],
        preferred_element_type=jnp.float32,
    )
    alive_band = lax.dynamic_slice_in_dim(alive_mask, band_index * item_count, item_count)
    first_re = first_rows[0][:, None]
    first_im = first_rows[1][:, None]
    second_re = second_rows[0][None]
    second_im = second_rows[1][None]
    alive_col = alive_band[None, None, :, None]
    cross = (
        jnp.concatenate(
            [
                first_re * second_re + first_im * second_im,
                first_im * second_re - first_re * second_im,
            ],
            axis=3,
        )
        * alive_col
    ).astype(jnp.bfloat16)
    station_iota = lax.iota(jnp.int32, per_block)
    correlation = jnp.dot(
        cross.reshape(9 * item_count, 2 * NF), basis, preferred_element_type=jnp.float32
    )
    residual = (
        (correlation - observed_rows) * jnp.tile(alive_band, 9)[:, None] * window[None, :]
    ).astype(jnp.bfloat16)
    adjoint_rows = lax.reduce_precision(
        lax.dot_general(
            residual, basis, (((1,), (1,)), ((), ())), preferred_element_type=jnp.float32
        ),
        exponent_bits=8,
        mantissa_bits=7,
    ).reshape(3, 3, item_count, 2 * NF)
    adj_re = adjoint_rows[..., :NF]
    adj_im = adjoint_rows[..., NF:]
    own_re = jnp.sum(adj_re * second_re - adj_im * second_im, axis=1)
    own_im = jnp.sum(adj_re * second_im + adj_im * second_re, axis=1)
    far_re = jnp.sum(adj_re * first_re + adj_im * first_im, axis=0)
    far_im = jnp.sum(adj_re * first_im - adj_im * first_re, axis=0)
    own_onehot = (own_group[None, :] == station_iota[:, None]).astype(jnp.float32)
    grad_group = lax.dot_general(
        own_onehot,
        jnp.stack([own_re, own_im]),
        (((1,), (2,)), ((), ())),
        precision=lax.Precision.HIGHEST,
        preferred_element_type=jnp.float32,
    )
    output_scale = 1.0 / math.sqrt(2.0 * block_total * slot_cap / per_block)
    phase_full = phase_table(0, NF, NT)
    cos_full = jnp.cos(phase_full) / math.sqrt(NF)
    sin_full = jnp.sin(phase_full) / math.sqrt(NF)
    own_matrix = jnp.transpose(grad_group, (1, 3, 2, 0)).reshape(2 * NF, 3 * per_block)
    product_own = lax.dot_general(
        jnp.concatenate([cos_full, -sin_full], axis=0),
        own_matrix,
        (((0,), (0,)), ((), ())),
        precision=lax.Precision.HIGHEST,
        preferred_element_type=jnp.float32,
    )
    product_own = lax.optimization_barrier(product_own)
    far_grad = jnp.transpose(jnp.stack([far_re, far_im]), (2, 0, 1, 3)).astype(jnp.bfloat16)
    back_sent = jnp.transpose(
        far_grad.reshape(item_count, 2, 3, band_total, freq_dev), (3, 0, 1, 2, 4)
    ).reshape(band_total, item_count // slot_cap, 4, slot_cap * 2 * 3 * freq_dev // 4)
    band_back = lax.all_to_all(back_sent, "frq", split_axis=0, concat_axis=0, tiled=True)
    far_band = band_back.reshape(block_total, slot_cap * 2 * 3 * freq_dev)
    back_grad = blk_exchange(far_band).astype(jnp.float32)
    back_onehot = (asked_ids.reshape(slot_total)[None, :] == station_iota[:, None]).astype(
        jnp.float32
    )
    station_grad = jnp.dot(
        back_onehot,
        back_grad.reshape(slot_total, 6 * freq_dev),
        preferred_element_type=jnp.float32,
    )
    grad_matrix = jnp.transpose(
        station_grad.reshape(per_block, 2, 3, freq_dev), (1, 3, 2, 0)
    ).reshape(2 * freq_dev, 3 * per_block)
    basis_part = jnp.concatenate(
        [
            lax.dynamic_slice_in_dim(cos_full, band_index * freq_dev, freq_dev),
            -lax.dynamic_slice_in_dim(sin_full, band_index * freq_dev, freq_dev),
        ],
        axis=0,
    )
    product = product_own + lax.dot_general(
        basis_part,
        grad_matrix,
        (((0,), (0,)), ((), ())),
        precision=lax.Precision.HIGH,
        preferred_element_type=jnp.float32,
    )
    lag_parts = lax.all_to_all(
        product.reshape(band_total, NT // band_total, 3, per_block) * output_scale,
        "frq",
        split_axis=0,
        concat_axis=0,
        tiled=True,
    )
    return jnp.sum(lag_parts, axis=0)


def solution(mesh):
    return jax.shard_map(
        local,
        mesh=mesh,
        in_specs=(
            P(None, None, "blk", "frq"),
            P(("blk", "frq"), None, None, None),
            P("blk", None, None),
            P("blk", None, None),
            P("blk", None),
        ),
        out_specs=P("frq", None, "blk"),
        check_vma=False,
    )
```

```python
import math

import jax
import jax.numpy as jnp
from jax import lax
from jax.sharding import PartitionSpec as P

NF = 512
NT = 1024


def phase_table(freq_start, freq_count, time_count):
    freq_index = lax.iota(jnp.int32, freq_count) + freq_start
    time_index = lax.iota(jnp.int32, time_count)
    phase_num = (2 * freq_index + 1)[:, None] * time_index[None, :] % (2 * NT)
    return phase_num.astype(jnp.float32) * (math.pi / NT)


def lag_window():
    time_index = lax.iota(jnp.int32, NT)
    lag_size = jnp.minimum(time_index, NT - time_index)
    return ((lag_size >= NT // 32) & (lag_size < NT // 4)).astype(jnp.float32)


def cross_spectra(first_rows, second_rows):
    real_part = (
        first_rows[:, 0, :, None] * second_rows[:, 0, None, :]
        + first_rows[:, 1, :, None] * second_rows[:, 1, None, :]
    )
    imag_part = (
        first_rows[:, 1, :, None] * second_rows[:, 0, None, :]
        - first_rows[:, 0, :, None] * second_rows[:, 1, None, :]
    )
    return jnp.stack([real_part, imag_part], axis=3)


def pair_gradients(adjoint_rows, first_rows, second_rows):
    adj_real = adjoint_rows[:, :, :, 0]
    adj_imag = adjoint_rows[:, :, :, 1]
    own_real = jnp.sum(
        adj_real * second_rows[:, 0, None] - adj_imag * second_rows[:, 1, None], axis=2
    )
    own_imag = jnp.sum(
        adj_real * second_rows[:, 1, None] + adj_imag * second_rows[:, 0, None], axis=2
    )
    far_real = jnp.sum(
        adj_real * first_rows[:, 0, :, None] + adj_imag * first_rows[:, 1, :, None], axis=1
    )
    far_imag = jnp.sum(
        adj_real * first_rows[:, 1, :, None] - adj_imag * first_rows[:, 0, :, None], axis=1
    )
    return (jnp.stack([own_real, own_imag], axis=1), jnp.stack([far_real, far_imag], axis=1))


def blk_exchange(chunks):
    count, width = chunks.shape
    moved = lax.all_to_all(
        chunks.reshape(count, 4, width // 4), "blk", split_axis=0, concat_axis=0, tiled=True
    )
    return moved.reshape(count, width)


def local(spectra, observed, own_station, partner_station, pair_count):
    block_total = lax.axis_size("blk")
    band_total = lax.axis_size("frq")
    per_block = spectra.shape[2]
    freq_dev = spectra.shape[3]
    slot_cap = own_station.shape[2]
    slot_total = block_total * slot_cap
    item_count = slot_total // band_total
    band_index = lax.axis_index("frq")
    spec_rows = jnp.transpose(spectra, (2, 0, 1, 3))
    own_ids = own_station[0].reshape(slot_total)
    partner_local = partner_station[0]
    partner_ids = partner_local.reshape(slot_total)
    alive_mask = (
        (lax.iota(jnp.int32, slot_cap)[None, :] < pair_count[0][:, None])
        .reshape(slot_total)
        .astype(jnp.float32)
    )
    asked_ids = lax.all_to_all(
        jnp.pad(partner_local[:, None, :], ((0, 0), (0, 0), (0, 128 - slot_cap))),
        "blk",
        split_axis=0,
        concat_axis=0,
        tiled=True,
    )[:, 0, :slot_cap]
    asked_onehot = (
        asked_ids.reshape(slot_total)[:, None] == lax.iota(jnp.int32, per_block)[None, :]
    ).astype(spectra.dtype)
    asked_rows = jnp.dot(
        asked_onehot, spec_rows.reshape(per_block, -1), preferred_element_type=jnp.float32
    ).astype(spectra.dtype)
    rows_new = blk_exchange(asked_rows.reshape(block_total, -1)).reshape(
        band_total, item_count, 2, 3, freq_dev
    )
    lag_low = NT // 32
    lag_high = NT // 4
    lag_index = jnp.concatenate(
        [
            lax.iota(jnp.int32, lag_high - lag_low) + lag_low,
            lax.iota(jnp.int32, lag_high - lag_low) + (NT - lag_high + 1),
        ]
    )
    phase = (2 * lax.iota(jnp.int32, NF) + 1)[:, None] * lag_index[None, :] % (2 * NT)
    phase = phase.astype(jnp.float32) * (math.pi / NT)
    basis = jnp.concatenate(
        [
            (jnp.cos(phase) / math.sqrt(NF)).astype(jnp.bfloat16),
            -(jnp.sin(phase) / math.sqrt(NF)).astype(jnp.bfloat16),
        ],
        axis=0,
    )
    lag_size = jnp.minimum(lag_index, NT - lag_index)
    window = ((lag_size >= lag_low) & (lag_size < lag_high)).astype(jnp.float32)
    observed_all = jnp.transpose(observed, (1, 2, 0, 3)).reshape(9 * item_count, NT)
    observed_rows = jnp.concatenate(
        [
            observed_all[:, lag_low:lag_high],
            observed_all[:, NT - lag_high + 1 : NT - lag_low + 1],
        ],
        axis=1,
    ).astype(jnp.float32)
    basis, observed_rows, window, rows_new = lax.optimization_barrier(
        (basis, observed_rows, window, rows_new)
    )
    own_table = jnp.broadcast_to(spec_rows[None], (band_total, per_block, 2, 3, freq_dev))
    sent = jnp.concatenate([rows_new, own_table], axis=1)
    whole_band = lax.all_to_all(sent, "frq", split_axis=0, concat_axis=0, tiled=True)
    whole_band = jnp.transpose(whole_band, (2, 3, 1, 0, 4)).reshape(
        2, 3, item_count + per_block, NF
    )
    second_rows = whole_band[:, :, :item_count].astype(jnp.float32)
    own_group = lax.dynamic_slice_in_dim(own_ids, band_index * item_count, item_count)
    group_onehot = (own_group[:, None] == lax.iota(jnp.int32, per_block)[None, :]).astype(
        whole_band.dtype
    )
    first_rows = jnp.einsum(
        "pn,rcnk->rcpk",
        group_onehot,
        whole_band[:, :, item_count:],
        preferred_element_type=jnp.float32,
    )
    alive_band = lax.dynamic_slice_in_dim(alive_mask, band_index * item_count, item_count)
    first_re = first_rows[0][:, None]
    first_im = first_rows[1][:, None]
    second_re = second_rows[0][None]
    second_im = second_rows[1][None]
    alive_col = alive_band[None, None, :, None]
    cross = (
        jnp.concatenate(
            [
                first_re * second_re + first_im * second_im,
                first_im * second_re - first_re * second_im,
            ],
            axis=3,
        )
        * alive_col
    ).astype(jnp.bfloat16)
    station_iota = lax.iota(jnp.int32, per_block)
    correlation = jnp.dot(
        cross.reshape(9 * item_count, 2 * NF), basis, preferred_element_type=jnp.float32
    )
    residual = (
        (correlation - observed_rows) * jnp.tile(alive_band, 9)[:, None] * window[None, :]
    ).astype(jnp.bfloat16)
    adjoint_rows = (
        lax.dot_general(
            residual, basis, (((1,), (1,)), ((), ())), preferred_element_type=jnp.float32
        )
        .astype(jnp.bfloat16)
        .astype(jnp.float32)
        .reshape(3, 3, item_count, 2 * NF)
    )
    adj_re = adjoint_rows[..., :NF]
    adj_im = adjoint_rows[..., NF:]
    own_re = jnp.sum(adj_re * second_re - adj_im * second_im, axis=1)
    own_im = jnp.sum(adj_re * second_im + adj_im * second_re, axis=1)
    far_re = jnp.sum(adj_re * first_re + adj_im * first_im, axis=0)
    far_im = jnp.sum(adj_re * first_im - adj_im * first_re, axis=0)
    own_onehot = (own_group[None, :] == station_iota[:, None]).astype(jnp.float32)
    grad_group = lax.dot_general(
        own_onehot,
        jnp.stack([own_re, own_im]),
        (((1,), (2,)), ((), ())),
        precision=lax.Precision.HIGHEST,
        preferred_element_type=jnp.float32,
    )
    output_scale = 1.0 / math.sqrt(2.0 * block_total * slot_cap / per_block)
    phase_full = phase_table(0, NF, NT)
    cos_full = jnp.cos(phase_full) / math.sqrt(NF)
    sin_full = jnp.sin(phase_full) / math.sqrt(NF)
    own_matrix = jnp.transpose(grad_group, (1, 3, 2, 0)).reshape(2 * NF, 3 * per_block)
    product_own = lax.dot_general(
        jnp.concatenate([cos_full, -sin_full], axis=0),
        own_matrix,
        (((0,), (0,)), ((), ())),
        precision=lax.Precision.HIGHEST,
        preferred_element_type=jnp.float32,
    )
    product_own = lax.optimization_barrier(product_own)
    far_grad = jnp.transpose(jnp.stack([far_re, far_im]), (2, 0, 1, 3)).astype(jnp.bfloat16)
    back_sent = jnp.transpose(
        far_grad.reshape(item_count, 2, 3, band_total, freq_dev), (3, 0, 1, 2, 4)
    ).reshape(band_total, item_count // slot_cap, 4, slot_cap * 2 * 3 * freq_dev // 4)
    band_back = lax.all_to_all(back_sent, "frq", split_axis=0, concat_axis=0, tiled=True)
    far_band = band_back.reshape(block_total, slot_cap * 2 * 3 * freq_dev)
    back_grad = blk_exchange(far_band).astype(jnp.float32)
    back_onehot = (asked_ids.reshape(slot_total)[None, :] == station_iota[:, None]).astype(
        jnp.float32
    )
    station_grad = jnp.dot(
        back_onehot,
        back_grad.reshape(slot_total, 6 * freq_dev),
        precision=lax.Precision.HIGHEST,
        preferred_element_type=jnp.float32,
    )
    grad_matrix = jnp.transpose(
        station_grad.reshape(per_block, 2, 3, freq_dev), (1, 3, 2, 0)
    ).reshape(2 * freq_dev, 3 * per_block)
    basis_part = jnp.concatenate(
        [
            lax.dynamic_slice_in_dim(cos_full, band_index * freq_dev, freq_dev),
            -lax.dynamic_slice_in_dim(sin_full, band_index * freq_dev, freq_dev),
        ],
        axis=0,
    )
    product = product_own + lax.dot_general(
        basis_part,
        grad_matrix,
        (((0,), (0,)), ((), ())),
        precision=lax.Precision.HIGHEST,
        preferred_element_type=jnp.float32,
    )
    lag_parts = lax.all_to_all(
        product.reshape(band_total, NT // band_total, 3, per_block) * output_scale,
        "frq",
        split_axis=0,
        concat_axis=0,
        tiled=True,
    )
    return jnp.sum(lag_parts, axis=0)


def solution(mesh):
    return jax.shard_map(
        local,
        mesh=mesh,
        in_specs=(
            P(None, None, "blk", "frq"),
            P(("blk", "frq"), None, None, None),
            P("blk", None, None),
            P("blk", None, None),
            P("blk", None),
        ),
        out_specs=P("frq", None, "blk"),
        check_vma=False,
    )
```

```python
import math

import jax
import jax.numpy as jnp
from jax import lax
from jax.sharding import PartitionSpec as P

NF = 512
NT = 1024


def phase_table(freq_start, freq_count, time_count):
    freq_index = lax.iota(jnp.int32, freq_count) + freq_start
    time_index = lax.iota(jnp.int32, time_count)
    phase_num = (2 * freq_index + 1)[:, None] * time_index[None, :] % (2 * NT)
    return phase_num.astype(jnp.float32) * (math.pi / NT)


def lag_window():
    time_index = lax.iota(jnp.int32, NT)
    lag_size = jnp.minimum(time_index, NT - time_index)
    return ((lag_size >= NT // 32) & (lag_size < NT // 4)).astype(jnp.float32)


def cross_spectra(first_rows, second_rows):
    real_part = (
        first_rows[:, 0, :, None] * second_rows[:, 0, None, :]
        + first_rows[:, 1, :, None] * second_rows[:, 1, None, :]
    )
    imag_part = (
        first_rows[:, 1, :, None] * second_rows[:, 0, None, :]
        - first_rows[:, 0, :, None] * second_rows[:, 1, None, :]
    )
    return jnp.stack([real_part, imag_part], axis=3)


def pair_gradients(adjoint_rows, first_rows, second_rows):
    adj_real = adjoint_rows[:, :, :, 0]
    adj_imag = adjoint_rows[:, :, :, 1]
    own_real = jnp.sum(
        adj_real * second_rows[:, 0, None] - adj_imag * second_rows[:, 1, None], axis=2
    )
    own_imag = jnp.sum(
        adj_real * second_rows[:, 1, None] + adj_imag * second_rows[:, 0, None], axis=2
    )
    far_real = jnp.sum(
        adj_real * first_rows[:, 0, :, None] + adj_imag * first_rows[:, 1, :, None], axis=1
    )
    far_imag = jnp.sum(
        adj_real * first_rows[:, 1, :, None] - adj_imag * first_rows[:, 0, :, None], axis=1
    )
    return (jnp.stack([own_real, own_imag], axis=1), jnp.stack([far_real, far_imag], axis=1))


def blk_exchange(chunks):
    count, width = chunks.shape
    moved = lax.all_to_all(
        chunks.reshape(count, 4, width // 4), "blk", split_axis=0, concat_axis=0, tiled=True
    )
    return moved.reshape(count, width)


def local(spectra, observed, own_station, partner_station, pair_count):
    block_total = lax.axis_size("blk")
    band_total = lax.axis_size("frq")
    per_block = spectra.shape[2]
    freq_dev = spectra.shape[3]
    slot_cap = own_station.shape[2]
    slot_total = block_total * slot_cap
    item_count = slot_total // band_total
    band_index = lax.axis_index("frq")
    spec_rows = jnp.transpose(spectra, (2, 0, 1, 3))
    own_ids = own_station[0].reshape(slot_total)
    partner_local = partner_station[0]
    partner_ids = partner_local.reshape(slot_total)
    alive_mask = (
        (lax.iota(jnp.int32, slot_cap)[None, :] < pair_count[0][:, None])
        .reshape(slot_total)
        .astype(jnp.float32)
    )
    asked_ids = lax.all_to_all(
        jnp.pad(partner_local[:, None, :], ((0, 0), (0, 0), (0, 128 - slot_cap))),
        "blk",
        split_axis=0,
        concat_axis=0,
        tiled=True,
    )[:, 0, :slot_cap]
    asked_onehot = (
        asked_ids.reshape(slot_total)[:, None] == lax.iota(jnp.int32, per_block)[None, :]
    ).astype(spectra.dtype)
    asked_rows = jnp.dot(
        asked_onehot, spec_rows.reshape(per_block, -1), preferred_element_type=jnp.float32
    ).astype(spectra.dtype)
    rows_new = blk_exchange(asked_rows.reshape(block_total, -1)).reshape(
        band_total, item_count, 2, 3, freq_dev
    )
    lag_low = NT // 32
    lag_high = NT // 4
    lag_index = jnp.concatenate(
        [
            lax.iota(jnp.int32, lag_high - lag_low) + lag_low,
            lax.iota(jnp.int32, lag_high - lag_low) + (NT - lag_high + 1),
        ]
    )
    phase = (2 * lax.iota(jnp.int32, NF) + 1)[:, None] * lag_index[None, :] % (2 * NT)
    phase = phase.astype(jnp.float32) * (math.pi / NT)
    basis = jnp.concatenate(
        [
            (jnp.cos(phase) / math.sqrt(NF)).astype(jnp.bfloat16),
            -(jnp.sin(phase) / math.sqrt(NF)).astype(jnp.bfloat16),
        ],
        axis=0,
    )
    lag_size = jnp.minimum(lag_index, NT - lag_index)
    window = ((lag_size >= lag_low) & (lag_size < lag_high)).astype(jnp.float32)
    observed_all = jnp.transpose(observed, (1, 2, 0, 3)).reshape(9 * item_count, NT)
    observed_rows = jnp.concatenate(
        [
            observed_all[:, lag_low:lag_high],
            observed_all[:, NT - lag_high + 1 : NT - lag_low + 1],
        ],
        axis=1,
    ).astype(jnp.float32)
    basis, observed_rows, window, rows_new = lax.optimization_barrier(
        (basis, observed_rows, window, rows_new)
    )
    own_table = jnp.broadcast_to(spec_rows[None], (band_total, per_block, 2, 3, freq_dev))
    sent = jnp.concatenate([rows_new, own_table], axis=1)
    whole_band = lax.all_to_all(sent, "frq", split_axis=0, concat_axis=0, tiled=True)
    whole_band = jnp.transpose(whole_band, (2, 3, 1, 0, 4)).reshape(
        2, 3, item_count + per_block, NF
    )
    second_rows = whole_band[:, :, :item_count].astype(jnp.float32)
    own_group = lax.dynamic_slice_in_dim(own_ids, band_index * item_count, item_count)
    group_onehot = (own_group[:, None] == lax.iota(jnp.int32, per_block)[None, :]).astype(
        whole_band.dtype
    )
    first_rows = jnp.einsum(
        "pn,rcnk->rcpk",
        group_onehot,
        whole_band[:, :, item_count:],
        preferred_element_type=jnp.float32,
    )
    alive_band = lax.dynamic_slice_in_dim(alive_mask, band_index * item_count, item_count)
    first_re = first_rows[0][:, None]
    first_im = first_rows[1][:, None]
    second_re = second_rows[0][None]
    second_im = second_rows[1][None]
    alive_col = alive_band[None, None, :, None]
    cross = (
        jnp.concatenate(
            [
                first_re * second_re + first_im * second_im,
                first_im * second_re - first_re * second_im,
            ],
            axis=3,
        )
        * alive_col
    ).astype(jnp.bfloat16)
    station_iota = lax.iota(jnp.int32, per_block)
    correlation = jnp.dot(
        cross.reshape(9 * item_count, 2 * NF), basis, preferred_element_type=jnp.float32
    )
    residual = (
        (correlation - observed_rows) * jnp.tile(alive_band, 9)[:, None] * window[None, :]
    ).astype(jnp.bfloat16)
    adjoint_rows = (
        lax.dot_general(
            residual, basis, (((1,), (1,)), ((), ())), preferred_element_type=jnp.float32
        )
        .astype(jnp.bfloat16)
        .astype(jnp.float32)
        .reshape(3, 3, item_count, 2 * NF)
    )
    adj_re = adjoint_rows[..., :NF]
    adj_im = adjoint_rows[..., NF:]
    own_re = jnp.sum(adj_re * second_re - adj_im * second_im, axis=1)
    own_im = jnp.sum(adj_re * second_im + adj_im * second_re, axis=1)
    far_re = jnp.sum(adj_re * first_re + adj_im * first_im, axis=0)
    far_im = jnp.sum(adj_re * first_im - adj_im * first_re, axis=0)
    own_onehot = (own_group[None, :] == station_iota[:, None]).astype(jnp.float32)
    grad_group = lax.dot_general(
        own_onehot,
        jnp.stack([own_re, own_im]),
        (((1,), (2,)), ((), ())),
        precision=lax.Precision.HIGHEST,
        preferred_element_type=jnp.float32,
    )
    output_scale = 1.0 / math.sqrt(2.0 * block_total * slot_cap / per_block)
    phase_full = phase_table(0, NF, NT)
    cos_full = jnp.cos(phase_full) / math.sqrt(NF)
    sin_full = jnp.sin(phase_full) / math.sqrt(NF)
    own_matrix = jnp.transpose(grad_group, (1, 3, 2, 0)).reshape(2 * NF, 3 * per_block)
    product_own = lax.dot_general(
        jnp.concatenate([cos_full, -sin_full], axis=0),
        own_matrix,
        (((0,), (0,)), ((), ())),
        precision=lax.Precision.HIGHEST,
        preferred_element_type=jnp.float32,
    )
    product_own = lax.optimization_barrier(product_own)
    far_grad = jnp.transpose(jnp.stack([far_re, far_im]), (2, 0, 1, 3)).astype(jnp.bfloat16)
    back_sent = jnp.transpose(
        far_grad.reshape(item_count, 2, 3, band_total, freq_dev), (3, 0, 1, 2, 4)
    ).reshape(band_total, item_count // slot_cap, 4, slot_cap * 2 * 3 * freq_dev // 4)
    band_back = lax.all_to_all(back_sent, "frq", split_axis=0, concat_axis=0, tiled=True)
    far_band = band_back.reshape(block_total, slot_cap * 2 * 3 * freq_dev)
    back_grad = blk_exchange(far_band).astype(jnp.float32)
    back_onehot = (asked_ids.reshape(slot_total)[None, :] == station_iota[:, None]).astype(
        jnp.float32
    )
    station_grad = jnp.dot(
        back_onehot,
        back_grad.reshape(slot_total, 6 * freq_dev),
        preferred_element_type=jnp.float32,
    )
    grad_matrix = jnp.transpose(
        station_grad.reshape(per_block, 2, 3, freq_dev), (1, 3, 2, 0)
    ).reshape(2 * freq_dev, 3 * per_block)
    basis_part = jnp.concatenate(
        [
            lax.dynamic_slice_in_dim(cos_full, band_index * freq_dev, freq_dev),
            -lax.dynamic_slice_in_dim(sin_full, band_index * freq_dev, freq_dev),
        ],
        axis=0,
    )
    product = product_own + lax.dot_general(
        basis_part,
        grad_matrix,
        (((0,), (0,)), ((), ())),
        precision=lax.Precision.HIGH,
        preferred_element_type=jnp.float32,
    )
    lag_parts = lax.all_to_all(
        product.reshape(band_total, NT // band_total, 3, per_block) * output_scale,
        "frq",
        split_axis=0,
        concat_axis=0,
        tiled=True,
    )
    return jnp.sum(lag_parts, axis=0)


def solution(mesh):
    return jax.shard_map(
        local,
        mesh=mesh,
        in_specs=(
            P(None, None, "blk", "frq"),
            P(("blk", "frq"), None, None, None),
            P("blk", None, None),
            P("blk", None, None),
            P("blk", None),
        ),
        out_specs=P("frq", None, "blk"),
        check_vma=False,
    )
```
